32 devices in a mesh: groups: 2 (over y), tiles: 4 (over z), sections: 2 (over x), chan: 2 (over core).
Axes of the slice: x: 2, y: 2, z: 4, core: 2. Of those that a mesh axis runs over, the one named last changes fastest.
Arguments:
- features: bfloat16 [8, 16, 64, 1024], P('groups', ('tiles', 'chan')), parts along dimension 0, may hold values from -6 to 6
- tissue: int32 [8, 16, 64], P('groups', ('tiles', 'chan')), parts along dimension 0, may hold values from 0 to 1, as said below
- row_label: int32 [8, 16], P('groups', ('tiles', 'chan')), parts along dimension 0, may hold values from 0 to 1
- prototypes: bfloat16 [2, 1024], replicated, may hold values from -5 to 5
- reduce_weight: bfloat16 [2, 1024, 256], P('sections', 'chan'), may hold values from -0.1875 to 0.1875
- spatial_weight: bfloat16 [2, 3, 3, 256, 256], P('sections', None, None, None, 'chan'), may hold values from -0.125 to 0.125
- expand_weight: bfloat16 [2, 256, 1024], P('sections', None, 'chan'), may hold values from -0.375 to 0.375
- norm_gain: float32 [2, 2, 256], P('sections'), may hold values from 0.25 to 1.75
- norm_bias: float32 [2, 2, 256], P('sections'), may hold values from -3 to 3
Outputs:
- grad_reduce: bfloat16 [4, 1024, 256], P(('groups', 'sections'), 'chan'), parts along dimension 0
- grad_spatial: bfloat16 [4, 3, 3, 256, 256], P(('groups', 'sections'), None, None, None, 'chan'), parts along dimension 0
- grad_expand: bfloat16 [4, 256, 1024], P(('groups', 'sections'), None, 'chan'), parts along dimension 0
- grad_gain: float32 [4, 2, 256], P(('groups', 'sections'), None, 'chan'), parts along dimension 0
- grad_bias: float32 [4, 2, 256], P(('groups', 'sections'), None, 'chan'), parts along dimension 0
The draws below stay inside these ranges and needn't reach their ends.
There are 2 independent parts, one for each index of `groups`. The reference program is written for one: setup_inputs(seed, part) draws one part's arguments, and reference() takes and returns one part's arrays. A program takes and returns all parts, laid end to end along the dimension named above; an argument that names none is the same for every part. Nothing has to cross between parts.
Inputs may be any that keep to these rules, and one draw needn't show every extreme that they name: 1 marks a tissue cell, 0 background.
All inputs are finite; a program needn't handle non-finite values.
Results may differ from the reference program's by a relative error of at most 0.011.
Values may be sent and summed in bfloat16 or wider, within the bound.
No kernel may reach another device: no remote copies, remote signals or barrier semaphores. Data moves between devices by JAX's collectives and lax.ppermute only.
A program may use at most 128 MiB of HBM per device.

```python
import jax
import jax.numpy as jnp
from jax import lax

CH = 1024
MID = 256
CLASSES = 2
MICRO = 4
ROWS_DEV = 2
COLS = 64
BLOCKS = 2
ROWS = 16
N_TILES = 4
N_CHAN = 2


def draw_tissue(key, part):
    level_key = jax.random.fold_in(key, 11)
    cell_key = jax.random.fold_in(key, 23)
    levels = jax.random.randint(level_key, (MICRO, ROWS // ROWS_DEV), 1, 5)
    band_level = jnp.repeat(levels, ROWS_DEV, axis=1)
    cell_draw = jax.random.randint(cell_key, (MICRO, ROWS, COLS), 0, 4)
    return (cell_draw < band_level[:, :, None]).astype(jnp.int32)


def set_ends(entries, stream_key, smallest, high):
    longest = entries.shape.index(max(entries.shape))
    spots = []
    for shift in (0, 1):
        where = [jax.random.randint(jax.random.fold_in(stream_key, axis), (), 0, length) for axis, length in enumerate(entries.shape)]
        where[longest] = (where[longest] + shift) % entries.shape[longest]
        spots.append(tuple(where))
    return entries.at[spots[0]].set(smallest).at[spots[1]].set(high)


def level_of(own_key, shape, split, low, top_value):
    def one(position, parts):
        steps = jax.random.uniform(jax.random.fold_in(jax.random.fold_in(own_key, 6), position), (parts,), jnp.float32, low / len(split), top_value / len(split))
        return jnp.repeat(jnp.exp(steps), shape[position] // parts).reshape((-1,) + (1,) * (len(shape) - position - 1))

    factor_of = one(*split[0])
    for cut in split[1:]:
        factor_of = factor_of * one(*cut)
    return factor_of


def scatter_about(stream_key, dims, deviation, limit, split=(), dtype=jnp.bfloat16):
    values = jax.random.normal(stream_key, dims, jnp.float32) * deviation
    if len(split) > 0:
        values = level_of(stream_key, dims, split, -0.22, 0.18) * values
    return jnp.clip(values, min=-limit, max=limit).astype(dtype)


def setup_inputs(seed: int = 0, part: int = 0) -> dict:
    keys = jax.random.split(jax.random.key(seed), 10)
    part_splits = jax.random.split(jax.random.fold_in(keys[9], part), 10)
    features = scatter_about(part_splits[0], (MICRO, ROWS, COLS, CH), 1.0, 6.0, ((1, 8),))
    tissue = draw_tissue(jax.random.fold_in(jax.random.fold_in(keys[9], part), 71), part)
    row_label = set_ends(jax.random.randint(part_splits[2], (MICRO, ROWS), 0, CLASSES), jax.random.fold_in(part_splits[2], 1), 0, CLASSES - 1).astype(jnp.int32)
    prototypes = scatter_about(keys[3], (CLASSES, CH), 1.0, 5.0)
    reduce_weight = scatter_about(keys[4], (BLOCKS, CH, MID), CH ** -0.5, 0.1875, ((0, 2), (1, 2)))
    spatial_weight = scatter_about(keys[5], (BLOCKS, 3, 3, MID, MID), (9 * MID) ** -0.5, 0.125, ((0, 2), (4, 2)))
    expand_weight = scatter_about(keys[6], (BLOCKS, MID, CH), MID ** -0.5, 0.375, ((0, 2), (2, 2)))
    norm_gain = jnp.clip(1.0 + 0.15 * jax.random.normal(keys[7], (BLOCKS, 2, MID), jnp.float32), 0.25, 1.75)
    norm_bias = scatter_about(keys[8], (BLOCKS, 2, MID), 0.5, 3.0, ((0, 2),), jnp.float32)
    return dict(features=features, tissue=tissue, row_label=row_label, prototypes=prototypes, reduce_weight=reduce_weight, spatial_weight=spatial_weight, expand_weight=expand_weight, norm_gain=norm_gain, norm_bias=norm_bias)


def grid_taps(grid_field, mirrored):
    height = grid_field.shape[1]
    breadth = grid_field.shape[2]
    padded = jnp.pad(grid_field, ((0, 0), (1, 1), (1, 1), (0, 0)))
    tap_list = []
    for shift_row in range(3):
        for shift_col in range(3):
            if mirrored:
                start_row = 2 - shift_row
                start_col = 2 - shift_col
            else:
                start_row = shift_row
                start_col = shift_col
            tap_list.append(padded[:, start_row:start_row + height, start_col:start_col + breadth])
    return jnp.concatenate(tap_list, axis=3)


def split_bands(values):
    band_count = N_TILES * N_CHAN
    region_count = values.shape[0]
    row_count = values.shape[1]
    col_count = values.shape[2]
    depth = values.shape[3]
    grouped = values.reshape(region_count, band_count, row_count // band_count, col_count, depth)
    return jnp.transpose(grouped, (1, 0, 2, 3, 4)).reshape(band_count, -1, depth)


def banded_product(left_side, right_side):
    left_bands = split_bands(left_side)
    right_bands = split_bands(right_side)

    def add_band(running, matched):
        portion = jnp.dot(matched[0].T, matched[1], preferred_element_type=jnp.float32)
        rounded = lax.optimization_barrier(portion.astype(jnp.bfloat16))
        return running + rounded.astype(jnp.float32), None

    start_value = jnp.zeros((left_side.shape[3], right_side.shape[3]), jnp.float32)
    running, _ = lax.scan(add_band, start_value, (left_bands, right_bands))
    return running


def banded_sum(values):
    portions = jnp.sum(split_bands(values), axis=1)
    rounded = lax.optimization_barrier(portions.astype(jnp.bfloat16))
    return jnp.sum(rounded.astype(jnp.float32), axis=0)


def reference(features, tissue, row_label, prototypes, reduce_weight, spatial_weight, expand_weight, norm_gain, norm_bias):
    tissue_mask = tissue.astype(jnp.float32)[:, :, :, None]
    cell_count = MICRO * ROWS * COLS
    grid_shape = (MICRO, ROWS, COLS, MID)
    current = features
    stored = []
    for block_index in range(BLOCKS):
        reduced = jnp.dot(current.reshape(cell_count, CH), reduce_weight[block_index], preferred_element_type=jnp.float32).reshape(grid_shape)
        pre_reduce = norm_gain[block_index, 0] * reduced + norm_bias[block_index, 0]
        hidden_one = jnp.maximum(pre_reduce, 0.0).astype(jnp.bfloat16)
        forward_taps = grid_taps(hidden_one, False).reshape(cell_count, 9 * MID)
        spatial_out = jnp.dot(forward_taps, spatial_weight[block_index].reshape(9 * MID, MID), preferred_element_type=jnp.float32).reshape(grid_shape)
        pre_spatial = norm_gain[block_index, 1] * spatial_out + norm_bias[block_index, 1]
        hidden_two = jnp.maximum(pre_spatial, 0.0).astype(jnp.bfloat16)
        expanded = jnp.dot(hidden_two.reshape(cell_count, MID), expand_weight[block_index], preferred_element_type=jnp.float32).reshape(MICRO, ROWS, COLS, CH)
        block_out = (tissue_mask * jnp.maximum(current.astype(jnp.float32) + expanded, 0.0)).astype(jnp.bfloat16)
        stored.append((current, hidden_one, reduced, pre_reduce, spatial_out, pre_spatial, hidden_two, block_out))
        current = block_out
    target = prototypes.astype(jnp.float32)[row_label][:, :, None, :]
    upstream = (tissue_mask * (current.astype(jnp.float32) - target) / cell_count).astype(jnp.bfloat16)
    reduce_list = [None] * BLOCKS
    spatial_list = [None] * BLOCKS
    expand_list = [None] * BLOCKS
    gain_list = [None] * BLOCKS
    shift_list = [None] * BLOCKS
    for block_index in reversed(range(BLOCKS)):
        block_in, hidden_one, reduced, pre_reduce, spatial_out, pre_spatial, hidden_two, block_out = stored[block_index]
        grad_block = jnp.where(block_out > 0, upstream, jnp.zeros_like(upstream))
        block_flat = grad_block.reshape(cell_count, CH)
        expand_list[block_index] = banded_product(hidden_two, grad_block)
        back_two = jnp.dot(block_flat, expand_weight[block_index].T, preferred_element_type=jnp.float32).reshape(grid_shape)
        masked_two = jnp.where(pre_spatial > 0, back_two, jnp.float32(0.0))
        grad_two = (masked_two * norm_gain[block_index, 1]).astype(jnp.bfloat16)
        spatial_list[block_index] = banded_product(grid_taps(hidden_one, False), grad_two).reshape(3, 3, MID, MID)
        back_matrix = jnp.transpose(spatial_weight[block_index], (0, 1, 3, 2)).reshape(9 * MID, MID)
        back_one = jnp.dot(grid_taps(grad_two, True).reshape(cell_count, 9 * MID), back_matrix, preferred_element_type=jnp.float32).reshape(grid_shape)
        masked_one = jnp.where(pre_reduce > 0, back_one, jnp.float32(0.0))
        grad_one = (masked_one * norm_gain[block_index, 0]).astype(jnp.bfloat16)
        one_flat = grad_one.reshape(cell_count, MID)
        reduce_list[block_index] = banded_product(block_in, grad_one)
        gain_list[block_index] = jnp.stack([banded_sum(masked_one * reduced), banded_sum(masked_two * spatial_out)])
        shift_list[block_index] = jnp.stack([banded_sum(masked_one), banded_sum(masked_two)])
        upstream = (grad_block.astype(jnp.float32) + jnp.dot(one_flat, reduce_weight[block_index].T, preferred_element_type=jnp.float32).reshape(MICRO, ROWS, COLS, CH)).astype(jnp.bfloat16)
    return (jnp.stack(reduce_list).astype(jnp.bfloat16), jnp.stack(spatial_list).astype(jnp.bfloat16), jnp.stack(expand_list).astype(jnp.bfloat16), jnp.stack(gain_list), jnp.stack(shift_list))
```

```python
import functools

import jax
import jax.numpy as jnp
from jax import lax
from jax.sharding import PartitionSpec as P

ROW_AXES = ("tiles", "chan")


def halo_rows(block):
    count = lax.axis_size(ROW_AXES)
    forward = [(i, i + 1) for i in range(count - 1)]
    backward = [(target, source) for source, target in forward]
    low = lax.ppermute(block[:, -1:], ROW_AXES, forward)
    high = lax.ppermute(block[:, :1], ROW_AXES, backward)
    return jnp.concatenate([low, block, high], axis=1)


def grid_taps(extended, height, breadth, mirrored):
    padded = jnp.pad(extended, ((0, 0), (0, 0), (1, 1), (0, 0)))
    tap_list = []
    for shift_row in range(3):
        for shift_col in range(3):
            if mirrored:
                start_row = 2 - shift_row
                start_col = 2 - shift_col
            else:
                start_row = shift_row
                start_col = shift_col
            tap_list.append(
                padded[:, start_row : start_row + height, start_col : start_col + breadth]
            )
    stacked = jnp.concatenate(tap_list, axis=3)
    return stacked.reshape(extended.shape[0] * height * breadth, stacked.shape[3])


def gather_blocks(half, chan_axis, chain, position):
    received = [
        lax.ppermute(half, "sections", [(i, (i + k) % chain) for i in range(chain)])
        for k in range(1, chain)
    ]
    stacked = jnp.stack([half] + received)
    if chan_axis is not None:
        stacked = lax.all_gather(stacked, "chan", axis=chan_axis + 1, tiled=True)
    return [
        lax.dynamic_index_in_dim(stacked, (position - b + chain) % chain, 0, keepdims=False)
        for b in range(chain)
    ]


def weight_partials(ops, cells, height, breadth):
    cur, h1e, h2, reduced, spatial_out, grad_block, masked_two, grad_two, masked_one, grad_one = ops
    full = cur.shape[-1]
    inner = h2.shape[-1]
    cur_flat = cur.reshape(cells, 2, full // 2)
    block_flat = grad_block.reshape(cells, 2, full // 2)
    two_flat = grad_two.reshape(cells, 2, inner // 2)
    one_flat = grad_one.reshape(cells, inner)
    reduce_term = jnp.einsum("cki,cm->kim", cur_flat, one_flat, preferred_element_type=jnp.float32)
    spatial_term = jnp.einsum(
        "ci,cko->kio",
        grid_taps(h1e, height, breadth, False),
        two_flat,
        preferred_element_type=jnp.float32,
    )
    expand_term = jnp.einsum(
        "cm,ckn->kmn", h2.reshape(cells, inner), block_flat, preferred_element_type=jnp.float32
    )
    gain = jnp.stack(
        [jnp.sum(masked_one * reduced, axis=(0, 1, 2)), jnp.sum(masked_two * spatial_out, axis=(0, 1, 2))]
    )
    bias = jnp.stack([jnp.sum(masked_one, axis=(0, 1, 2)), jnp.sum(masked_two, axis=(0, 1, 2))])
    small = jnp.concatenate([gain, bias]).reshape(4, 2, inner // 2).transpose(1, 0, 2)
    pieces = [reduce_term, spatial_term, expand_term, small]
    return jnp.concatenate(
        [piece.astype(jnp.bfloat16).reshape(2, -1) for piece in pieces], axis=1
    )


def local(
    features,
    tissue,
    row_label,
    prototypes,
    reduce_weight,
    spatial_weight,
    expand_weight,
    norm_gain,
    norm_bias,
):
    regions, height, breadth, full_width = features.shape
    chain = lax.axis_size("sections")
    position = lax.axis_index("sections")
    chan_index = lax.axis_index("chan")
    reduce_all = gather_blocks(reduce_weight[0], 0, chain, position)
    spatial_all = gather_blocks(spatial_weight[0], 3, chain, position)
    expand_all = gather_blocks(expand_weight[0], 1, chain, position)
    gain_all = gather_blocks(norm_gain[0], None, chain, position)
    bias_all = gather_blocks(norm_bias[0], None, chain, position)
    inner_width = reduce_all[0].shape[1]
    tissue_mask = tissue.astype(jnp.float32)[:, :, :, None]
    cells = regions * height * breadth
    inner_shape = (regions, height, breadth, inner_width)
    outer_shape = (regions, height, breadth, full_width)

    current = features
    saved = []
    for b in range(chain):
        gain_pair, bias_pair = gain_all[b], bias_all[b]
        reduced = jnp.dot(
            current.reshape(cells, full_width), reduce_all[b], preferred_element_type=jnp.float32
        ).reshape(inner_shape)
        pre_reduce = gain_pair[0] * reduced + bias_pair[0]
        hidden_one = jnp.maximum(pre_reduce, 0.0).astype(jnp.bfloat16)
        hidden_ext = halo_rows(hidden_one)
        spatial_out = jnp.dot(
            grid_taps(hidden_ext, height, breadth, False),
            spatial_all[b].reshape(9 * inner_width, inner_width),
            preferred_element_type=jnp.float32,
        ).reshape(inner_shape)
        pre_spatial = gain_pair[1] * spatial_out + bias_pair[1]
        hidden_two = jnp.maximum(pre_spatial, 0.0).astype(jnp.bfloat16)
        expanded = jnp.dot(
            hidden_two.reshape(cells, inner_width), expand_all[b], preferred_element_type=jnp.float32
        ).reshape(outer_shape)
        block_out = (
            tissue_mask * jnp.maximum(current.astype(jnp.float32) + expanded, 0.0)
        ).astype(jnp.bfloat16)
        saved.append((current, hidden_ext, reduced, pre_reduce, spatial_out, pre_spatial, hidden_two, block_out))
        current = block_out

    classes = prototypes.shape[0]
    chosen = (row_label[:, :, None] == jnp.arange(classes, dtype=jnp.int32)).astype(jnp.float32)
    target_rows = jnp.einsum("mrk,kc->mrc", chosen, prototypes.astype(jnp.float32))
    total_cells = regions * height * lax.axis_size("tiles") * lax.axis_size("chan") * breadth
    upstream = (
        tissue_mask * (current.astype(jnp.float32) - target_rows[:, :, None, :]) / total_cells
    ).astype(jnp.bfloat16)

    block_ops = [None] * chain
    for b in reversed(range(chain)):
        block_in, hidden_ext, reduced, pre_reduce, spatial_out, pre_spatial, hidden_two, block_out = saved[b]
        needed = b >= position
        gain_pair = gain_all[b]

        def first_back(upstream=upstream, block_out=block_out, pre_spatial=pre_spatial, b=b, gain_pair=gain_pair):
            grad_block = jnp.where(block_out > 0, upstream, jnp.zeros_like(upstream))
            back_two = jnp.dot(
                grad_block.reshape(cells, full_width), expand_all[b].T, preferred_element_type=jnp.float32
            ).reshape(inner_shape)
            masked_two = jnp.where(pre_spatial > 0, back_two, jnp.float32(0.0))
            grad_two = (masked_two * gain_pair[1]).astype(jnp.bfloat16)
            return grad_block, masked_two, grad_two

        def first_skip():
            return (
                jnp.zeros(outer_shape, jnp.bfloat16),
                jnp.zeros(inner_shape, jnp.float32),
                jnp.zeros(inner_shape, jnp.bfloat16),
            )

        grad_block, masked_two, grad_two = lax.cond(needed, first_back, first_skip)
        grad_ext = halo_rows(grad_two)

        def second_back(grad_ext=grad_ext, pre_reduce=pre_reduce, b=b, gain_pair=gain_pair):
            back_one = jnp.dot(
                grid_taps(grad_ext, height, breadth, True),
                jnp.transpose(spatial_all[b], (0, 1, 3, 2)).reshape(9 * inner_width, inner_width),
                preferred_element_type=jnp.float32,
            ).reshape(inner_shape)
            masked_one = jnp.where(pre_reduce > 0, back_one, jnp.float32(0.0))
            grad_one = (masked_one * gain_pair[0]).astype(jnp.bfloat16)
            return masked_one, grad_one

        def second_skip():
            return (jnp.zeros(inner_shape, jnp.float32), jnp.zeros(inner_shape, jnp.bfloat16))

        masked_one, grad_one = lax.cond(needed, second_back, second_skip)
        block_ops[b] = (
            block_in, hidden_ext, hidden_two, reduced, spatial_out,
            grad_block, masked_two, grad_two, masked_one, grad_one,
        )
        if b > 0:

            def pass_back(grad_block=grad_block, grad_one=grad_one, b=b):
                return (
                    grad_block.astype(jnp.float32)
                    + jnp.dot(
                        grad_one.reshape(cells, inner_width),
                        reduce_all[b].T,
                        preferred_element_type=jnp.float32,
                    ).reshape(outer_shape)
                ).astype(jnp.bfloat16)

            upstream = lax.cond(
                b > position, pass_back, lambda: jnp.zeros(outer_shape, jnp.bfloat16)
            )

    partials = lax.switch(
        position,
        [
            functools.partial(
                lambda k: weight_partials(block_ops[k], cells, height, breadth), k
            )
            for k in range(chain)
        ],
    )
    mine = lax.dynamic_index_in_dim(partials, chan_index, 0, keepdims=False)
    theirs = lax.dynamic_index_in_dim(partials, 1 - chan_index, 0, keepdims=False)
    arrived = lax.ppermute(theirs, "chan", [(0, 1), (1, 0)])
    pair_sum = (mine.astype(jnp.float32) + arrived.astype(jnp.float32)).astype(jnp.bfloat16)
    total = lax.psum(pair_sum, "tiles").astype(jnp.float32)

    half_full = full_width // 2
    half_inner = inner_width // 2
    sizes = [half_full * inner_width, 9 * inner_width * half_inner, inner_width * half_full, 4 * half_inner]
    offsets = [0]
    for size in sizes:
        offsets.append(offsets[-1] + size)
    parts = [total[offsets[i] : offsets[i + 1]] for i in range(4)]
    grad_reduce = parts[0].reshape(half_full, inner_width).astype(jnp.bfloat16)[None]
    grad_spatial = parts[1].reshape(3, 3, inner_width, half_inner).astype(jnp.bfloat16)[None]
    grad_expand = parts[2].reshape(inner_width, half_full).astype(jnp.bfloat16)[None]
    small = parts[3].reshape(4, half_inner)
    return (grad_reduce, grad_spatial, grad_expand, small[0:2][None], small[2:4][None])


def solution(mesh):
    placed = (
        P("groups", ("tiles", "chan"), None, None),
        P("groups", ("tiles", "chan"), None),
        P("groups", ("tiles", "chan")),
        P(),
        P("sections", "chan", None),
        P("sections", None, None, None, "chan"),
        P("sections", None, "chan"),
        P("sections", None, None),
        P("sections", None, None),
    )
    return jax.shard_map(
        local,
        mesh=mesh,
        in_specs=placed,
        out_specs=(
            P(("groups", "sections"), "chan", None),
            P(("groups", "sections"), None, None, None, "chan"),
            P(("groups", "sections"), None, "chan"),
            P(("groups", "sections"), None, "chan"),
            P(("groups", "sections"), None, "chan"),
        ),
        check_vma=False,
    )
```

```python
import functools

import jax
import jax.numpy as jnp
from jax import lax
from jax.sharding import PartitionSpec as P

ROW_AXES = ("tiles", "chan")


def halo_rows(block):
    count = lax.axis_size(ROW_AXES)
    forward = [(i, i + 1) for i in range(count - 1)]
    backward = [(target, source) for source, target in forward]
    low = lax.ppermute(block[:, -1:], ROW_AXES, forward)
    high = lax.ppermute(block[:, :1], ROW_AXES, backward)
    return jnp.concatenate([low, block, high], axis=1)


def grid_taps(extended, height, breadth, mirrored):
    padded = jnp.pad(extended, ((0, 0), (0, 0), (1, 1), (0, 0)))
    tap_list = []
    for shift_row in range(3):
        for shift_col in range(3):
            if mirrored:
                start_row = 2 - shift_row
                start_col = 2 - shift_col
            else:
                start_row = shift_row
                start_col = shift_col
            tap_list.append(
                padded[:, start_row : start_row + height, start_col : start_col + breadth]
            )
    stacked = jnp.concatenate(tap_list, axis=3)
    return stacked.reshape(extended.shape[0] * height * breadth, stacked.shape[3])


def gather_blocks(half, chan_axis, chain, position):
    received = [
        lax.ppermute(half, "sections", [(i, (i + k) % chain) for i in range(chain)])
        for k in range(1, chain)
    ]
    stacked = jnp.stack([half] + received)
    if chan_axis is not None:
        stacked = lax.all_gather(stacked, "chan", axis=chan_axis + 1, tiled=True)
    return [
        lax.dynamic_index_in_dim(stacked, (position - b + chain) % chain, 0, keepdims=False)
        for b in range(chain)
    ]


def weight_partials(ops, cells, height, breadth):
    cur, h1e, h2, reduced, spatial_out, grad_block, masked_two, grad_two, masked_one, grad_one = ops
    full = cur.shape[-1]
    inner = h2.shape[-1]
    block_flat = grad_block.reshape(cells, full)
    two_flat = grad_two.reshape(cells, inner)
    one_flat = grad_one.reshape(cells, inner)
    reduce_term = jnp.dot(
        one_flat.T, cur.reshape(cells, full), preferred_element_type=jnp.float32
    ).astype(jnp.bfloat16)
    spatial_term = jnp.dot(
        grid_taps(h1e, height, breadth, False).T, two_flat, preferred_element_type=jnp.float32
    ).astype(jnp.bfloat16)
    expand_term = jnp.dot(
        h2.reshape(cells, inner).T, block_flat, preferred_element_type=jnp.float32
    ).astype(jnp.bfloat16)
    gain = jnp.stack(
        [jnp.sum(masked_one * reduced, axis=(0, 1, 2)), jnp.sum(masked_two * spatial_out, axis=(0, 1, 2))]
    )
    bias = jnp.stack([jnp.sum(masked_one, axis=(0, 1, 2)), jnp.sum(masked_two, axis=(0, 1, 2))])
    small = jnp.concatenate([gain, bias]).astype(jnp.bfloat16)
    pieces = [
        reduce_term.reshape(inner, 2, full // 2).transpose(1, 2, 0),
        spatial_term.reshape(9 * inner, 2, inner // 2).transpose(1, 0, 2),
        expand_term.reshape(inner, 2, full // 2).transpose(1, 0, 2),
        small.reshape(4, 2, inner // 2).transpose(1, 0, 2),
    ]
    return jnp.concatenate([piece.reshape(2, -1) for piece in pieces], axis=1)


def local(
    features,
    tissue,
    row_label,
    prototypes,
    reduce_weight,
    spatial_weight,
    expand_weight,
    norm_gain,
    norm_bias,
):
    regions, height, breadth, full_width = features.shape
    chain = lax.axis_size("sections")
    position = lax.axis_index("sections")
    chan_index = lax.axis_index("chan")
    reduce_all = gather_blocks(reduce_weight[0], 0, chain, position)
    spatial_all = gather_blocks(spatial_weight[0], 3, chain, position)
    expand_all = gather_blocks(expand_weight[0], 1, chain, position)
    gain_all = gather_blocks(norm_gain[0], None, chain, position)
    bias_all = gather_blocks(norm_bias[0], None, chain, position)
    inner_width = reduce_all[0].shape[1]
    tissue_mask = tissue.astype(jnp.float32)[:, :, :, None]
    cells = regions * height * breadth
    inner_shape = (regions, height, breadth, inner_width)
    outer_shape = (regions, height, breadth, full_width)

    current = features
    saved = []
    for b in range(chain):
        gain_pair, bias_pair = gain_all[b], bias_all[b]
        reduced = jnp.dot(
            current.reshape(cells, full_width), reduce_all[b], preferred_element_type=jnp.float32
        ).reshape(inner_shape)
        pre_reduce = gain_pair[0] * reduced + bias_pair[0]
        hidden_one = jnp.maximum(pre_reduce, 0.0).astype(jnp.bfloat16)
        hidden_ext = halo_rows(hidden_one)
        spatial_out = jnp.dot(
            grid_taps(hidden_ext, height, breadth, False),
            spatial_all[b].reshape(9 * inner_width, inner_width),
            preferred_element_type=jnp.float32,
        ).reshape(inner_shape)
        pre_spatial = gain_pair[1] * spatial_out + bias_pair[1]
        hidden_two = jnp.maximum(pre_spatial, 0.0).astype(jnp.bfloat16)
        expanded = jnp.dot(
            hidden_two.reshape(cells, inner_width), expand_all[b], preferred_element_type=jnp.float32
        ).reshape(outer_shape)
        block_out = (
            tissue_mask * jnp.maximum(current.astype(jnp.float32) + expanded, 0.0)
        ).astype(jnp.bfloat16)
        saved.append((current, hidden_ext, reduced, pre_reduce, spatial_out, pre_spatial, hidden_two, block_out))
        current = block_out

    classes = prototypes.shape[0]
    chosen = (row_label[:, :, None] == jnp.arange(classes, dtype=jnp.int32)).astype(jnp.float32)
    target_rows = jnp.einsum("mrk,kc->mrc", chosen, prototypes.astype(jnp.float32))
    total_cells = regions * height * lax.axis_size("tiles") * lax.axis_size("chan") * breadth
    upstream = (
        tissue_mask * (current.astype(jnp.float32) - target_rows[:, :, None, :]) / total_cells
    ).astype(jnp.bfloat16)

    block_ops = [None] * chain
    for b in reversed(range(chain)):
        block_in, hidden_ext, reduced, pre_reduce, spatial_out, pre_spatial, hidden_two, block_out = saved[b]
        needed = b >= position
        gain_pair = gain_all[b]

        def first_back(upstream=upstream, block_out=block_out, pre_spatial=pre_spatial, b=b, gain_pair=gain_pair):
            grad_block = jnp.where(block_out > 0, upstream, jnp.zeros_like(upstream))
            back_two = jnp.dot(
                grad_block.reshape(cells, full_width), expand_all[b].T, preferred_element_type=jnp.float32
            ).reshape(inner_shape)
            masked_two = jnp.where(pre_spatial > 0, back_two, jnp.float32(0.0))
            grad_two = (masked_two * gain_pair[1]).astype(jnp.bfloat16)
            return grad_block, masked_two, grad_two

        def first_skip():
            return (
                jnp.zeros(outer_shape, jnp.bfloat16),
                jnp.zeros(inner_shape, jnp.float32),
                jnp.zeros(inner_shape, jnp.bfloat16),
            )

        grad_block, masked_two, grad_two = lax.cond(needed, first_back, first_skip)
        grad_ext = halo_rows(grad_two)

        def second_back(grad_ext=grad_ext, pre_reduce=pre_reduce, b=b, gain_pair=gain_pair):
            back_one = jnp.dot(
                grid_taps(grad_ext, height, breadth, True),
                jnp.transpose(spatial_all[b], (0, 1, 3, 2)).reshape(9 * inner_width, inner_width),
                preferred_element_type=jnp.float32,
            ).reshape(inner_shape)
            masked_one = jnp.where(pre_reduce > 0, back_one, jnp.float32(0.0))
            grad_one = (masked_one * gain_pair[0]).astype(jnp.bfloat16)
            return masked_one, grad_one

        def second_skip():
            return (jnp.zeros(inner_shape, jnp.float32), jnp.zeros(inner_shape, jnp.bfloat16))

        masked_one, grad_one = lax.cond(needed, second_back, second_skip)
        block_ops[b] = (
            block_in, hidden_ext, hidden_two, reduced, spatial_out,
            grad_block, masked_two, grad_two, masked_one, grad_one,
        )
        if b > 0:

            def pass_back(grad_block=grad_block, grad_one=grad_one, b=b):
                return (
                    grad_block.astype(jnp.float32)
                    + jnp.dot(
                        grad_one.reshape(cells, inner_width),
                        reduce_all[b].T,
                        preferred_element_type=jnp.float32,
                    ).reshape(outer_shape)
                ).astype(jnp.bfloat16)

            upstream = lax.cond(
                b > position, pass_back, lambda: jnp.zeros(outer_shape, jnp.bfloat16)
            )

    partials = lax.switch(
        position,
        [
            functools.partial(
                lambda k: weight_partials(block_ops[k], cells, height, breadth), k
            )
            for k in range(chain)
        ],
    )
    mine = lax.dynamic_index_in_dim(partials, chan_index, 0, keepdims=False)
    theirs = lax.dynamic_index_in_dim(partials, 1 - chan_index, 0, keepdims=False)
    arrived = lax.ppermute(theirs, "chan", [(0, 1), (1, 0)])
    pair_sum = (mine.astype(jnp.float32) + arrived.astype(jnp.float32)).astype(jnp.bfloat16)
    total = lax.psum(pair_sum, "tiles").astype(jnp.float32)

    half_full = full_width // 2
    half_inner = inner_width // 2
    sizes = [half_full * inner_width, 9 * inner_width * half_inner, inner_width * half_full, 4 * half_inner]
    offsets = [0]
    for size in sizes:
        offsets.append(offsets[-1] + size)
    parts = [total[offsets[i] : offsets[i + 1]] for i in range(4)]
    grad_reduce = parts[0].reshape(half_full, inner_width).astype(jnp.bfloat16)[None]
    grad_spatial = parts[1].reshape(3, 3, inner_width, half_inner).astype(jnp.bfloat16)[None]
    grad_expand = parts[2].reshape(inner_width, half_full).astype(jnp.bfloat16)[None]
    small = parts[3].reshape(4, half_inner)
    return (grad_reduce, grad_spatial, grad_expand, small[0:2][None], small[2:4][None])


def solution(mesh):
    placed = (
        P("groups", ("tiles", "chan"), None, None),
        P("groups", ("tiles", "chan"), None),
        P("groups", ("tiles", "chan")),
        P(),
        P("sections", "chan", None),
        P("sections", None, None, None, "chan"),
        P("sections", None, "chan"),
        P("sections", None, None),
        P("sections", None, None),
    )
    return jax.shard_map(
        local,
        mesh=mesh,
        in_specs=placed,
        out_specs=(
            P(("groups", "sections"), "chan", None),
            P(("groups", "sections"), None, None, None, "chan"),
            P(("groups", "sections"), None, "chan"),
            P(("groups", "sections"), None, "chan"),
            P(("groups", "sections"), None, "chan"),
        ),
        check_vma=False,
    )
```

```python
import functools

import jax
import jax.numpy as jnp
from jax import lax
from jax.sharding import PartitionSpec as P

ROW_AXES = ("tiles", "chan")


def halo_rows(block):
    count = lax.axis_size(ROW_AXES)
    forward = [(i, i + 1) for i in range(count - 1)]
    backward = [(target, source) for source, target in forward]
    low = lax.ppermute(block[:, -1:], ROW_AXES, forward)
    high = lax.ppermute(block[:, :1], ROW_AXES, backward)
    return jnp.concatenate([low, block, high], axis=1)


def grid_taps(extended, height, breadth, mirrored):
    padded = jnp.pad(extended, ((0, 0), (0, 0), (1, 1), (0, 0)))
    tap_list = []
    for shift_row in range(3):
        for shift_col in range(3):
            if mirrored:
                start_row = 2 - shift_row
                start_col = 2 - shift_col
            else:
                start_row = shift_row
                start_col = shift_col
            tap_list.append(
                padded[:, start_row : start_row + height, start_col : start_col + breadth]
            )
    stacked = jnp.concatenate(tap_list, axis=3)
    return stacked.reshape(extended.shape[0] * height * breadth, stacked.shape[3])


def gather_blocks(half, chan_axis, chain, position):
    received = [
        lax.ppermute(half, "sections", [(i, (i + k) % chain) for i in range(chain)])
        for k in range(1, chain)
    ]
    stacked = jnp.stack([half] + received)
    if chan_axis is not None:
        stacked = lax.all_gather(stacked, "chan", axis=chan_axis + 1, tiled=True)
    return [
        lax.dynamic_index_in_dim(stacked, (position - b + chain) % chain, 0, keepdims=False)
        for b in range(chain)
    ]


def weight_partials(ops, cells, height, breadth):
    cur, h1e, h2, reduced, spatial_out, grad_block, masked_two, grad_two, masked_one, grad_one = ops
    full = cur.shape[-1]
    inner = h2.shape[-1]
    block_flat = grad_block.reshape(cells, full)
    two_flat = grad_two.reshape(cells, inner)
    one_flat = grad_one.reshape(cells, inner)
    reduce_term = jnp.dot(
        cur.reshape(cells, full).T, one_flat, preferred_element_type=jnp.float32
    ).astype(jnp.bfloat16)
    spatial_term = jnp.dot(
        grid_taps(h1e, height, breadth, False).T, two_flat, preferred_element_type=jnp.float32
    ).astype(jnp.bfloat16)
    expand_term = jnp.dot(
        h2.reshape(cells, inner).T, block_flat, preferred_element_type=jnp.float32
    ).astype(jnp.bfloat16)
    gain = jnp.stack(
        [jnp.sum(masked_one * reduced, axis=(0, 1, 2)), jnp.sum(masked_two * spatial_out, axis=(0, 1, 2))]
    )
    bias = jnp.stack([jnp.sum(masked_one, axis=(0, 1, 2)), jnp.sum(masked_two, axis=(0, 1, 2))])
    small = jnp.concatenate([gain, bias]).astype(jnp.bfloat16)
    return (
        reduce_term.reshape(2, full // 2, inner),
        spatial_term.reshape(9 * inner, 2, inner // 2).transpose(1, 0, 2),
        expand_term.reshape(inner, 2, full // 2).transpose(1, 0, 2),
        small.reshape(4, 2, inner // 2).transpose(1, 0, 2),
    )


def local(
    features,
    tissue,
    row_label,
    prototypes,
    reduce_weight,
    spatial_weight,
    expand_weight,
    norm_gain,
    norm_bias,
):
    regions, height, breadth, full_width = features.shape
    chain = lax.axis_size("sections")
    position = lax.axis_index("sections")
    chan_index = lax.axis_index("chan")
    reduce_all = gather_blocks(reduce_weight[0], 0, chain, position)
    spatial_all = gather_blocks(spatial_weight[0], 3, chain, position)
    expand_all = gather_blocks(expand_weight[0], 1, chain, position)
    gain_all = gather_blocks(norm_gain[0], None, chain, position)
    bias_all = gather_blocks(norm_bias[0], None, chain, position)
    inner_width = reduce_all[0].shape[1]
    tissue_mask = tissue.astype(jnp.float32)[:, :, :, None]
    cells = regions * height * breadth
    inner_shape = (regions, height, breadth, inner_width)
    outer_shape = (regions, height, breadth, full_width)

    current = features
    saved = []
    for b in range(chain):
        gain_pair, bias_pair = gain_all[b], bias_all[b]
        reduced = jnp.dot(
            current.reshape(cells, full_width), reduce_all[b], preferred_element_type=jnp.float32
        ).reshape(inner_shape)
        pre_reduce = gain_pair[0] * reduced + bias_pair[0]
        hidden_one = jnp.maximum(pre_reduce, 0.0).astype(jnp.bfloat16)
        hidden_ext = halo_rows(hidden_one)
        spatial_out = jnp.dot(
            grid_taps(hidden_ext, height, breadth, False),
            spatial_all[b].reshape(9 * inner_width, inner_width),
            preferred_element_type=jnp.float32,
        ).reshape(inner_shape)
        pre_spatial = gain_pair[1] * spatial_out + bias_pair[1]
        hidden_two = jnp.maximum(pre_spatial, 0.0).astype(jnp.bfloat16)
        expanded = jnp.dot(
            hidden_two.reshape(cells, inner_width), expand_all[b], preferred_element_type=jnp.float32
        ).reshape(outer_shape)
        block_out = (
            tissue_mask * jnp.maximum(current.astype(jnp.float32) + expanded, 0.0)
        ).astype(jnp.bfloat16)
        saved.append((current, hidden_ext, reduced, pre_reduce, spatial_out, pre_spatial, hidden_two, block_out))
        current = block_out

    classes = prototypes.shape[0]
    chosen = (row_label[:, :, None] == jnp.arange(classes, dtype=jnp.int32)).astype(jnp.float32)
    target_rows = jnp.einsum("mrk,kc->mrc", chosen, prototypes.astype(jnp.float32))
    total_cells = regions * height * lax.axis_size("tiles") * lax.axis_size("chan") * breadth
    upstream = (
        tissue_mask * (current.astype(jnp.float32) - target_rows[:, :, None, :]) / total_cells
    ).astype(jnp.bfloat16)

    block_ops = [None] * chain
    for b in reversed(range(chain)):
        block_in, hidden_ext, reduced, pre_reduce, spatial_out, pre_spatial, hidden_two, block_out = saved[b]
        needed = b >= position
        gain_pair = gain_all[b]

        def first_back(upstream=upstream, block_out=block_out, pre_spatial=pre_spatial, b=b, gain_pair=gain_pair):
            grad_block = jnp.where(block_out > 0, upstream, jnp.zeros_like(upstream))
            back_two = jnp.dot(
                grad_block.reshape(cells, full_width), expand_all[b].T, preferred_element_type=jnp.float32
            ).reshape(inner_shape)
            masked_two = jnp.where(pre_spatial > 0, back_two, jnp.float32(0.0))
            grad_two = (masked_two * gain_pair[1]).astype(jnp.bfloat16)
            return grad_block, masked_two, grad_two

        def first_skip():
            return (
                jnp.zeros(outer_shape, jnp.bfloat16),
                jnp.zeros(inner_shape, jnp.float32),
                jnp.zeros(inner_shape, jnp.bfloat16),
            )

        grad_block, masked_two, grad_two = lax.cond(needed, first_back, first_skip)
        grad_ext = halo_rows(grad_two)

        def second_back(grad_ext=grad_ext, pre_reduce=pre_reduce, b=b, gain_pair=gain_pair):
            back_one = jnp.dot(
                grid_taps(grad_ext, height, breadth, True),
                jnp.transpose(spatial_all[b], (0, 1, 3, 2)).reshape(9 * inner_width, inner_width),
                preferred_element_type=jnp.float32,
            ).reshape(inner_shape)
            masked_one = jnp.where(pre_reduce > 0, back_one, jnp.float32(0.0))
            grad_one = (masked_one * gain_pair[0]).astype(jnp.bfloat16)
            return masked_one, grad_one

        def second_skip():
            return (jnp.zeros(inner_shape, jnp.float32), jnp.zeros(inner_shape, jnp.bfloat16))

        masked_one, grad_one = lax.cond(needed, second_back, second_skip)
        block_ops[b] = (
            block_in, hidden_ext, hidden_two, reduced, spatial_out,
            grad_block, masked_two, grad_two, masked_one, grad_one,
        )
        if b > 0:

            def pass_back(grad_block=grad_block, grad_one=grad_one, b=b):
                return (
                    grad_block.astype(jnp.float32)
                    + jnp.dot(
                        grad_one.reshape(cells, inner_width),
                        reduce_all[b].T,
                        preferred_element_type=jnp.float32,
                    ).reshape(outer_shape)
                ).astype(jnp.bfloat16)

            upstream = lax.cond(
                b > position, pass_back, lambda: jnp.zeros(outer_shape, jnp.bfloat16)
            )

    partials = lax.switch(
        position,
        [
            functools.partial(
                lambda k: weight_partials(block_ops[k], cells, height, breadth), k
            )
            for k in range(chain)
        ],
    )
    totals = []
    for piece in partials:
        mine = lax.dynamic_index_in_dim(piece, chan_index, 0, keepdims=False)
        theirs = lax.dynamic_index_in_dim(piece, 1 - chan_index, 0, keepdims=False)
        arrived = lax.ppermute(theirs, "chan", [(0, 1), (1, 0)])
        pair_sum = (mine.astype(jnp.float32) + arrived.astype(jnp.float32)).astype(jnp.bfloat16)
        totals.append(lax.psum(pair_sum, "tiles"))
    half_inner = inner_width // 2
    grad_reduce = totals[0][None]
    grad_spatial = totals[1].reshape(3, 3, inner_width, half_inner)[None]
    grad_expand = totals[2][None]
    small = totals[3].astype(jnp.float32)
    return (grad_reduce, grad_spatial, grad_expand, small[0:2][None], small[2:4][None])


def solution(mesh):
    placed = (
        P("groups", ("tiles", "chan"), None, None),
        P("groups", ("tiles", "chan"), None),
        P("groups", ("tiles", "chan")),
        P(),
        P("sections", "chan", None),
        P("sections", None, None, None, "chan"),
        P("sections", None, "chan"),
        P("sections", None, None),
        P("sections", None, None),
    )
    return jax.shard_map(
        local,
        mesh=mesh,
        in_specs=placed,
        out_specs=(
            P(("groups", "sections"), "chan", None),
            P(("groups", "sections"), None, None, None, "chan"),
            P(("groups", "sections"), None, "chan"),
            P(("groups", "sections"), None, "chan"),
            P(("groups", "sections"), None, "chan"),
        ),
        check_vma=False,
    )
```

```python
import functools

import jax
import jax.numpy as jnp
from jax import lax
from jax.sharding import PartitionSpec as P

ROW_AXES = ("tiles", "chan")


def halo_rows(block):
    count = lax.axis_size(ROW_AXES)
    forward = [(i, i + 1) for i in range(count - 1)]
    backward = [(target, source) for source, target in forward]
    low = lax.ppermute(block[:, -1:], ROW_AXES, forward)
    high = lax.ppermute(block[:, :1], ROW_AXES, backward)
    return jnp.concatenate([low, block, high], axis=1)


def grid_taps(extended, height, breadth, mirrored):
    padded = jnp.pad(extended, ((0, 0), (0, 0), (1, 1), (0, 0)))
    tap_list = []
    for shift_row in range(3):
        for shift_col in range(3):
            if mirrored:
                start_row = 2 - shift_row
                start_col = 2 - shift_col
            else:
                start_row = shift_row
                start_col = shift_col
            tap_list.append(
                padded[:, start_row : start_row + height, start_col : start_col + breadth]
            )
    stacked = jnp.concatenate(tap_list, axis=3)
    return stacked.reshape(extended.shape[0] * height * breadth, stacked.shape[3])


def gather_blocks(half, chan_axis, chain, position, chan_index):
    received = [
        lax.ppermute(half, "sections", [(i, (i + k) % chain) for i in range(chain)])
        for k in range(1, chain)
    ]
    stacked = jnp.stack([half] + received)
    if chan_axis is not None:
        other = lax.ppermute(stacked, "chan", [(0, 1), (1, 0)])
        stacked = jnp.where(
            chan_index == 0,
            jnp.concatenate([stacked, other], axis=chan_axis + 1),
            jnp.concatenate([other, stacked], axis=chan_axis + 1),
        )
    return [
        lax.dynamic_index_in_dim(stacked, (position - b + chain) % chain, 0, keepdims=False)
        for b in range(chain)
    ]


def weight_partials(ops, cells, height, breadth):
    cur, h1e, h2, reduced, spatial_out, grad_block, masked_two, grad_two, masked_one, grad_one = ops
    full = cur.shape[-1]
    inner = h2.shape[-1]
    block_flat = grad_block.reshape(cells, full)
    two_flat = grad_two.reshape(cells, inner)
    one_flat = grad_one.reshape(cells, inner)
    reduce_term = jnp.dot(
        cur.reshape(cells, full).T, one_flat, preferred_element_type=jnp.float32
    ).astype(jnp.bfloat16)
    spatial_term = jnp.dot(
        grid_taps(h1e, height, breadth, False).T, two_flat, preferred_element_type=jnp.float32
    ).astype(jnp.bfloat16)
    expand_term = jnp.dot(
        h2.reshape(cells, inner).T, block_flat, preferred_element_type=jnp.float32
    ).astype(jnp.bfloat16)
    gain = jnp.stack(
        [jnp.sum(masked_one * reduced, axis=(0, 1, 2)), jnp.sum(masked_two * spatial_out, axis=(0, 1, 2))]
    )
    bias = jnp.stack([jnp.sum(masked_one, axis=(0, 1, 2)), jnp.sum(masked_two, axis=(0, 1, 2))])
    small = jnp.concatenate([gain, bias]).astype(jnp.bfloat16)
    spatial_small = jnp.concatenate([spatial_term, small], axis=0)
    return (
        reduce_term.reshape(2, full // 2, inner),
        spatial_small.reshape(9 * inner + 4, 2, inner // 2).transpose(1, 0, 2),
        expand_term.reshape(inner, 2, full // 2).transpose(1, 0, 2),
    )


def local(
    features,
    tissue,
    row_label,
    prototypes,
    reduce_weight,
    spatial_weight,
    expand_weight,
    norm_gain,
    norm_bias,
):
    regions, height, breadth, full_width = features.shape
    chain = lax.axis_size("sections")
    position = lax.axis_index("sections")
    chan_index = lax.axis_index("chan")
    reduce_all = gather_blocks(reduce_weight[0], 0, chain, position, chan_index)
    spatial_all = gather_blocks(spatial_weight[0], 3, chain, position, chan_index)
    expand_all = gather_blocks(expand_weight[0], 1, chain, position, chan_index)
    gain_all = gather_blocks(norm_gain[0], None, chain, position, chan_index)
    bias_all = gather_blocks(norm_bias[0], None, chain, position, chan_index)
    inner_width = reduce_all[0].shape[1]
    tissue_mask = tissue.astype(jnp.float32)[:, :, :, None]
    cells = regions * height * breadth
    inner_shape = (regions, height, breadth, inner_width)
    outer_shape = (regions, height, breadth, full_width)

    current = features
    saved = []
    for b in range(chain):
        gain_pair, bias_pair = gain_all[b], bias_all[b]
        reduced = jnp.dot(
            current.reshape(cells, full_width), reduce_all[b], preferred_element_type=jnp.float32
        ).reshape(inner_shape)
        pre_reduce = gain_pair[0] * reduced + bias_pair[0]
        hidden_one = jnp.maximum(pre_reduce, 0.0).astype(jnp.bfloat16)
        hidden_ext = halo_rows(hidden_one)
        spatial_out = jnp.dot(
            grid_taps(hidden_ext, height, breadth, False),
            spatial_all[b].reshape(9 * inner_width, inner_width),
            preferred_element_type=jnp.float32,
        ).reshape(inner_shape)
        pre_spatial = gain_pair[1] * spatial_out + bias_pair[1]
        hidden_two = jnp.maximum(pre_spatial, 0.0).astype(jnp.bfloat16)
        expanded = jnp.dot(
            hidden_two.reshape(cells, inner_width), expand_all[b], preferred_element_type=jnp.float32
        ).reshape(outer_shape)
        block_out = (
            tissue_mask * jnp.maximum(current.astype(jnp.float32) + expanded, 0.0)
        ).astype(jnp.bfloat16)
        saved.append((current, hidden_ext, reduced, pre_reduce, spatial_out, pre_spatial, hidden_two, block_out))
        current = block_out

    classes = prototypes.shape[0]
    chosen = (row_label[:, :, None] == jnp.arange(classes, dtype=jnp.int32)).astype(jnp.float32)
    target_rows = jnp.einsum("mrk,kc->mrc", chosen, prototypes.astype(jnp.float32))
    total_cells = regions * height * lax.axis_size("tiles") * lax.axis_size("chan") * breadth
    upstream = (
        tissue_mask * (current.astype(jnp.float32) - target_rows[:, :, None, :]) / total_cells
    ).astype(jnp.bfloat16)

    block_ops = [None] * chain
    for b in reversed(range(chain)):
        block_in, hidden_ext, reduced, pre_reduce, spatial_out, pre_spatial, hidden_two, block_out = saved[b]
        needed = b >= position
        gain_pair = gain_all[b]

        def first_back(upstream=upstream, block_out=block_out, pre_spatial=pre_spatial, b=b, gain_pair=gain_pair):
            grad_block = jnp.where(block_out > 0, upstream, jnp.zeros_like(upstream))
            back_two = jnp.dot(
                grad_block.reshape(cells, full_width), expand_all[b].T, preferred_element_type=jnp.float32
            ).reshape(inner_shape)
            masked_two = jnp.where(pre_spatial > 0, back_two, jnp.float32(0.0))
            grad_two = (masked_two * gain_pair[1]).astype(jnp.bfloat16)
            return grad_block, masked_two, grad_two

        def first_skip():
            return (
                jnp.zeros(outer_shape, jnp.bfloat16),
                jnp.zeros(inner_shape, jnp.float32),
                jnp.zeros(inner_shape, jnp.bfloat16),
            )

        grad_block, masked_two, grad_two = lax.cond(needed, first_back, first_skip)
        grad_ext = halo_rows(grad_two)

        def second_back(grad_ext=grad_ext, pre_reduce=pre_reduce, b=b, gain_pair=gain_pair):
            back_one = jnp.dot(
                grid_taps(grad_ext, height, breadth, True),
                jnp.transpose(spatial_all[b], (0, 1, 3, 2)).reshape(9 * inner_width, inner_width),
                preferred_element_type=jnp.float32,
            ).reshape(inner_shape)
            masked_one = jnp.where(pre_reduce > 0, back_one, jnp.float32(0.0))
            grad_one = (masked_one * gain_pair[0]).astype(jnp.bfloat16)
            return masked_one, grad_one

        def second_skip():
            return (jnp.zeros(inner_shape, jnp.float32), jnp.zeros(inner_shape, jnp.bfloat16))

        masked_one, grad_one = lax.cond(needed, second_back, second_skip)
        block_ops[b] = (
            block_in, hidden_ext, hidden_two, reduced, spatial_out,
            grad_block, masked_two, grad_two, masked_one, grad_one,
        )
        if b > 0:

            def pass_back(grad_block=grad_block, grad_one=grad_one, b=b):
                return (
                    grad_block.astype(jnp.float32)
                    + jnp.dot(
                        grad_one.reshape(cells, inner_width),
                        reduce_all[b].T,
                        preferred_element_type=jnp.float32,
                    ).reshape(outer_shape)
                ).astype(jnp.bfloat16)

            upstream = lax.cond(
                b > position, pass_back, lambda: jnp.zeros(outer_shape, jnp.bfloat16)
            )

    partials = lax.switch(
        position,
        [
            functools.partial(
                lambda k: weight_partials(block_ops[k], cells, height, breadth), k
            )
            for k in range(chain)
        ],
    )
    totals = []
    for piece in partials:
        mine = lax.dynamic_index_in_dim(piece, chan_index, 0, keepdims=False)
        theirs = lax.dynamic_index_in_dim(piece, 1 - chan_index, 0, keepdims=False)
        arrived = lax.ppermute(theirs, "chan", [(0, 1), (1, 0)])
        pair_sum = (mine.astype(jnp.float32) + arrived.astype(jnp.float32)).astype(jnp.bfloat16)
        totals.append(lax.psum(pair_sum, "tiles"))
    half_inner = inner_width // 2
    grad_reduce = totals[0][None]
    grad_spatial = totals[1][: 9 * inner_width].reshape(3, 3, inner_width, half_inner)[None]
    grad_expand = totals[2][None]
    small = totals[1][9 * inner_width :].astype(jnp.float32)
    return (grad_reduce, grad_spatial, grad_expand, small[0:2][None], small[2:4][None])


def solution(mesh):
    placed = (
        P("groups", ("tiles", "chan"), None, None),
        P("groups", ("tiles", "chan"), None),
        P("groups", ("tiles", "chan")),
        P(),
        P("sections", "chan", None),
        P("sections", None, None, None, "chan"),
        P("sections", None, "chan"),
        P("sections", None, None),
        P("sections", None, None),
    )
    return jax.shard_map(
        local,
        mesh=mesh,
        in_specs=placed,
        out_specs=(
            P(("groups", "sections"), "chan", None),
            P(("groups", "sections"), None, None, None, "chan"),
            P(("groups", "sections"), None, "chan"),
            P(("groups", "sections"), None, "chan"),
            P(("groups", "sections"), None, "chan"),
        ),
        check_vma=False,
    )
```

```python
import functools

import jax
import jax.numpy as jnp
from jax import lax
from jax.sharding import PartitionSpec as P

ROW_AXES = ("tiles", "chan")


def halo_rows(block):
    count = lax.axis_size(ROW_AXES)
    forward = [(i, i + 1) for i in range(count - 1)]
    backward = [(target, source) for source, target in forward]
    low = lax.ppermute(block[:, -1:], ROW_AXES, forward)
    high = lax.ppermute(block[:, :1], ROW_AXES, backward)
    return jnp.concatenate([low, block, high], axis=1)


def grid_taps(extended, height, breadth, mirrored):
    padded = jnp.pad(extended, ((0, 0), (0, 0), (1, 1), (0, 0)))
    tap_list = []
    for shift_row in range(3):
        for shift_col in range(3):
            if mirrored:
                start_row = 2 - shift_row
                start_col = 2 - shift_col
            else:
                start_row = shift_row
                start_col = shift_col
            tap_list.append(
                padded[:, start_row : start_row + height, start_col : start_col + breadth]
            )
    stacked = jnp.concatenate(tap_list, axis=3)
    return stacked.reshape(extended.shape[0] * height * breadth, stacked.shape[3])


def gather_blocks(half, chan_axis, chain, position, chan_index):
    received = [
        lax.ppermute(half, "sections", [(i, (i + k) % chain) for i in range(chain)])
        for k in range(1, chain)
    ]
    stacked = jnp.stack([half] + received)
    if chan_axis is not None:
        other = lax.ppermute(stacked, "chan", [(0, 1), (1, 0)])
        stacked = jnp.where(
            chan_index == 0,
            jnp.concatenate([stacked, other], axis=chan_axis + 1),
            jnp.concatenate([other, stacked], axis=chan_axis + 1),
        )
    return [
        lax.dynamic_index_in_dim(stacked, (position - b + chain) % chain, 0, keepdims=False)
        for b in range(chain)
    ]


def halves_major(term, split_axis):
    shape = term.shape
    parts = shape[:split_axis] + (2, shape[split_axis] // 2) + shape[split_axis + 1 :]
    order = (split_axis,) + tuple(i for i in range(len(parts)) if i != split_axis)
    return term.reshape(parts).transpose(order)


def early_pieces(hidden_ext, hidden_two, spatial_out, grad_block, masked_two, grad_two, cells, height, breadth):
    full = grad_block.shape[-1]
    inner = hidden_two.shape[-1]
    expand_term = jnp.dot(
        hidden_two.reshape(cells, inner).T,
        grad_block.reshape(cells, full),
        preferred_element_type=jnp.float32,
    ).astype(jnp.bfloat16)
    spatial_term = jnp.dot(
        grid_taps(hidden_ext, height, breadth, False).T,
        grad_two.reshape(cells, inner),
        preferred_element_type=jnp.float32,
    ).astype(jnp.bfloat16)
    gain_two = jnp.sum(masked_two * spatial_out, axis=(0, 1, 2))
    bias_two = jnp.sum(masked_two, axis=(0, 1, 2))
    small = jnp.stack([gain_two, bias_two]).astype(jnp.bfloat16)
    spatial_small = jnp.concatenate([spatial_term, small], axis=0)
    return halves_major(expand_term, 1), halves_major(spatial_small, 1)


def late_piece(block_in, reduced, masked_one, grad_one, cells):
    full = block_in.shape[-1]
    inner = grad_one.shape[-1]
    reduce_term = jnp.dot(
        block_in.reshape(cells, full).T,
        grad_one.reshape(cells, inner),
        preferred_element_type=jnp.float32,
    ).astype(jnp.bfloat16)
    gain_one = jnp.sum(masked_one * reduced, axis=(0, 1, 2))
    bias_one = jnp.sum(masked_one, axis=(0, 1, 2))
    small = jnp.stack([gain_one, bias_one]).astype(jnp.bfloat16)
    small_halves = halves_major(small, 1).reshape(2, 1, inner)
    return jnp.concatenate([reduce_term.reshape(2, full // 2, inner), small_halves], axis=1)


def pair_piece(piece, chan_index):
    mine = lax.dynamic_index_in_dim(piece, chan_index, 0, keepdims=False)
    theirs = lax.dynamic_index_in_dim(piece, 1 - chan_index, 0, keepdims=False)
    arrived = lax.ppermute(theirs, "chan", [(0, 1), (1, 0)])
    return (mine.astype(jnp.float32) + arrived.astype(jnp.float32)).astype(jnp.bfloat16)


def local(
    features,
    tissue,
    row_label,
    prototypes,
    reduce_weight,
    spatial_weight,
    expand_weight,
    norm_gain,
    norm_bias,
):
    regions, height, breadth, full_width = features.shape
    chain = lax.axis_size("sections")
    position = lax.axis_index("sections")
    chan_index = lax.axis_index("chan")
    reduce_all = gather_blocks(reduce_weight[0], 0, chain, position, chan_index)
    spatial_all = gather_blocks(spatial_weight[0], 3, chain, position, chan_index)
    expand_all = gather_blocks(expand_weight[0], 1, chain, position, chan_index)
    gain_all = gather_blocks(norm_gain[0], None, chain, position, chan_index)
    bias_all = gather_blocks(norm_bias[0], None, chain, position, chan_index)
    inner_width = reduce_all[0].shape[1]
    tissue_mask = tissue.astype(jnp.float32)[:, :, :, None]
    cells = regions * height * breadth
    inner_shape = (regions, height, breadth, inner_width)
    outer_shape = (regions, height, breadth, full_width)

    current = features
    saved = []
    for b in range(chain):
        gain_pair, bias_pair = gain_all[b], bias_all[b]
        reduced = jnp.dot(
            current.reshape(cells, full_width), reduce_all[b], preferred_element_type=jnp.float32
        ).reshape(inner_shape)
        pre_reduce = gain_pair[0] * reduced + bias_pair[0]
        hidden_one = jnp.maximum(pre_reduce, 0.0).astype(jnp.bfloat16)
        hidden_ext = halo_rows(hidden_one)
        spatial_out = jnp.dot(
            grid_taps(hidden_ext, height, breadth, False),
            spatial_all[b].reshape(9 * inner_width, inner_width),
            preferred_element_type=jnp.float32,
        ).reshape(inner_shape)
        pre_spatial = gain_pair[1] * spatial_out + bias_pair[1]
        hidden_two = jnp.maximum(pre_spatial, 0.0).astype(jnp.bfloat16)
        expanded = jnp.dot(
            hidden_two.reshape(cells, inner_width), expand_all[b], preferred_element_type=jnp.float32
        ).reshape(outer_shape)
        block_out = (
            tissue_mask * jnp.maximum(current.astype(jnp.float32) + expanded, 0.0)
        ).astype(jnp.bfloat16)
        saved.append((current, hidden_ext, reduced, pre_reduce, spatial_out, pre_spatial, hidden_two, block_out))
        current = block_out

    classes = prototypes.shape[0]
    chosen = (row_label[:, :, None] == jnp.arange(classes, dtype=jnp.int32)).astype(jnp.float32)
    target_rows = jnp.einsum("mrk,kc->mrc", chosen, prototypes.astype(jnp.float32))
    total_cells = regions * height * lax.axis_size("tiles") * lax.axis_size("chan") * breadth
    upstream = (
        tissue_mask * (current.astype(jnp.float32) - target_rows[:, :, None, :]) / total_cells
    ).astype(jnp.bfloat16)

    early_sum = None
    late_sum = None
    for b in reversed(range(chain)):
        block_in, hidden_ext, reduced, pre_reduce, spatial_out, pre_spatial, hidden_two, block_out = saved[b]
        needed = b >= position
        gain_pair = gain_all[b]

        def first_back(upstream=upstream, block_out=block_out, pre_spatial=pre_spatial, b=b, gain_pair=gain_pair):
            grad_block = jnp.where(block_out > 0, upstream, jnp.zeros_like(upstream))
            back_two = jnp.dot(
                grad_block.reshape(cells, full_width), expand_all[b].T, preferred_element_type=jnp.float32
            ).reshape(inner_shape)
            masked_two = jnp.where(pre_spatial > 0, back_two, jnp.float32(0.0))
            grad_two = (masked_two * gain_pair[1]).astype(jnp.bfloat16)
            return grad_block, masked_two, grad_two

        def first_skip():
            return (
                jnp.zeros(outer_shape, jnp.bfloat16),
                jnp.zeros(inner_shape, jnp.float32),
                jnp.zeros(inner_shape, jnp.bfloat16),
            )

        grad_block, masked_two, grad_two = lax.cond(needed, first_back, first_skip)
        own = b == position
        early = lax.cond(
            own,
            functools.partial(
                early_pieces, hidden_ext, hidden_two, spatial_out, grad_block, masked_two, grad_two,
                cells, height, breadth,
            ),
            lambda: (
                jnp.zeros((2, inner_width, full_width // 2), jnp.bfloat16),
                jnp.zeros((2, 9 * inner_width + 2, inner_width // 2), jnp.bfloat16),
            ),
        )
        early_sum = early if early_sum is None else tuple(x + y for x, y in zip(early_sum, early))
        grad_ext = halo_rows(grad_two)

        def second_back(grad_ext=grad_ext, pre_reduce=pre_reduce, b=b, gain_pair=gain_pair):
            back_one = jnp.dot(
                grid_taps(grad_ext, height, breadth, True),
                jnp.transpose(spatial_all[b], (0, 1, 3, 2)).reshape(9 * inner_width, inner_width),
                preferred_element_type=jnp.float32,
            ).reshape(inner_shape)
            masked_one = jnp.where(pre_reduce > 0, back_one, jnp.float32(0.0))
            grad_one = (masked_one * gain_pair[0]).astype(jnp.bfloat16)
            return masked_one, grad_one

        def second_skip():
            return (jnp.zeros(inner_shape, jnp.float32), jnp.zeros(inner_shape, jnp.bfloat16))

        masked_one, grad_one = lax.cond(needed, second_back, second_skip)
        late = lax.cond(
            own,
            functools.partial(late_piece, block_in, reduced, masked_one, grad_one, cells),
            lambda: jnp.zeros((2, full_width // 2 + 1, inner_width), jnp.bfloat16),
        )
        late_sum = late if late_sum is None else late_sum + late
        if b > 0:

            def pass_back(grad_block=grad_block, grad_one=grad_one, b=b):
                return (
                    grad_block.astype(jnp.float32)
                    + jnp.dot(
                        grad_one.reshape(cells, inner_width),
                        reduce_all[b].T,
                        preferred_element_type=jnp.float32,
                    ).reshape(outer_shape)
                ).astype(jnp.bfloat16)

            upstream = lax.cond(
                b > position, pass_back, lambda: jnp.zeros(outer_shape, jnp.bfloat16)
            )

    expand_total, spatial_total = lax.psum(
        (pair_piece(early_sum[0], chan_index), pair_piece(early_sum[1], chan_index)), "tiles"
    )
    late_pair, expand_total, spatial_total = lax.optimization_barrier(
        (pair_piece(late_sum, chan_index), expand_total, spatial_total)
    )
    reduce_total = lax.psum(late_pair, "tiles")
    half_full = full_width // 2
    half_inner = inner_width // 2
    grad_reduce = reduce_total[:half_full][None]
    grad_spatial = spatial_total[: 9 * inner_width].reshape(3, 3, inner_width, half_inner)[None]
    grad_expand = expand_total[None]
    first_small = reduce_total[half_full].astype(jnp.float32).reshape(2, half_inner)
    second_small = spatial_total[9 * inner_width :].astype(jnp.float32)
    grad_gain = jnp.stack([first_small[0], second_small[0]])[None]
    grad_bias = jnp.stack([first_small[1], second_small[1]])[None]
    return (grad_reduce, grad_spatial, grad_expand, grad_gain, grad_bias)


def solution(mesh):
    placed = (
        P("groups", ("tiles", "chan"), None, None),
        P("groups", ("tiles", "chan"), None),
        P("groups", ("tiles", "chan")),
        P(),
        P("sections", "chan", None),
        P("sections", None, None, None, "chan"),
        P("sections", None, "chan"),
        P("sections", None, None),
        P("sections", None, None),
    )
    return jax.shard_map(
        local,
        mesh=mesh,
        in_specs=placed,
        out_specs=(
            P(("groups", "sections"), "chan", None),
            P(("groups", "sections"), None, None, None, "chan"),
            P(("groups", "sections"), None, "chan"),
            P(("groups", "sections"), None, "chan"),
            P(("groups", "sections"), None, "chan"),
        ),
        check_vma=False,
    )
```

```python
import functools

import jax
import jax.numpy as jnp
from jax import lax
from jax.sharding import PartitionSpec as P

ROW_AXES = ("tiles", "chan")


def halo_rows(block):
    count = lax.axis_size(ROW_AXES)
    forward = [(i, i + 1) for i in range(count - 1)]
    backward = [(target, source) for source, target in forward]
    low = lax.ppermute(block[:, -1:], ROW_AXES, forward)
    high = lax.ppermute(block[:, :1], ROW_AXES, backward)
    return jnp.concatenate([low, block, high], axis=1)


def grid_taps(extended, height, breadth, mirrored):
    padded = jnp.pad(extended, ((0, 0), (0, 0), (1, 1), (0, 0)))
    tap_list = []
    for shift_row in range(3):
        for shift_col in range(3):
            if mirrored:
                start_row = 2 - shift_row
                start_col = 2 - shift_col
            else:
                start_row = shift_row
                start_col = shift_col
            tap_list.append(
                padded[:, start_row : start_row + height, start_col : start_col + breadth]
            )
    stacked = jnp.concatenate(tap_list, axis=3)
    return stacked.reshape(extended.shape[0] * height * breadth, stacked.shape[3])


def gather_blocks(half, chan_axis, chain, position, chan_index):
    received = [
        lax.ppermute(half, "sections", [(i, (i + k) % chain) for i in range(chain)])
        for k in range(1, chain)
    ]
    stacked = jnp.stack([half] + received)
    if chan_axis is not None:
        other = lax.ppermute(stacked, "chan", [(0, 1), (1, 0)])
        stacked = jnp.where(
            chan_index == 0,
            jnp.concatenate([stacked, other], axis=chan_axis + 1),
            jnp.concatenate([other, stacked], axis=chan_axis + 1),
        )
    return [
        lax.dynamic_index_in_dim(stacked, (position - b + chain) % chain, 0, keepdims=False)
        for b in range(chain)
    ]


def weight_partials(ops, cells, height, breadth):
    cur, h1e, h2, reduced, spatial_out, grad_block, masked_two, grad_two, masked_one, grad_one = ops
    full = cur.shape[-1]
    inner = h2.shape[-1]
    block_flat = grad_block.reshape(cells, full)
    two_flat = grad_two.reshape(cells, inner)
    one_flat = grad_one.reshape(cells, inner)
    reduce_term = jnp.dot(
        cur.reshape(cells, full).T, one_flat, preferred_element_type=jnp.float32
    ).astype(jnp.bfloat16)
    spatial_term = jnp.dot(
        grid_taps(h1e, height, breadth, False).T, two_flat, preferred_element_type=jnp.float32
    ).astype(jnp.bfloat16)
    expand_term = jnp.dot(
        h2.reshape(cells, inner).T, block_flat, preferred_element_type=jnp.float32
    ).astype(jnp.bfloat16)
    gain = jnp.stack(
        [jnp.sum(masked_one * reduced, axis=(0, 1, 2)), jnp.sum(masked_two * spatial_out, axis=(0, 1, 2))]
    )
    bias = jnp.stack([jnp.sum(masked_one, axis=(0, 1, 2)), jnp.sum(masked_two, axis=(0, 1, 2))])
    small = jnp.concatenate([gain, bias]).astype(jnp.bfloat16)
    spatial_small = jnp.concatenate([spatial_term, small], axis=0)
    return (
        reduce_term.reshape(2, full // 2, inner),
        spatial_small.reshape(9 * inner + 4, 2, inner // 2).transpose(1, 0, 2),
        expand_term.reshape(inner, 2, full // 2).transpose(1, 0, 2),
    )


def local(
    features,
    tissue,
    row_label,
    prototypes,
    reduce_weight,
    spatial_weight,
    expand_weight,
    norm_gain,
    norm_bias,
):
    regions, height, breadth, full_width = features.shape
    chain = lax.axis_size("sections")
    position = lax.axis_index("sections")
    chan_index = lax.axis_index("chan")
    reduce_all = gather_blocks(reduce_weight[0], 0, chain, position, chan_index)
    spatial_all = gather_blocks(spatial_weight[0], 3, chain, position, chan_index)
    expand_all = gather_blocks(expand_weight[0], 1, chain, position, chan_index)
    gain_all = gather_blocks(norm_gain[0], None, chain, position, chan_index)
    bias_all = gather_blocks(norm_bias[0], None, chain, position, chan_index)
    inner_width = reduce_all[0].shape[1]
    tissue_mask = tissue.astype(jnp.float32)[:, :, :, None]
    cells = regions * height * breadth
    inner_shape = (regions, height, breadth, inner_width)
    outer_shape = (regions, height, breadth, full_width)

    current = features
    saved = []
    for b in range(chain):
        gain_pair, bias_pair = gain_all[b], bias_all[b]
        reduced = jnp.dot(
            current.reshape(cells, full_width), reduce_all[b], preferred_element_type=jnp.float32
        ).reshape(inner_shape)
        pre_reduce = gain_pair[0] * reduced + bias_pair[0]
        hidden_one = jnp.maximum(pre_reduce, 0.0).astype(jnp.bfloat16)
        hidden_ext = halo_rows(hidden_one)
        spatial_out = jnp.dot(
            grid_taps(hidden_ext, height, breadth, False),
            spatial_all[b].reshape(9 * inner_width, inner_width),
            preferred_element_type=jnp.float32,
        ).reshape(inner_shape)
        pre_spatial = gain_pair[1] * spatial_out + bias_pair[1]
        hidden_two = jnp.maximum(pre_spatial, 0.0).astype(jnp.bfloat16)
        expanded = jnp.dot(
            hidden_two.reshape(cells, inner_width), expand_all[b], preferred_element_type=jnp.float32
        ).reshape(outer_shape)
        block_out = (
            tissue_mask * jnp.maximum(current.astype(jnp.float32) + expanded, 0.0)
        ).astype(jnp.bfloat16)
        saved.append((current, hidden_ext, reduced, pre_reduce, spatial_out, pre_spatial, hidden_two, block_out))
        current = block_out

    classes = prototypes.shape[0]
    chosen = (row_label[:, :, None] == jnp.arange(classes, dtype=jnp.int32)).astype(jnp.float32)
    target_rows = jnp.einsum("mrk,kc->mrc", chosen, prototypes.astype(jnp.float32))
    total_cells = regions * height * lax.axis_size("tiles") * lax.axis_size("chan") * breadth
    upstream = (
        tissue_mask * (current.astype(jnp.float32) - target_rows[:, :, None, :]) / total_cells
    ).astype(jnp.bfloat16)

    block_ops = [None] * chain
    for b in reversed(range(chain)):
        block_in, hidden_ext, reduced, pre_reduce, spatial_out, pre_spatial, hidden_two, block_out = saved[b]
        needed = b >= position
        gain_pair = gain_all[b]

        def first_back(upstream=upstream, block_out=block_out, pre_spatial=pre_spatial, b=b, gain_pair=gain_pair):
            grad_block = jnp.where(block_out > 0, upstream, jnp.zeros_like(upstream))
            back_two = jnp.dot(
                grad_block.reshape(cells, full_width), expand_all[b].T, preferred_element_type=jnp.float32
            ).reshape(inner_shape)
            masked_two = jnp.where(pre_spatial > 0, back_two, jnp.float32(0.0))
            grad_two = (masked_two * gain_pair[1]).astype(jnp.bfloat16)
            return grad_block, masked_two, grad_two

        def first_skip():
            return (
                jnp.zeros(outer_shape, jnp.bfloat16),
                jnp.zeros(inner_shape, jnp.float32),
                jnp.zeros(inner_shape, jnp.bfloat16),
            )

        grad_block, masked_two, grad_two = lax.cond(needed, first_back, first_skip)
        grad_ext = halo_rows(grad_two)

        def second_back(grad_ext=grad_ext, pre_reduce=pre_reduce, b=b, gain_pair=gain_pair):
            back_one = jnp.dot(
                grid_taps(grad_ext, height, breadth, True),
                jnp.transpose(spatial_all[b], (0, 1, 3, 2)).reshape(9 * inner_width, inner_width),
                preferred_element_type=jnp.float32,
            ).reshape(inner_shape)
            masked_one = jnp.where(pre_reduce > 0, back_one, jnp.float32(0.0))
            grad_one = (masked_one * gain_pair[0]).astype(jnp.bfloat16)
            return masked_one, grad_one

        def second_skip():
            return (jnp.zeros(inner_shape, jnp.float32), jnp.zeros(inner_shape, jnp.bfloat16))

        masked_one, grad_one = lax.cond(needed, second_back, second_skip)
        block_ops[b] = (
            block_in, hidden_ext, hidden_two, reduced, spatial_out,
            grad_block, masked_two, grad_two, masked_one, grad_one,
        )
        if b > 0:

            def pass_back(grad_block=grad_block, grad_one=grad_one, b=b):
                return (
                    grad_block.astype(jnp.float32)
                    + jnp.dot(
                        grad_one.reshape(cells, inner_width),
                        reduce_all[b].T,
                        preferred_element_type=jnp.float32,
                    ).reshape(outer_shape)
                ).astype(jnp.bfloat16)

            upstream = lax.cond(
                b > position, pass_back, lambda: jnp.zeros(outer_shape, jnp.bfloat16)
            )

    partials = lax.switch(
        position,
        [
            functools.partial(
                lambda k: weight_partials(block_ops[k], cells, height, breadth), k
            )
            for k in range(chain)
        ],
    )
    tile_count = lax.axis_size("tiles")
    lanes = 128
    flat = [piece.reshape(2, -1, lanes) for piece in partials]
    piece_rows = [piece.shape[1] for piece in flat]
    joined = jnp.concatenate(flat, axis=1)
    rows = joined.shape[1]
    spare = (-rows) % tile_count
    joined = jnp.pad(joined, ((0, 0), (0, spare), (0, 0)))
    quarter = (rows + spare) // tile_count
    joined = joined.reshape(2, tile_count, quarter, lanes).transpose(1, 0, 2, 3)
    joined = joined.reshape(2 * tile_count, quarter, lanes)
    scattered = lax.psum_scatter(joined, ROW_AXES, scatter_dimension=0, tiled=True)
    gathered = lax.all_gather(scattered, "tiles", axis=0, tiled=True)
    total = gathered.reshape(tile_count * quarter, lanes)
    offsets = [0]
    for count in piece_rows:
        offsets.append(offsets[-1] + count)
    totals = [total[offsets[i] : offsets[i + 1]] for i in range(len(piece_rows))]
    half_full = full_width // 2
    half_inner = inner_width // 2
    grad_reduce = totals[0].reshape(half_full, inner_width)[None]
    spatial_small = totals[1].reshape(9 * inner_width + 4, half_inner)
    grad_spatial = spatial_small[: 9 * inner_width].reshape(3, 3, inner_width, half_inner)[None]
    grad_expand = totals[2].reshape(inner_width, half_full)[None]
    small = spatial_small[9 * inner_width :].astype(jnp.float32)
    return (grad_reduce, grad_spatial, grad_expand, small[0:2][None], small[2:4][None])


def solution(mesh):
    placed = (
        P("groups", ("tiles", "chan"), None, None),
        P("groups", ("tiles", "chan"), None),
        P("groups", ("tiles", "chan")),
        P(),
        P("sections", "chan", None),
        P("sections", None, None, None, "chan"),
        P("sections", None, "chan"),
        P("sections", None, None),
        P("sections", None, None),
    )
    return jax.shard_map(
        local,
        mesh=mesh,
        in_specs=placed,
        out_specs=(
            P(("groups", "sections"), "chan", None),
            P(("groups", "sections"), None, None, None, "chan"),
            P(("groups", "sections"), None, "chan"),
            P(("groups", "sections"), None, "chan"),
            P(("groups", "sections"), None, "chan"),
        ),
        check_vma=False,
    )
```

```python
import functools

import jax
import jax.numpy as jnp
from jax import lax
from jax.sharding import PartitionSpec as P

ROW_AXES = ("tiles", "chan")


def halo_rows(block):
    count = lax.axis_size(ROW_AXES)
    forward = [(i, i + 1) for i in range(count - 1)]
    backward = [(target, source) for source, target in forward]
    low = lax.ppermute(block[:, -1:], ROW_AXES, forward)
    high = lax.ppermute(block[:, :1], ROW_AXES, backward)
    return jnp.concatenate([low, block, high], axis=1)


def grid_taps(extended, height, breadth, mirrored):
    padded = jnp.pad(extended, ((0, 0), (0, 0), (1, 1), (0, 0)))
    tap_list = []
    for shift_row in range(3):
        for shift_col in range(3):
            if mirrored:
                start_row = 2 - shift_row
                start_col = 2 - shift_col
            else:
                start_row = shift_row
                start_col = shift_col
            tap_list.append(
                padded[:, start_row : start_row + height, start_col : start_col + breadth]
            )
    stacked = jnp.concatenate(tap_list, axis=3)
    return stacked.reshape(extended.shape[0] * height * breadth, stacked.shape[3])


def gather_blocks(half, chan_axis, chain, position, chan_index):
    received = [
        lax.ppermute(half, "sections", [(i, (i + k) % chain) for i in range(chain)])
        for k in range(1, chain)
    ]
    stacked = jnp.stack([half] + received)
    if chan_axis is not None:
        other = lax.ppermute(stacked, "chan", [(0, 1), (1, 0)])
        stacked = jnp.where(
            chan_index == 0,
            jnp.concatenate([stacked, other], axis=chan_axis + 1),
            jnp.concatenate([other, stacked], axis=chan_axis + 1),
        )
    return [
        lax.dynamic_index_in_dim(stacked, (position - b + chain) % chain, 0, keepdims=False)
        for b in range(chain)
    ]


def weight_halves(ops, cells, height, breadth, half_index):
    cur, h1e, h2, reduced, spatial_out, grad_block, masked_two, grad_two, masked_one, grad_one = ops
    full = cur.shape[-1]
    inner = h2.shape[-1]
    half_full = full // 2
    half_inner = inner // 2
    cur_half = lax.dynamic_slice_in_dim(cur.reshape(cells, full), half_index * half_full, half_full, 1)
    block_half = lax.dynamic_slice_in_dim(
        grad_block.reshape(cells, full), half_index * half_full, half_full, 1
    )
    two_half = lax.dynamic_slice_in_dim(
        grad_two.reshape(cells, inner), half_index * half_inner, half_inner, 1
    )
    reduce_term = jnp.dot(cur_half.T, grad_one.reshape(cells, inner), preferred_element_type=jnp.float32)
    spatial_term = jnp.dot(
        grid_taps(h1e, height, breadth, False).T, two_half, preferred_element_type=jnp.float32
    )
    expand_term = jnp.dot(h2.reshape(cells, inner).T, block_half, preferred_element_type=jnp.float32)
    small = jnp.stack(
        [
            jnp.sum(masked_one * reduced, axis=(0, 1, 2)),
            jnp.sum(masked_two * spatial_out, axis=(0, 1, 2)),
            jnp.sum(masked_one, axis=(0, 1, 2)),
            jnp.sum(masked_two, axis=(0, 1, 2)),
        ]
    )
    small = lax.dynamic_slice_in_dim(small, half_index * half_inner, half_inner, 1)
    small_rows = jnp.pad(small, ((0, 8 - small.shape[0]), (0, 0)))
    spatial_small = jnp.concatenate([spatial_term, small_rows], axis=0)
    return tuple(piece.astype(jnp.bfloat16) for piece in (reduce_term, spatial_small, expand_term))


def weight_pair(ops, cells, height, breadth, chan_index):
    theirs = weight_halves(ops, cells, height, breadth, 1 - chan_index)
    mine = weight_halves(ops, cells, height, breadth, chan_index)
    return theirs + mine


def local(
    features,
    tissue,
    row_label,
    prototypes,
    reduce_weight,
    spatial_weight,
    expand_weight,
    norm_gain,
    norm_bias,
):
    regions, height, breadth, full_width = features.shape
    chain = lax.axis_size("sections")
    position = lax.axis_index("sections")
    chan_index = lax.axis_index("chan")
    reduce_all = gather_blocks(reduce_weight[0], 0, chain, position, chan_index)
    spatial_all = gather_blocks(spatial_weight[0], 3, chain, position, chan_index)
    expand_all = gather_blocks(expand_weight[0], 1, chain, position, chan_index)
    gain_all = gather_blocks(norm_gain[0], None, chain, position, chan_index)
    bias_all = gather_blocks(norm_bias[0], None, chain, position, chan_index)
    inner_width = reduce_all[0].shape[1]
    tissue_mask = tissue.astype(jnp.float32)[:, :, :, None]
    cells = regions * height * breadth
    inner_shape = (regions, height, breadth, inner_width)
    outer_shape = (regions, height, breadth, full_width)

    current = features
    saved = []
    for b in range(chain):
        gain_pair, bias_pair = gain_all[b], bias_all[b]
        reduced = jnp.dot(
            current.reshape(cells, full_width), reduce_all[b], preferred_element_type=jnp.float32
        ).reshape(inner_shape)
        pre_reduce = gain_pair[0] * reduced + bias_pair[0]
        hidden_one = jnp.maximum(pre_reduce, 0.0).astype(jnp.bfloat16)
        hidden_ext = halo_rows(hidden_one)
        spatial_out = jnp.dot(
            grid_taps(hidden_ext, height, breadth, False),
            spatial_all[b].reshape(9 * inner_width, inner_width),
            preferred_element_type=jnp.float32,
        ).reshape(inner_shape)
        pre_spatial = gain_pair[1] * spatial_out + bias_pair[1]
        hidden_two = jnp.maximum(pre_spatial, 0.0).astype(jnp.bfloat16)
        expanded = jnp.dot(
            hidden_two.reshape(cells, inner_width), expand_all[b], preferred_element_type=jnp.float32
        ).reshape(outer_shape)
        block_out = (
            tissue_mask * jnp.maximum(current.astype(jnp.float32) + expanded, 0.0)
        ).astype(jnp.bfloat16)
        saved.append((current, hidden_ext, reduced, pre_reduce, spatial_out, pre_spatial, hidden_two, block_out))
        current = block_out

    classes = prototypes.shape[0]
    chosen = (row_label[:, :, None] == jnp.arange(classes, dtype=jnp.int32)).astype(jnp.float32)
    target_rows = jnp.einsum("mrk,kc->mrc", chosen, prototypes.astype(jnp.float32))
    total_cells = regions * height * lax.axis_size("tiles") * lax.axis_size("chan") * breadth
    upstream = (
        tissue_mask * (current.astype(jnp.float32) - target_rows[:, :, None, :]) / total_cells
    ).astype(jnp.bfloat16)

    block_ops = [None] * chain
    for b in reversed(range(chain)):
        block_in, hidden_ext, reduced, pre_reduce, spatial_out, pre_spatial, hidden_two, block_out = saved[b]
        needed = b >= position
        gain_pair = gain_all[b]

        def first_back(upstream=upstream, block_out=block_out, pre_spatial=pre_spatial, b=b, gain_pair=gain_pair):
            grad_block = jnp.where(block_out > 0, upstream, jnp.zeros_like(upstream))
            back_two = jnp.dot(
                grad_block.reshape(cells, full_width), expand_all[b].T, preferred_element_type=jnp.float32
            ).reshape(inner_shape)
            masked_two = jnp.where(pre_spatial > 0, back_two, jnp.float32(0.0))
            grad_two = (masked_two * gain_pair[1]).astype(jnp.bfloat16)
            return grad_block, masked_two, grad_two

        def first_skip():
            return (
                jnp.zeros(outer_shape, jnp.bfloat16),
                jnp.zeros(inner_shape, jnp.float32),
                jnp.zeros(inner_shape, jnp.bfloat16),
            )

        grad_block, masked_two, grad_two = lax.cond(needed, first_back, first_skip)
        grad_ext = halo_rows(grad_two)

        def second_back(grad_ext=grad_ext, pre_reduce=pre_reduce, b=b, gain_pair=gain_pair):
            back_one = jnp.dot(
                grid_taps(grad_ext, height, breadth, True),
                jnp.transpose(spatial_all[b], (0, 1, 3, 2)).reshape(9 * inner_width, inner_width),
                preferred_element_type=jnp.float32,
            ).reshape(inner_shape)
            masked_one = jnp.where(pre_reduce > 0, back_one, jnp.float32(0.0))
            grad_one = (masked_one * gain_pair[0]).astype(jnp.bfloat16)
            return masked_one, grad_one

        def second_skip():
            return (jnp.zeros(inner_shape, jnp.float32), jnp.zeros(inner_shape, jnp.bfloat16))

        masked_one, grad_one = lax.cond(needed, second_back, second_skip)
        block_ops[b] = (
            block_in, hidden_ext, hidden_two, reduced, spatial_out,
            grad_block, masked_two, grad_two, masked_one, grad_one,
        )
        if b > 0:

            def pass_back(grad_block=grad_block, grad_one=grad_one, b=b):
                return (
                    grad_block.astype(jnp.float32)
                    + jnp.dot(
                        grad_one.reshape(cells, inner_width),
                        reduce_all[b].T,
                        preferred_element_type=jnp.float32,
                    ).reshape(outer_shape)
                ).astype(jnp.bfloat16)

            upstream = lax.cond(
                b > position, pass_back, lambda: jnp.zeros(outer_shape, jnp.bfloat16)
            )

    pieces = lax.switch(
        position,
        [
            functools.partial(
                lambda k: weight_pair(block_ops[k], cells, height, breadth, chan_index), k
            )
            for k in range(chain)
        ],
    )
    theirs, mine = pieces[:3], pieces[3:]
    pair_sums = []
    for own_piece, other_piece in zip(mine, theirs):
        arrived = lax.ppermute(other_piece, "chan", [(0, 1), (1, 0)])
        pair_sums.append(
            (own_piece.astype(jnp.float32) + arrived.astype(jnp.float32)).astype(jnp.bfloat16)
        )
    totals = lax.psum(tuple(pair_sums), "tiles")
    half_inner = inner_width // 2
    grad_reduce = totals[0][None]
    grad_spatial = totals[1][: 9 * inner_width].reshape(3, 3, inner_width, half_inner)[None]
    grad_expand = totals[2][None]
    small = totals[1][9 * inner_width : 9 * inner_width + 4].astype(jnp.float32)
    return (grad_reduce, grad_spatial, grad_expand, small[0:2][None], small[2:4][None])


def solution(mesh):
    placed = (
        P("groups", ("tiles", "chan"), None, None),
        P("groups", ("tiles", "chan"), None),
        P("groups", ("tiles", "chan")),
        P(),
        P("sections", "chan", None),
        P("sections", None, None, None, "chan"),
        P("sections", None, "chan"),
        P("sections", None, None),
        P("sections", None, None),
    )
    return jax.shard_map(
        local,
        mesh=mesh,
        in_specs=placed,
        out_specs=(
            P(("groups", "sections"), "chan", None),
            P(("groups", "sections"), None, None, None, "chan"),
            P(("groups", "sections"), None, "chan"),
            P(("groups", "sections"), None, "chan"),
            P(("groups", "sections"), None, "chan"),
        ),
        check_vma=False,
    )
```

```python
import functools

import jax
import jax.numpy as jnp
from jax import lax
from jax.sharding import PartitionSpec as P

ROW_AXES = ("tiles", "chan")


def halo_rows(block):
    count = lax.axis_size(ROW_AXES)
    forward = [(i, i + 1) for i in range(count - 1)]
    backward = [(target, source) for source, target in forward]
    low = lax.ppermute(block[:, -1:], ROW_AXES, forward)
    high = lax.ppermute(block[:, :1], ROW_AXES, backward)
    return jnp.concatenate([low, block, high], axis=1)


def grid_taps(extended, height, breadth, mirrored):
    padded = jnp.pad(extended, ((0, 0), (0, 0), (1, 1), (0, 0)))
    tap_list = []
    for shift_row in range(3):
        for shift_col in range(3):
            if mirrored:
                start_row = 2 - shift_row
                start_col = 2 - shift_col
            else:
                start_row = shift_row
                start_col = shift_col
            tap_list.append(
                padded[:, start_row : start_row + height, start_col : start_col + breadth]
            )
    stacked = jnp.concatenate(tap_list, axis=3)
    return stacked.reshape(extended.shape[0] * height * breadth, stacked.shape[3])


def gather_chan(half, chan_axis, chan_index):
    if chan_axis is None:
        return half
    other = lax.ppermute(half, "chan", [(0, 1), (1, 0)])
    return jnp.where(
        chan_index == 0,
        jnp.concatenate([half, other], axis=chan_axis),
        jnp.concatenate([other, half], axis=chan_axis),
    )


def gather_blocks(half, chan_axis, chain, position, chan_index):
    own_full = gather_chan(half, chan_axis, chan_index)
    received = [
        gather_chan(
            lax.ppermute(half, "sections", [(i, i + k - chain) for i in range(chain - k, chain)]),
            chan_axis,
            chan_index,
        )
        for k in range(1, chain)
    ]
    stacked = jnp.stack([own_full] + received)
    return [own_full] + [
        lax.dynamic_index_in_dim(stacked, (position - b + chain) % chain, 0, keepdims=False)
        for b in range(1, chain)
    ]


def weight_halves(ops, cells, height, breadth, half_index):
    cur, h1e, h2, reduced, spatial_out, grad_block, masked_two, grad_two, masked_one, grad_one = ops
    full = cur.shape[-1]
    inner = h2.shape[-1]
    half_full = full // 2
    half_inner = inner // 2
    cur_half = lax.dynamic_slice_in_dim(cur.reshape(cells, full), half_index * half_full, half_full, 1)
    block_half = lax.dynamic_slice_in_dim(
        grad_block.reshape(cells, full), half_index * half_full, half_full, 1
    )
    two_half = lax.dynamic_slice_in_dim(
        grad_two.reshape(cells, inner), half_index * half_inner, half_inner, 1
    )
    reduce_term = jnp.dot(cur_half.T, grad_one.reshape(cells, inner), preferred_element_type=jnp.float32)
    spatial_term = jnp.dot(
        grid_taps(h1e, height, breadth, False).T, two_half, preferred_element_type=jnp.float32
    )
    expand_term = jnp.dot(h2.reshape(cells, inner).T, block_half, preferred_element_type=jnp.float32)
    small = jnp.stack(
        [
            jnp.sum(masked_one * reduced, axis=(0, 1, 2)),
            jnp.sum(masked_two * spatial_out, axis=(0, 1, 2)),
            jnp.sum(masked_one, axis=(0, 1, 2)),
            jnp.sum(masked_two, axis=(0, 1, 2)),
        ]
    )
    small = lax.dynamic_slice_in_dim(small, half_index * half_inner, half_inner, 1)
    small_rows = jnp.pad(small, ((0, 8 - small.shape[0]), (0, 0)))
    spatial_small = jnp.concatenate([spatial_term, small_rows], axis=0)
    return tuple(piece.astype(jnp.bfloat16) for piece in (reduce_term, spatial_small, expand_term))


def weight_pair(ops, cells, height, breadth, chan_index):
    theirs = weight_halves(ops, cells, height, breadth, 1 - chan_index)
    mine = weight_halves(ops, cells, height, breadth, chan_index)
    return theirs + mine


def local(
    features,
    tissue,
    row_label,
    prototypes,
    reduce_weight,
    spatial_weight,
    expand_weight,
    norm_gain,
    norm_bias,
):
    regions, height, breadth, full_width = features.shape
    chain = lax.axis_size("sections")
    position = lax.axis_index("sections")
    chan_index = lax.axis_index("chan")
    reduce_all = gather_blocks(reduce_weight[0], 0, chain, position, chan_index)
    spatial_all = gather_blocks(spatial_weight[0], 3, chain, position, chan_index)
    expand_all = gather_blocks(expand_weight[0], 1, chain, position, chan_index)
    gain_all = gather_blocks(norm_gain[0], None, chain, position, chan_index)
    bias_all = gather_blocks(norm_bias[0], None, chain, position, chan_index)
    inner_width = reduce_all[0].shape[1]
    tissue_mask = tissue.astype(jnp.float32)[:, :, :, None]
    cells = regions * height * breadth
    inner_shape = (regions, height, breadth, inner_width)
    outer_shape = (regions, height, breadth, full_width)

    current = features
    saved = []
    for b in range(chain):
        gain_pair, bias_pair = gain_all[b], bias_all[b]
        if b > 0:
            handed = lax.ppermute(current, "sections", [(b - 1, b)])
            current = jnp.where(position == b, handed, current)
        reduced = jnp.dot(
            current.reshape(cells, full_width), reduce_all[b], preferred_element_type=jnp.float32
        ).reshape(inner_shape)
        pre_reduce = gain_pair[0] * reduced + bias_pair[0]
        hidden_one = jnp.maximum(pre_reduce, 0.0).astype(jnp.bfloat16)
        hidden_ext = halo_rows(hidden_one)
        spatial_out = jnp.dot(
            grid_taps(hidden_ext, height, breadth, False),
            spatial_all[b].reshape(9 * inner_width, inner_width),
            preferred_element_type=jnp.float32,
        ).reshape(inner_shape)
        pre_spatial = gain_pair[1] * spatial_out + bias_pair[1]
        hidden_two = jnp.maximum(pre_spatial, 0.0).astype(jnp.bfloat16)
        expanded = jnp.dot(
            hidden_two.reshape(cells, inner_width), expand_all[b], preferred_element_type=jnp.float32
        ).reshape(outer_shape)
        block_out = (
            tissue_mask * jnp.maximum(current.astype(jnp.float32) + expanded, 0.0)
        ).astype(jnp.bfloat16)
        saved.append((current, hidden_ext, reduced, pre_reduce, spatial_out, pre_spatial, hidden_two, block_out))
        current = block_out

    classes = prototypes.shape[0]
    chosen = (row_label[:, :, None] == jnp.arange(classes, dtype=jnp.int32)).astype(jnp.float32)
    target_rows = jnp.einsum("mrk,kc->mrc", chosen, prototypes.astype(jnp.float32))
    total_cells = regions * height * lax.axis_size("tiles") * lax.axis_size("chan") * breadth
    upstream = (
        tissue_mask * (current.astype(jnp.float32) - target_rows[:, :, None, :]) / total_cells
    ).astype(jnp.bfloat16)

    block_ops = [None] * chain
    for b in reversed(range(chain)):
        block_in, hidden_ext, reduced, pre_reduce, spatial_out, pre_spatial, hidden_two, block_out = saved[b]
        needed = b >= position
        gain_pair = gain_all[b]

        def first_back(upstream=upstream, block_out=block_out, pre_spatial=pre_spatial, b=b, gain_pair=gain_pair):
            grad_block = jnp.where(block_out > 0, upstream, jnp.zeros_like(upstream))
            back_two = jnp.dot(
                grad_block.reshape(cells, full_width), expand_all[b].T, preferred_element_type=jnp.float32
            ).reshape(inner_shape)
            masked_two = jnp.where(pre_spatial > 0, back_two, jnp.float32(0.0))
            grad_two = (masked_two * gain_pair[1]).astype(jnp.bfloat16)
            return grad_block, masked_two, grad_two

        def first_skip():
            return (
                jnp.zeros(outer_shape, jnp.bfloat16),
                jnp.zeros(inner_shape, jnp.float32),
                jnp.zeros(inner_shape, jnp.bfloat16),
            )

        grad_block, masked_two, grad_two = lax.cond(needed, first_back, first_skip)
        grad_ext = halo_rows(grad_two)

        def second_back(grad_ext=grad_ext, pre_reduce=pre_reduce, b=b, gain_pair=gain_pair):
            back_one = jnp.dot(
                grid_taps(grad_ext, height, breadth, True),
                jnp.transpose(spatial_all[b], (0, 1, 3, 2)).reshape(9 * inner_width, inner_width),
                preferred_element_type=jnp.float32,
            ).reshape(inner_shape)
            masked_one = jnp.where(pre_reduce > 0, back_one, jnp.float32(0.0))
            grad_one = (masked_one * gain_pair[0]).astype(jnp.bfloat16)
            return masked_one, grad_one

        def second_skip():
            return (jnp.zeros(inner_shape, jnp.float32), jnp.zeros(inner_shape, jnp.bfloat16))

        masked_one, grad_one = lax.cond(needed, second_back, second_skip)
        block_ops[b] = (
            block_in, hidden_ext, hidden_two, reduced, spatial_out,
            grad_block, masked_two, grad_two, masked_one, grad_one,
        )
        if b > 0:

            def pass_back(grad_block=grad_block, grad_one=grad_one, b=b):
                return (
                    grad_block.astype(jnp.float32)
                    + jnp.dot(
                        grad_one.reshape(cells, inner_width),
                        reduce_all[b].T,
                        preferred_element_type=jnp.float32,
                    ).reshape(outer_shape)
                ).astype(jnp.bfloat16)

            upstream = lax.cond(
                b > position, pass_back, lambda: jnp.zeros(outer_shape, jnp.bfloat16)
            )

    pieces = lax.switch(
        position,
        [
            functools.partial(
                lambda k: weight_pair(block_ops[k], cells, height, breadth, chan_index), k
            )
            for k in range(chain)
        ],
    )
    theirs, mine = pieces[:3], pieces[3:]
    pair_sums = []
    for own_piece, other_piece in zip(mine, theirs):
        arrived = lax.ppermute(other_piece, "chan", [(0, 1), (1, 0)])
        pair_sums.append(
            (own_piece.astype(jnp.float32) + arrived.astype(jnp.float32)).astype(jnp.bfloat16)
        )
    totals = lax.psum(tuple(pair_sums), "tiles")
    half_inner = inner_width // 2
    grad_reduce = totals[0][None]
    grad_spatial = totals[1][: 9 * inner_width].reshape(3, 3, inner_width, half_inner)[None]
    grad_expand = totals[2][None]
    small = totals[1][9 * inner_width : 9 * inner_width + 4].astype(jnp.float32)
    return (grad_reduce, grad_spatial, grad_expand, small[0:2][None], small[2:4][None])


def solution(mesh):
    placed = (
        P("groups", ("tiles", "chan"), None, None),
        P("groups", ("tiles", "chan"), None),
        P("groups", ("tiles", "chan")),
        P(),
        P("sections", "chan", None),
        P("sections", None, None, None, "chan"),
        P("sections", None, "chan"),
        P("sections", None, None),
        P("sections", None, None),
    )
    return jax.shard_map(
        local,
        mesh=mesh,
        in_specs=placed,
        out_specs=(
            P(("groups", "sections"), "chan", None),
            P(("groups", "sections"), None, None, None, "chan"),
            P(("groups", "sections"), None, "chan"),
            P(("groups", "sections"), None, "chan"),
            P(("groups", "sections"), None, "chan"),
        ),
        check_vma=False,
    )
```

```python
import functools

import jax
import jax.numpy as jnp
from jax import lax
from jax.sharding import PartitionSpec as P

ROW_AXES = ("tiles", "chan")


def halo_rows(block):
    count = lax.axis_size(ROW_AXES)
    forward = [(i, i + 1) for i in range(count - 1)]
    backward = [(target, source) for source, target in forward]
    low = lax.ppermute(block[:, -1:], ROW_AXES, forward)
    high = lax.ppermute(block[:, :1], ROW_AXES, backward)
    return jnp.concatenate([low, block, high], axis=1)


def grid_taps(extended, height, breadth, mirrored):
    padded = jnp.pad(extended, ((0, 0), (0, 0), (1, 1), (0, 0)))
    tap_list = []
    for shift_row in range(3):
        for shift_col in range(3):
            if mirrored:
                start_row = 2 - shift_row
                start_col = 2 - shift_col
            else:
                start_row = shift_row
                start_col = shift_col
            tap_list.append(
                padded[:, start_row : start_row + height, start_col : start_col + breadth]
            )
    stacked = jnp.concatenate(tap_list, axis=3)
    return stacked.reshape(extended.shape[0] * height * breadth, stacked.shape[3])


def gather_blocks(half, chan_axis, chain, position, chan_index):
    received = [
        lax.ppermute(half, "sections", [(i, (i + k) % chain) for i in range(chain)])
        for k in range(1, chain)
    ]
    stacked = jnp.stack([half] + received)
    if chan_axis is not None:
        other = lax.ppermute(stacked, "chan", [(0, 1), (1, 0)])
        stacked = jnp.where(
            chan_index == 0,
            jnp.concatenate([stacked, other], axis=chan_axis + 1),
            jnp.concatenate([other, stacked], axis=chan_axis + 1),
        )
    return [
        lax.dynamic_index_in_dim(stacked, (position - b + chain) % chain, 0, keepdims=False)
        for b in range(chain)
    ]


def weight_halves(ops, taps, small, cells, half_index):
    cur, h1e, h2, reduced, spatial_out, grad_block, masked_two, grad_two, masked_one, grad_one = ops
    full = cur.shape[-1]
    inner = h2.shape[-1]
    half_full = full // 2
    half_inner = inner // 2
    cur_half = lax.dynamic_slice_in_dim(cur.reshape(cells, full), half_index * half_full, half_full, 1)
    block_half = lax.dynamic_slice_in_dim(
        grad_block.reshape(cells, full), half_index * half_full, half_full, 1
    )
    two_half = lax.dynamic_slice_in_dim(
        grad_two.reshape(cells, inner), half_index * half_inner, half_inner, 1
    )
    reduce_term = jnp.dot(cur_half.T, grad_one.reshape(cells, inner), preferred_element_type=jnp.float32)
    spatial_term = jnp.dot(taps.T, two_half, preferred_element_type=jnp.float32)
    expand_term = jnp.dot(h2.reshape(cells, inner).T, block_half, preferred_element_type=jnp.float32)
    small_half = lax.dynamic_slice_in_dim(small, half_index * half_inner, half_inner, 1)
    small_rows = jnp.pad(small_half, ((0, 8 - small_half.shape[0]), (0, 0)))
    spatial_small = jnp.concatenate([spatial_term, small_rows], axis=0)
    return tuple(
        piece.astype(jnp.bfloat16)[None] for piece in (reduce_term, spatial_small, expand_term)
    )


def weight_pair(ops, cells, height, breadth, chan_index):
    cur, h1e, h2, reduced, spatial_out, grad_block, masked_two, grad_two, masked_one, grad_one = ops
    taps = grid_taps(h1e, height, breadth, False)
    small = jnp.stack(
        [
            jnp.sum(masked_one * reduced, axis=(0, 1, 2)),
            jnp.sum(masked_two * spatial_out, axis=(0, 1, 2)),
            jnp.sum(masked_one, axis=(0, 1, 2)),
            jnp.sum(masked_two, axis=(0, 1, 2)),
        ]
    )
    theirs = weight_halves(ops, taps, small, cells, 1 - chan_index)
    mine = weight_halves(ops, taps, small, cells, chan_index)
    return theirs + mine


def local(
    features,
    tissue,
    row_label,
    prototypes,
    reduce_weight,
    spatial_weight,
    expand_weight,
    norm_gain,
    norm_bias,
):
    regions, height, breadth, full_width = features.shape
    chain = lax.axis_size("sections")
    position = lax.axis_index("sections")
    chan_index = lax.axis_index("chan")
    reduce_all = gather_blocks(reduce_weight[0], 0, chain, position, chan_index)
    spatial_all = gather_blocks(spatial_weight[0], 3, chain, position, chan_index)
    expand_all = gather_blocks(expand_weight[0], 1, chain, position, chan_index)
    gain_all = gather_blocks(norm_gain[0], None, chain, position, chan_index)
    bias_all = gather_blocks(norm_bias[0], None, chain, position, chan_index)
    inner_width = reduce_all[0].shape[1]
    tissue_mask = tissue.astype(jnp.float32)[:, :, :, None]
    cells = regions * height * breadth
    inner_shape = (regions, height, breadth, inner_width)
    outer_shape = (regions, height, breadth, full_width)

    current = features
    saved = []
    for b in range(chain):
        gain_pair, bias_pair = gain_all[b], bias_all[b]
        reduced = jnp.dot(
            current.reshape(cells, full_width), reduce_all[b], preferred_element_type=jnp.float32
        ).reshape(inner_shape)
        pre_reduce = gain_pair[0] * reduced + bias_pair[0]
        hidden_one = jnp.maximum(pre_reduce, 0.0).astype(jnp.bfloat16)
        hidden_ext = halo_rows(hidden_one)
        spatial_out = jnp.dot(
            grid_taps(hidden_ext, height, breadth, False),
            spatial_all[b].reshape(9 * inner_width, inner_width),
            preferred_element_type=jnp.float32,
        ).reshape(inner_shape)
        pre_spatial = gain_pair[1] * spatial_out + bias_pair[1]
        hidden_two = jnp.maximum(pre_spatial, 0.0).astype(jnp.bfloat16)
        expanded = jnp.dot(
            hidden_two.reshape(cells, inner_width), expand_all[b], preferred_element_type=jnp.float32
        ).reshape(outer_shape)
        block_out = (
            tissue_mask * jnp.maximum(current.astype(jnp.float32) + expanded, 0.0)
        ).astype(jnp.bfloat16)
        saved.append((current, hidden_ext, reduced, pre_reduce, spatial_out, pre_spatial, hidden_two, block_out))
        current = block_out

    classes = prototypes.shape[0]
    chosen = (row_label[:, :, None] == jnp.arange(classes, dtype=jnp.int32)).astype(jnp.float32)
    target_rows = jnp.einsum("mrk,kc->mrc", chosen, prototypes.astype(jnp.float32))
    total_cells = regions * height * lax.axis_size("tiles") * lax.axis_size("chan") * breadth
    upstream = (
        tissue_mask * (current.astype(jnp.float32) - target_rows[:, :, None, :]) / total_cells
    ).astype(jnp.bfloat16)

    block_ops = [None] * chain
    for b in reversed(range(chain)):
        block_in, hidden_ext, reduced, pre_reduce, spatial_out, pre_spatial, hidden_two, block_out = saved[b]
        needed = b >= position
        gain_pair = gain_all[b]

        def first_back(upstream=upstream, block_out=block_out, pre_spatial=pre_spatial, b=b, gain_pair=gain_pair):
            grad_block = jnp.where(block_out > 0, upstream, jnp.zeros_like(upstream))
            back_two = jnp.dot(
                grad_block.reshape(cells, full_width), expand_all[b].T, preferred_element_type=jnp.float32
            ).reshape(inner_shape)
            masked_two = jnp.where(pre_spatial > 0, back_two, jnp.float32(0.0))
            grad_two = (masked_two * gain_pair[1]).astype(jnp.bfloat16)
            return grad_block, masked_two, grad_two

        def first_skip():
            return (
                jnp.zeros(outer_shape, jnp.bfloat16),
                jnp.zeros(inner_shape, jnp.float32),
                jnp.zeros(inner_shape, jnp.bfloat16),
            )

        grad_block, masked_two, grad_two = lax.cond(needed, first_back, first_skip)
        grad_ext = halo_rows(grad_two)

        def second_back(grad_ext=grad_ext, pre_reduce=pre_reduce, b=b, gain_pair=gain_pair):
            back_one = jnp.dot(
                grid_taps(grad_ext, height, breadth, True),
                jnp.transpose(spatial_all[b], (0, 1, 3, 2)).reshape(9 * inner_width, inner_width),
                preferred_element_type=jnp.float32,
            ).reshape(inner_shape)
            masked_one = jnp.where(pre_reduce > 0, back_one, jnp.float32(0.0))
            grad_one = (masked_one * gain_pair[0]).astype(jnp.bfloat16)
            return masked_one, grad_one

        def second_skip():
            return (jnp.zeros(inner_shape, jnp.float32), jnp.zeros(inner_shape, jnp.bfloat16))

        masked_one, grad_one = lax.cond(needed, second_back, second_skip)
        block_ops[b] = (
            block_in, hidden_ext, hidden_two, reduced, spatial_out,
            grad_block, masked_two, grad_two, masked_one, grad_one,
        )
        if b > 0:

            def pass_back(grad_block=grad_block, grad_one=grad_one, b=b):
                return (
                    grad_block.astype(jnp.float32)
                    + jnp.dot(
                        grad_one.reshape(cells, inner_width),
                        reduce_all[b].T,
                        preferred_element_type=jnp.float32,
                    ).reshape(outer_shape)
                ).astype(jnp.bfloat16)

            upstream = lax.cond(
                b > position, pass_back, lambda: jnp.zeros(outer_shape, jnp.bfloat16)
            )

    pieces = lax.switch(
        position,
        [
            functools.partial(
                lambda k: weight_pair(block_ops[k], cells, height, breadth, chan_index), k
            )
            for k in range(chain)
        ],
    )
    theirs, mine = pieces[:3], pieces[3:]
    pair_sums = []
    for own_piece, other_piece in zip(mine, theirs):
        arrived = lax.ppermute(other_piece, "chan", [(0, 1), (1, 0)])
        pair_sums.append(
            (own_piece.astype(jnp.float32) + arrived.astype(jnp.float32)).astype(jnp.bfloat16)
        )
    totals = lax.psum(tuple(pair_sums), "tiles")
    half_inner = inner_width // 2
    grad_reduce = totals[0]
    grad_spatial = totals[1][:, : 9 * inner_width].reshape(1, 3, 3, inner_width, half_inner)
    grad_expand = totals[2]
    small = totals[1][:, 9 * inner_width : 9 * inner_width + 4].astype(jnp.float32)
    return (grad_reduce, grad_spatial, grad_expand, small[:, 0:2], small[:, 2:4])


def solution(mesh):
    placed = (
        P("groups", ("tiles", "chan"), None, None),
        P("groups", ("tiles", "chan"), None),
        P("groups", ("tiles", "chan")),
        P(),
        P("sections", "chan", None),
        P("sections", None, None, None, "chan"),
        P("sections", None, "chan"),
        P("sections", None, None),
        P("sections", None, None),
    )
    return jax.shard_map(
        local,
        mesh=mesh,
        in_specs=placed,
        out_specs=(
            P(("groups", "sections"), "chan", None),
            P(("groups", "sections"), None, None, None, "chan"),
            P(("groups", "sections"), None, "chan"),
            P(("groups", "sections"), None, "chan"),
            P(("groups", "sections"), None, "chan"),
        ),
        check_vma=False,
    )
```

```python
import functools

import jax
import jax.numpy as jnp
from jax import lax
from jax.sharding import PartitionSpec as P

ROW_AXES = ("tiles", "chan")


def halo_rows(block):
    count = lax.axis_size(ROW_AXES)
    forward = [(i, i + 1) for i in range(count - 1)]
    backward = [(target, source) for source, target in forward]
    low = lax.ppermute(block[:, -1:], ROW_AXES, forward)
    high = lax.ppermute(block[:, :1], ROW_AXES, backward)
    return jnp.concatenate([low, block, high], axis=1)


def grid_taps(extended, height, breadth, mirrored):
    padded = jnp.pad(extended, ((0, 0), (0, 0), (1, 1), (0, 0)))
    tap_list = []
    for shift_row in range(3):
        for shift_col in range(3):
            if mirrored:
                start_row = 2 - shift_row
                start_col = 2 - shift_col
            else:
                start_row = shift_row
                start_col = shift_col
            tap_list.append(
                padded[:, start_row : start_row + height, start_col : start_col + breadth]
            )
    stacked = jnp.concatenate(tap_list, axis=3)
    return stacked.reshape(extended.shape[0] * height * breadth, stacked.shape[3])


def gather_blocks(half, chan_axis, chain, position, chan_index):
    received = [
        lax.ppermute(half, "sections", [(i, (i + k) % chain) for i in range(chain)])
        for k in range(1, chain)
    ]
    stacked = jnp.stack([half] + received)
    if chan_axis is not None:
        other = lax.ppermute(stacked, "chan", [(0, 1), (1, 0)])
        stacked = jnp.where(
            chan_index == 0,
            jnp.concatenate([stacked, other], axis=chan_axis + 1),
            jnp.concatenate([other, stacked], axis=chan_axis + 1),
        )
    blocks = []
    for b in range(chain):
        slot = (position - b + chain) % chain
        chosen = stacked[chain - 1]
        for k in reversed(range(chain - 1)):
            chosen = jnp.where(slot == k, stacked[k], chosen)
        blocks.append(chosen)
    return blocks


def weight_halves(ops, taps, small, cells, half_index):
    cur, h1e, h2, reduced, spatial_out, grad_block, masked_two, grad_two, masked_one, grad_one = ops
    full = cur.shape[-1]
    inner = h2.shape[-1]
    half_full = full // 2
    half_inner = inner // 2
    cur_half = lax.dynamic_slice_in_dim(cur.reshape(cells, full), half_index * half_full, half_full, 1)
    block_half = lax.dynamic_slice_in_dim(
        grad_block.reshape(cells, full), half_index * half_full, half_full, 1
    )
    two_half = lax.dynamic_slice_in_dim(
        grad_two.reshape(cells, inner), half_index * half_inner, half_inner, 1
    )
    reduce_term = jnp.dot(cur_half.T, grad_one.reshape(cells, inner), preferred_element_type=jnp.float32)
    spatial_term = jnp.dot(taps.T, two_half, preferred_element_type=jnp.float32)
    expand_term = jnp.dot(h2.reshape(cells, inner).T, block_half, preferred_element_type=jnp.float32)
    small_half = lax.dynamic_slice_in_dim(small, half_index * half_inner, half_inner, 1)
    small_rows = jnp.pad(small_half, ((0, 8 - small_half.shape[0]), (0, 0)))
    spatial_small = jnp.concatenate([spatial_term, small_rows], axis=0)
    return tuple(
        piece.astype(jnp.bfloat16)[None] for piece in (reduce_term, spatial_small, expand_term)
    )


def weight_pair(ops, cells, height, breadth, chan_index):
    cur, h1e, h2, reduced, spatial_out, grad_block, masked_two, grad_two, masked_one, grad_one = ops
    taps = grid_taps(h1e, height, breadth, False)
    small = jnp.stack(
        [
            jnp.sum(masked_one * reduced, axis=(0, 1, 2)),
            jnp.sum(masked_two * spatial_out, axis=(0, 1, 2)),
            jnp.sum(masked_one, axis=(0, 1, 2)),
            jnp.sum(masked_two, axis=(0, 1, 2)),
        ]
    )
    theirs = weight_halves(ops, taps, small, cells, 1 - chan_index)
    mine = weight_halves(ops, taps, small, cells, chan_index)
    return theirs + mine


def local(
    features,
    tissue,
    row_label,
    prototypes,
    reduce_weight,
    spatial_weight,
    expand_weight,
    norm_gain,
    norm_bias,
):
    regions, height, breadth, full_width = features.shape
    chain = lax.axis_size("sections")
    position = lax.axis_index("sections")
    chan_index = lax.axis_index("chan")
    reduce_all = gather_blocks(reduce_weight[0], 0, chain, position, chan_index)
    spatial_all = gather_blocks(spatial_weight[0], 3, chain, position, chan_index)
    expand_all = gather_blocks(expand_weight[0], 1, chain, position, chan_index)
    gain_all = gather_blocks(norm_gain[0], None, chain, position, chan_index)
    bias_all = gather_blocks(norm_bias[0], None, chain, position, chan_index)
    inner_width = reduce_all[0].shape[1]
    tissue_mask = tissue.astype(jnp.float32)[:, :, :, None]
    cells = regions * height * breadth
    inner_shape = (regions, height, breadth, inner_width)
    outer_shape = (regions, height, breadth, full_width)

    current = features
    saved = []
    for b in range(chain):
        gain_pair, bias_pair = gain_all[b], bias_all[b]
        reduced = jnp.dot(
            current.reshape(cells, full_width), reduce_all[b], preferred_element_type=jnp.float32
        ).reshape(inner_shape)
        pre_reduce = gain_pair[0] * reduced + bias_pair[0]
        hidden_one = jnp.maximum(pre_reduce, 0.0).astype(jnp.bfloat16)
        hidden_ext = halo_rows(hidden_one)
        spatial_out = jnp.dot(
            grid_taps(hidden_ext, height, breadth, False),
            spatial_all[b].reshape(9 * inner_width, inner_width),
            preferred_element_type=jnp.float32,
        ).reshape(inner_shape)
        pre_spatial = gain_pair[1] * spatial_out + bias_pair[1]
        hidden_two = jnp.maximum(pre_spatial, 0.0).astype(jnp.bfloat16)
        expanded = jnp.dot(
            hidden_two.reshape(cells, inner_width), expand_all[b], preferred_element_type=jnp.float32
        ).reshape(outer_shape)
        block_out = (
            tissue_mask * jnp.maximum(current.astype(jnp.float32) + expanded, 0.0)
        ).astype(jnp.bfloat16)
        saved.append((current, hidden_ext, reduced, pre_reduce, spatial_out, pre_spatial, hidden_two, block_out))
        current = block_out

    classes = prototypes.shape[0]
    chosen = (row_label[:, :, None] == jnp.arange(classes, dtype=jnp.int32)).astype(jnp.float32)
    target_rows = jnp.einsum("mrk,kc->mrc", chosen, prototypes.astype(jnp.float32))
    total_cells = regions * height * lax.axis_size("tiles") * lax.axis_size("chan") * breadth
    upstream = (
        tissue_mask * (current.astype(jnp.float32) - target_rows[:, :, None, :]) / total_cells
    ).astype(jnp.bfloat16)

    block_ops = [None] * chain
    for b in reversed(range(chain)):
        block_in, hidden_ext, reduced, pre_reduce, spatial_out, pre_spatial, hidden_two, block_out = saved[b]
        needed = b >= position
        gain_pair = gain_all[b]

        def first_back(upstream=upstream, block_out=block_out, pre_spatial=pre_spatial, b=b, gain_pair=gain_pair):
            grad_block = jnp.where(block_out > 0, upstream, jnp.zeros_like(upstream))
            back_two = jnp.dot(
                grad_block.reshape(cells, full_width), expand_all[b].T, preferred_element_type=jnp.float32
            ).reshape(inner_shape)
            masked_two = jnp.where(pre_spatial > 0, back_two, jnp.float32(0.0))
            grad_two = (masked_two * gain_pair[1]).astype(jnp.bfloat16)
            return grad_block, masked_two, grad_two

        def first_skip():
            return (
                jnp.zeros(outer_shape, jnp.bfloat16),
                jnp.zeros(inner_shape, jnp.float32),
                jnp.zeros(inner_shape, jnp.bfloat16),
            )

        grad_block, masked_two, grad_two = lax.cond(needed, first_back, first_skip)
        grad_ext = halo_rows(grad_two)

        def second_back(grad_ext=grad_ext, pre_reduce=pre_reduce, b=b, gain_pair=gain_pair):
            back_one = jnp.einsum(
                "cxyo,xyio->ci",
                grid_taps(grad_ext, height, breadth, True).reshape(cells, 3, 3, inner_width),
                spatial_all[b],
                preferred_element_type=jnp.float32,
            ).reshape(inner_shape)
            masked_one = jnp.where(pre_reduce > 0, back_one, jnp.float32(0.0))
            grad_one = (masked_one * gain_pair[0]).astype(jnp.bfloat16)
            return masked_one, grad_one

        def second_skip():
            return (jnp.zeros(inner_shape, jnp.float32), jnp.zeros(inner_shape, jnp.bfloat16))

        masked_one, grad_one = lax.cond(needed, second_back, second_skip)
        block_ops[b] = (
            block_in, hidden_ext, hidden_two, reduced, spatial_out,
            grad_block, masked_two, grad_two, masked_one, grad_one,
        )
        if b > 0:

            def pass_back(grad_block=grad_block, grad_one=grad_one, b=b):
                return (
                    grad_block.astype(jnp.float32)
                    + jnp.dot(
                        grad_one.reshape(cells, inner_width),
                        reduce_all[b].T,
                        preferred_element_type=jnp.float32,
                    ).reshape(outer_shape)
                ).astype(jnp.bfloat16)

            upstream = lax.cond(
                b > position, pass_back, lambda: jnp.zeros(outer_shape, jnp.bfloat16)
            )

    pieces = lax.switch(
        position,
        [
            functools.partial(
                lambda k: weight_pair(block_ops[k], cells, height, breadth, chan_index), k
            )
            for k in range(chain)
        ],
    )
    theirs, mine = pieces[:3], pieces[3:]
    pair_sums = []
    for own_piece, other_piece in zip(mine, theirs):
        arrived = lax.ppermute(other_piece, "chan", [(0, 1), (1, 0)])
        pair_sums.append(
            (own_piece.astype(jnp.float32) + arrived.astype(jnp.float32)).astype(jnp.bfloat16)
        )
    totals = lax.psum(tuple(pair_sums), "tiles")
    half_inner = inner_width // 2
    grad_reduce = totals[0]
    grad_spatial = totals[1][:, : 9 * inner_width].reshape(1, 3, 3, inner_width, half_inner)
    grad_expand = totals[2]
    small = totals[1][:, 9 * inner_width : 9 * inner_width + 4].astype(jnp.float32)
    return (grad_reduce, grad_spatial, grad_expand, small[:, 0:2], small[:, 2:4])


def solution(mesh):
    placed = (
        P("groups", ("tiles", "chan"), None, None),
        P("groups", ("tiles", "chan"), None),
        P("groups", ("tiles", "chan")),
        P(),
        P("sections", "chan", None),
        P("sections", None, None, None, "chan"),
        P("sections", None, "chan"),
        P("sections", None, None),
        P("sections", None, None),
    )
    return jax.shard_map(
        local,
        mesh=mesh,
        in_specs=placed,
        out_specs=(
            P(("groups", "sections"), "chan", None),
            P(("groups", "sections"), None, None, None, "chan"),
            P(("groups", "sections"), None, "chan"),
            P(("groups", "sections"), None, "chan"),
            P(("groups", "sections"), None, "chan"),
        ),
        check_vma=False,
    )
```

```python
import functools

import jax
import jax.numpy as jnp
from jax import lax
from jax.sharding import PartitionSpec as P

ROW_AXES = ("tiles", "chan")


def halo_rows(block):
    count = lax.axis_size(ROW_AXES)
    forward = [(i, i + 1) for i in range(count - 1)]
    backward = [(target, source) for source, target in forward]
    low = lax.ppermute(block[:, -1:], ROW_AXES, forward)
    high = lax.ppermute(block[:, :1], ROW_AXES, backward)
    return jnp.concatenate([low, block, high], axis=1)


def grid_taps(extended, height, breadth, mirrored):
    padded = jnp.pad(extended, ((0, 0), (0, 0), (1, 1), (0, 0)))
    tap_list = []
    for shift_row in range(3):
        for shift_col in range(3):
            if mirrored:
                start_row = 2 - shift_row
                start_col = 2 - shift_col
            else:
                start_row = shift_row
                start_col = shift_col
            tap_list.append(
                padded[:, start_row : start_row + height, start_col : start_col + breadth]
            )
    stacked = jnp.concatenate(tap_list, axis=3)
    return stacked.reshape(extended.shape[0] * height * breadth, stacked.shape[3])


def gather_blocks(half, chan_axis, chain, position, chan_index):
    received = [
        lax.ppermute(half, "sections", [(i, (i + k) % chain) for i in range(chain)])
        for k in range(1, chain)
    ]
    stacked = jnp.stack([half] + received)
    if chan_axis is not None:
        other = lax.ppermute(stacked, "chan", [(0, 1), (1, 0)])
        stacked = jnp.where(
            chan_index == 0,
            jnp.concatenate([stacked, other], axis=chan_axis + 1),
            jnp.concatenate([other, stacked], axis=chan_axis + 1),
        )
    blocks = []
    for b in range(chain):
        slot = (position - b + chain) % chain
        chosen = stacked[chain - 1]
        for k in reversed(range(chain - 1)):
            chosen = jnp.where(slot == k, stacked[k], chosen)
        blocks.append(chosen)
    return blocks


def weight_halves(ops, taps, small, cells, half_index):
    cur, h1e, h2, reduced, spatial_out, grad_block, masked_two, grad_two, masked_one, grad_one = ops
    full = cur.shape[-1]
    inner = h2.shape[-1]
    half_full = full // 2
    half_inner = inner // 2
    cur_half = lax.dynamic_slice_in_dim(cur.reshape(cells, full), half_index * half_full, half_full, 1)
    block_half = lax.dynamic_slice_in_dim(
        grad_block.reshape(cells, full), half_index * half_full, half_full, 1
    )
    two_half = lax.dynamic_slice_in_dim(
        grad_two.reshape(cells, inner), half_index * half_inner, half_inner, 1
    )
    reduce_term = jnp.dot(cur_half.T, grad_one.reshape(cells, inner), preferred_element_type=jnp.float32)
    spatial_term = jnp.dot(taps.T, two_half, preferred_element_type=jnp.float32)
    expand_term = jnp.dot(h2.reshape(cells, inner).T, block_half, preferred_element_type=jnp.float32)
    small_half = lax.dynamic_slice_in_dim(small, half_index * half_inner, half_inner, 1)
    small_rows = jnp.pad(small_half, ((0, 8 - small_half.shape[0]), (0, 0)))
    spatial_small = jnp.concatenate([spatial_term, small_rows], axis=0)
    return tuple(
        piece.astype(jnp.bfloat16)[None] for piece in (reduce_term, spatial_small, expand_term)
    )


def weight_pair(ops, cells, height, breadth, chan_index):
    cur, h1e, h2, reduced, spatial_out, grad_block, masked_two, grad_two, masked_one, grad_one = ops
    taps = grid_taps(h1e, height, breadth, False)
    small = jnp.stack(
        [
            jnp.sum(masked_one * reduced, axis=(0, 1, 2)),
            jnp.sum(masked_two * spatial_out, axis=(0, 1, 2)),
            jnp.sum(masked_one, axis=(0, 1, 2)),
            jnp.sum(masked_two, axis=(0, 1, 2)),
        ]
    )
    theirs = weight_halves(ops, taps, small, cells, 1 - chan_index)
    mine = weight_halves(ops, taps, small, cells, chan_index)
    return theirs + mine


def local(
    features,
    tissue,
    row_label,
    prototypes,
    reduce_weight,
    spatial_weight,
    expand_weight,
    norm_gain,
    norm_bias,
):
    regions, height, breadth, full_width = features.shape
    chain = lax.axis_size("sections")
    position = lax.axis_index("sections")
    chan_index = lax.axis_index("chan")
    reduce_all = gather_blocks(reduce_weight[0], 0, chain, position, chan_index)
    spatial_all = gather_blocks(spatial_weight[0], 3, chain, position, chan_index)
    expand_all = gather_blocks(expand_weight[0], 1, chain, position, chan_index)
    gain_all = gather_blocks(norm_gain[0], None, chain, position, chan_index)
    bias_all = gather_blocks(norm_bias[0], None, chain, position, chan_index)
    inner_width = reduce_all[0].shape[1]
    tissue_mask = tissue.astype(jnp.float32)[:, :, :, None]
    cells = regions * height * breadth
    inner_shape = (regions, height, breadth, inner_width)
    outer_shape = (regions, height, breadth, full_width)

    current = features
    saved = []
    for b in range(chain):
        gain_pair, bias_pair = gain_all[b], bias_all[b]
        reduced = jnp.dot(
            current.reshape(cells, full_width), reduce_all[b], preferred_element_type=jnp.float32
        ).reshape(inner_shape)
        pre_reduce = gain_pair[0] * reduced + bias_pair[0]
        hidden_one = jnp.maximum(pre_reduce, 0.0).astype(jnp.bfloat16)
        hidden_ext = halo_rows(hidden_one)
        spatial_out = jnp.dot(
            grid_taps(hidden_ext, height, breadth, False),
            spatial_all[b].reshape(9 * inner_width, inner_width),
            preferred_element_type=jnp.float32,
        ).reshape(inner_shape)
        pre_spatial = gain_pair[1] * spatial_out + bias_pair[1]
        hidden_two = jnp.maximum(pre_spatial, 0.0).astype(jnp.bfloat16)
        expanded = jnp.dot(
            hidden_two.reshape(cells, inner_width), expand_all[b], preferred_element_type=jnp.float32
        ).reshape(outer_shape)
        block_out = (
            tissue_mask * jnp.maximum(current.astype(jnp.float32) + expanded, 0.0)
        ).astype(jnp.bfloat16)
        saved.append((current, hidden_ext, reduced, pre_reduce, spatial_out, pre_spatial, hidden_two, block_out))
        current = block_out

    classes = prototypes.shape[0]
    chosen = (row_label[:, :, None] == jnp.arange(classes, dtype=jnp.int32)).astype(jnp.float32)
    target_rows = jnp.einsum("mrk,kc->mrc", chosen, prototypes.astype(jnp.float32))
    total_cells = regions * height * lax.axis_size("tiles") * lax.axis_size("chan") * breadth
    upstream = (
        tissue_mask * (current.astype(jnp.float32) - target_rows[:, :, None, :]) / total_cells
    ).astype(jnp.bfloat16)

    block_ops = [None] * chain
    for b in reversed(range(chain)):
        block_in, hidden_ext, reduced, pre_reduce, spatial_out, pre_spatial, hidden_two, block_out = saved[b]
        needed = b >= position
        gain_pair = gain_all[b]

        def first_back(upstream=upstream, block_out=block_out, pre_spatial=pre_spatial, b=b, gain_pair=gain_pair):
            grad_block = jnp.where(block_out > 0, upstream, jnp.zeros_like(upstream))
            back_two = jnp.dot(
                grad_block.reshape(cells, full_width), expand_all[b].T, preferred_element_type=jnp.float32
            ).reshape(inner_shape)
            masked_two = jnp.where(pre_spatial > 0, back_two, jnp.float32(0.0))
            grad_two = (masked_two * gain_pair[1]).astype(jnp.bfloat16)
            return grad_block, masked_two, grad_two

        def first_skip():
            return (
                jnp.zeros(outer_shape, jnp.bfloat16),
                jnp.zeros(inner_shape, jnp.float32),
                jnp.zeros(inner_shape, jnp.bfloat16),
            )

        grad_block, masked_two, grad_two = lax.cond(needed, first_back, first_skip)
        grad_ext = halo_rows(grad_two)

        def second_back(grad_ext=grad_ext, pre_reduce=pre_reduce, b=b, gain_pair=gain_pair):
            back_one = jnp.dot(
                grid_taps(grad_ext, height, breadth, True),
                jnp.transpose(spatial_all[b], (0, 1, 3, 2)).reshape(9 * inner_width, inner_width),
                preferred_element_type=jnp.float32,
            ).reshape(inner_shape)
            masked_one = jnp.where(pre_reduce > 0, back_one, jnp.float32(0.0))
            grad_one = (masked_one * gain_pair[0]).astype(jnp.bfloat16)
            return masked_one, grad_one

        def second_skip():
            return (jnp.zeros(inner_shape, jnp.float32), jnp.zeros(inner_shape, jnp.bfloat16))

        masked_one, grad_one = lax.cond(needed, second_back, second_skip)
        block_ops[b] = (
            block_in, hidden_ext, hidden_two, reduced, spatial_out,
            grad_block, masked_two, grad_two, masked_one, grad_one,
        )
        if b > 0:

            def pass_back(grad_block=grad_block, grad_one=grad_one, b=b):
                return (
                    grad_block.astype(jnp.float32)
                    + jnp.dot(
                        grad_one.reshape(cells, inner_width),
                        reduce_all[b].T,
                        preferred_element_type=jnp.float32,
                    ).reshape(outer_shape)
                ).astype(jnp.bfloat16)

            upstream = lax.cond(
                b > position, pass_back, lambda: jnp.zeros(outer_shape, jnp.bfloat16)
            )

    pieces = lax.switch(
        position,
        [
            functools.partial(
                lambda k: weight_pair(block_ops[k], cells, height, breadth, chan_index), k
            )
            for k in range(chain)
        ],
    )
    theirs, mine = pieces[:3], pieces[3:]
    pair_sums = []
    for own_piece, other_piece in zip(mine, theirs):
        arrived = lax.ppermute(other_piece, "chan", [(0, 1), (1, 0)])
        pair_sums.append(
            (own_piece.astype(jnp.float32) + arrived.astype(jnp.float32)).astype(jnp.bfloat16)
        )
    totals = lax.psum(tuple(pair_sums), "tiles")
    half_inner = inner_width // 2
    grad_reduce = totals[0]
    grad_spatial = totals[1][:, : 9 * inner_width].reshape(1, 3, 3, inner_width, half_inner)
    grad_expand = totals[2]
    small = totals[1][:, 9 * inner_width : 9 * inner_width + 4].astype(jnp.float32)
    return (grad_reduce, grad_spatial, grad_expand, small[:, 0:2], small[:, 2:4])


def solution(mesh):
    placed = (
        P("groups", ("tiles", "chan"), None, None),
        P("groups", ("tiles", "chan"), None),
        P("groups", ("tiles", "chan")),
        P(),
        P("sections", "chan", None),
        P("sections", None, None, None, "chan"),
        P("sections", None, "chan"),
        P("sections", None, None),
        P("sections", None, None),
    )
    return jax.shard_map(
        local,
        mesh=mesh,
        in_specs=placed,
        out_specs=(
            P(("groups", "sections"), "chan", None),
            P(("groups", "sections"), None, None, None, "chan"),
            P(("groups", "sections"), None, "chan"),
            P(("groups", "sections"), None, "chan"),
            P(("groups", "sections"), None, "chan"),
        ),
        check_vma=False,
    )
```

```python
import functools

import jax
import jax.numpy as jnp
from jax import lax
from jax.sharding import PartitionSpec as P

ROW_AXES = ("tiles", "chan")


def halo_rows(block):
    count = lax.axis_size(ROW_AXES)
    forward = [(i, i + 1) for i in range(count - 1)]
    backward = [(target, source) for source, target in forward]
    low = lax.ppermute(block[:, -1:], ROW_AXES, forward)
    high = lax.ppermute(block[:, :1], ROW_AXES, backward)
    return jnp.concatenate([low, block, high], axis=1)


def grid_taps(extended, height, breadth, mirrored):
    padded = jnp.pad(extended, ((0, 0), (0, 0), (1, 1), (0, 0)))
    tap_list = []
    for shift_row in range(3):
        for shift_col in range(3):
            if mirrored:
                start_row = 2 - shift_row
                start_col = 2 - shift_col
            else:
                start_row = shift_row
                start_col = shift_col
            tap_list.append(
                padded[:, start_row : start_row + height, start_col : start_col + breadth]
            )
    stacked = jnp.concatenate(tap_list, axis=3)
    return stacked.reshape(extended.shape[0] * height * breadth, stacked.shape[3])


def gather_blocks(half, chan_axis, chain, position, chan_index):
    received = [
        lax.ppermute(half, "sections", [(i, (i + k) % chain) for i in range(chain)])
        for k in range(1, chain)
    ]
    stacked = jnp.stack([half] + received)
    if chan_axis is not None:
        other = lax.ppermute(stacked, "chan", [(0, 1), (1, 0)])
        stacked = jnp.where(
            chan_index == 0,
            jnp.concatenate([stacked, other], axis=chan_axis + 1),
            jnp.concatenate([other, stacked], axis=chan_axis + 1),
        )
    return [
        lax.dynamic_index_in_dim(stacked, (position - b + chain) % chain, 0, keepdims=False)
        for b in range(chain)
    ]


def weight_halves(ops, taps, small, cells, half_index):
    cur, h1e, h2, reduced, spatial_out, grad_block, masked_two, grad_two, masked_one, grad_one = ops
    full = cur.shape[-1]
    inner = h2.shape[-1]
    half_full = full // 2
    half_inner = inner // 2
    cur_half = lax.dynamic_slice_in_dim(cur.reshape(cells, full), half_index * half_full, half_full, 1)
    block_half = lax.dynamic_slice_in_dim(
        grad_block.reshape(cells, full), half_index * half_full, half_full, 1
    )
    two_half = lax.dynamic_slice_in_dim(
        grad_two.reshape(cells, inner), half_index * half_inner, half_inner, 1
    )
    reduce_term = jnp.dot(cur_half.T, grad_one.reshape(cells, inner), preferred_element_type=jnp.float32)
    spatial_term = jnp.dot(taps.T, two_half, preferred_element_type=jnp.float32)
    expand_term = jnp.dot(h2.reshape(cells, inner).T, block_half, preferred_element_type=jnp.float32)
    small_half = lax.dynamic_slice_in_dim(small, half_index * half_inner, half_inner, 1)
    small_rows = jnp.pad(small_half, ((0, 8 - small_half.shape[0]), (0, 0)))
    spatial_small = jnp.concatenate([spatial_term, small_rows], axis=0)
    return tuple(
        piece.astype(jnp.bfloat16)[None] for piece in (reduce_term, spatial_small, expand_term)
    )


def weight_pair(ops, cells, height, breadth, chan_index):
    cur, h1e, h2, reduced, spatial_out, grad_block, masked_two, grad_two, masked_one, grad_one = ops
    taps = grid_taps(h1e, height, breadth, False)
    small = jnp.stack(
        [
            jnp.sum(masked_one * reduced, axis=(0, 1, 2)),
            jnp.sum(masked_two * spatial_out, axis=(0, 1, 2)),
            jnp.sum(masked_one, axis=(0, 1, 2)),
            jnp.sum(masked_two, axis=(0, 1, 2)),
        ]
    )
    theirs = weight_halves(ops, taps, small, cells, 1 - chan_index)
    mine = weight_halves(ops, taps, small, cells, chan_index)
    return theirs + mine


def halving_all_reduce(value, axis):
    count = lax.axis_size(axis)
    assert count & (count - 1) == 0
    place = lax.axis_index(axis)
    steps = count.bit_length() - 1
    current = value
    for step in range(steps):
        bit = 1 << step
        upper = (place // bit) % 2
        half = current.shape[0] // 2
        keep = lax.dynamic_slice_in_dim(current, upper * half, half, 0)
        send = lax.dynamic_slice_in_dim(current, (1 - upper) * half, half, 0)
        got = lax.ppermute(send, axis, [(i, i ^ bit) for i in range(count)])
        current = (keep.astype(jnp.float32) + got.astype(jnp.float32)).astype(value.dtype)
    for step in reversed(range(steps)):
        bit = 1 << step
        upper = (place // bit) % 2
        got = lax.ppermute(current, axis, [(i, i ^ bit) for i in range(count)])
        current = jnp.where(
            upper == 0,
            jnp.concatenate([current, got], axis=0),
            jnp.concatenate([got, current], axis=0),
        )
    return current


def local(
    features,
    tissue,
    row_label,
    prototypes,
    reduce_weight,
    spatial_weight,
    expand_weight,
    norm_gain,
    norm_bias,
):
    regions, height, breadth, full_width = features.shape
    chain = lax.axis_size("sections")
    position = lax.axis_index("sections")
    chan_index = lax.axis_index("chan")
    reduce_all = gather_blocks(reduce_weight[0], 0, chain, position, chan_index)
    spatial_all = gather_blocks(spatial_weight[0], 3, chain, position, chan_index)
    expand_all = gather_blocks(expand_weight[0], 1, chain, position, chan_index)
    gain_all = gather_blocks(norm_gain[0], None, chain, position, chan_index)
    bias_all = gather_blocks(norm_bias[0], None, chain, position, chan_index)
    inner_width = reduce_all[0].shape[1]
    tissue_mask = tissue.astype(jnp.float32)[:, :, :, None]
    cells = regions * height * breadth
    inner_shape = (regions, height, breadth, inner_width)
    outer_shape = (regions, height, breadth, full_width)

    current = features
    saved = []
    for b in range(chain):
        gain_pair, bias_pair = gain_all[b], bias_all[b]
        reduced = jnp.dot(
            current.reshape(cells, full_width), reduce_all[b], preferred_element_type=jnp.float32
        ).reshape(inner_shape)
        pre_reduce = gain_pair[0] * reduced + bias_pair[0]
        hidden_one = jnp.maximum(pre_reduce, 0.0).astype(jnp.bfloat16)
        hidden_ext = halo_rows(hidden_one)
        spatial_out = jnp.dot(
            grid_taps(hidden_ext, height, breadth, False),
            spatial_all[b].reshape(9 * inner_width, inner_width),
            preferred_element_type=jnp.float32,
        ).reshape(inner_shape)
        pre_spatial = gain_pair[1] * spatial_out + bias_pair[1]
        hidden_two = jnp.maximum(pre_spatial, 0.0).astype(jnp.bfloat16)
        expanded = jnp.dot(
            hidden_two.reshape(cells, inner_width), expand_all[b], preferred_element_type=jnp.float32
        ).reshape(outer_shape)
        block_out = (
            tissue_mask * jnp.maximum(current.astype(jnp.float32) + expanded, 0.0)
        ).astype(jnp.bfloat16)
        saved.append((current, hidden_ext, reduced, pre_reduce, spatial_out, pre_spatial, hidden_two, block_out))
        current = block_out

    classes = prototypes.shape[0]
    chosen = (row_label[:, :, None] == jnp.arange(classes, dtype=jnp.int32)).astype(jnp.float32)
    target_rows = jnp.einsum("mrk,kc->mrc", chosen, prototypes.astype(jnp.float32))
    total_cells = regions * height * lax.axis_size("tiles") * lax.axis_size("chan") * breadth
    upstream = (
        tissue_mask * (current.astype(jnp.float32) - target_rows[:, :, None, :]) / total_cells
    ).astype(jnp.bfloat16)

    block_ops = [None] * chain
    for b in reversed(range(chain)):
        block_in, hidden_ext, reduced, pre_reduce, spatial_out, pre_spatial, hidden_two, block_out = saved[b]
        needed = b >= position
        gain_pair = gain_all[b]

        def first_back(upstream=upstream, block_out=block_out, pre_spatial=pre_spatial, b=b, gain_pair=gain_pair):
            grad_block = jnp.where(block_out > 0, upstream, jnp.zeros_like(upstream))
            back_two = jnp.dot(
                grad_block.reshape(cells, full_width), expand_all[b].T, preferred_element_type=jnp.float32
            ).reshape(inner_shape)
            masked_two = jnp.where(pre_spatial > 0, back_two, jnp.float32(0.0))
            grad_two = (masked_two * gain_pair[1]).astype(jnp.bfloat16)
            return grad_block, masked_two, grad_two

        def first_skip():
            return (
                jnp.zeros(outer_shape, jnp.bfloat16),
                jnp.zeros(inner_shape, jnp.float32),
                jnp.zeros(inner_shape, jnp.bfloat16),
            )

        grad_block, masked_two, grad_two = lax.cond(needed, first_back, first_skip)
        grad_ext = halo_rows(grad_two)

        def second_back(grad_ext=grad_ext, pre_reduce=pre_reduce, b=b, gain_pair=gain_pair):
            back_one = jnp.dot(
                grid_taps(grad_ext, height, breadth, True),
                jnp.transpose(spatial_all[b], (0, 1, 3, 2)).reshape(9 * inner_width, inner_width),
                preferred_element_type=jnp.float32,
            ).reshape(inner_shape)
            masked_one = jnp.where(pre_reduce > 0, back_one, jnp.float32(0.0))
            grad_one = (masked_one * gain_pair[0]).astype(jnp.bfloat16)
            return masked_one, grad_one

        def second_skip():
            return (jnp.zeros(inner_shape, jnp.float32), jnp.zeros(inner_shape, jnp.bfloat16))

        masked_one, grad_one = lax.cond(needed, second_back, second_skip)
        block_ops[b] = (
            block_in, hidden_ext, hidden_two, reduced, spatial_out,
            grad_block, masked_two, grad_two, masked_one, grad_one,
        )
        if b > 0:

            def pass_back(grad_block=grad_block, grad_one=grad_one, b=b):
                return (
                    grad_block.astype(jnp.float32)
                    + jnp.dot(
                        grad_one.reshape(cells, inner_width),
                        reduce_all[b].T,
                        preferred_element_type=jnp.float32,
                    ).reshape(outer_shape)
                ).astype(jnp.bfloat16)

            upstream = lax.cond(
                b > position, pass_back, lambda: jnp.zeros(outer_shape, jnp.bfloat16)
            )

    pieces = lax.switch(
        position,
        [
            functools.partial(
                lambda k: weight_pair(block_ops[k], cells, height, breadth, chan_index), k
            )
            for k in range(chain)
        ],
    )
    theirs, mine = pieces[:3], pieces[3:]
    pair_sums = []
    for own_piece, other_piece in zip(mine, theirs):
        arrived = lax.ppermute(other_piece, "chan", [(0, 1), (1, 0)])
        pair_sums.append(
            (own_piece.astype(jnp.float32) + arrived.astype(jnp.float32)).astype(jnp.bfloat16)
        )
    totals = (
        halving_all_reduce(pair_sums[0][0], "tiles")[None],
        lax.psum(pair_sums[1], "tiles"),
        halving_all_reduce(pair_sums[2][0], "tiles")[None],
    )
    half_inner = inner_width // 2
    grad_reduce = totals[0]
    grad_spatial = totals[1][:, : 9 * inner_width].reshape(1, 3, 3, inner_width, half_inner)
    grad_expand = totals[2]
    small = totals[1][:, 9 * inner_width : 9 * inner_width + 4].astype(jnp.float32)
    return (grad_reduce, grad_spatial, grad_expand, small[:, 0:2], small[:, 2:4])


def solution(mesh):
    placed = (
        P("groups", ("tiles", "chan"), None, None),
        P("groups", ("tiles", "chan"), None),
        P("groups", ("tiles", "chan")),
        P(),
        P("sections", "chan", None),
        P("sections", None, None, None, "chan"),
        P("sections", None, "chan"),
        P("sections", None, None),
        P("sections", None, None),
    )
    return jax.shard_map(
        local,
        mesh=mesh,
        in_specs=placed,
        out_specs=(
            P(("groups", "sections"), "chan", None),
            P(("groups", "sections"), None, None, None, "chan"),
            P(("groups", "sections"), None, "chan"),
            P(("groups", "sections"), None, "chan"),
            P(("groups", "sections"), None, "chan"),
        ),
        check_vma=False,
    )
```

```python
import functools

import jax
import jax.numpy as jnp
from jax import lax
from jax.sharding import PartitionSpec as P

ROW_AXES = ("tiles", "chan")


def halo_rows(block):
    count = lax.axis_size(ROW_AXES)
    forward = [(i, i + 1) for i in range(count - 1)]
    backward = [(target, source) for source, target in forward]
    low = lax.ppermute(block[:, -1:], ROW_AXES, forward)
    high = lax.ppermute(block[:, :1], ROW_AXES, backward)
    return jnp.concatenate([low, block, high], axis=1)


def grid_taps(extended, height, breadth, mirrored):
    padded = jnp.pad(extended, ((0, 0), (0, 0), (1, 1), (0, 0)))
    tap_list = []
    for shift_row in range(3):
        for shift_col in range(3):
            if mirrored:
                start_row = 2 - shift_row
                start_col = 2 - shift_col
            else:
                start_row = shift_row
                start_col = shift_col
            tap_list.append(
                padded[:, start_row : start_row + height, start_col : start_col + breadth]
            )
    stacked = jnp.concatenate(tap_list, axis=3)
    return stacked.reshape(extended.shape[0] * height * breadth, stacked.shape[3])


def gather_blocks(half, chan_axis, chain, position, chan_index):
    received = [
        lax.ppermute(half, "sections", [(i, (i + k) % chain) for i in range(chain)])
        for k in range(1, chain)
    ]
    stacked = jnp.stack([half] + received)
    if chan_axis is not None:
        other = lax.ppermute(stacked, "chan", [(0, 1), (1, 0)])
        stacked = jnp.where(
            chan_index == 0,
            jnp.concatenate([stacked, other], axis=chan_axis + 1),
            jnp.concatenate([other, stacked], axis=chan_axis + 1),
        )
    return [
        lax.dynamic_index_in_dim(stacked, (position - b + chain) % chain, 0, keepdims=False)
        for b in range(chain)
    ]


def weight_halves(ops, taps, small, cells, half_index):
    cur, h1e, h2, reduced, spatial_out, grad_block, masked_two, grad_two, masked_one, grad_one = ops
    full = cur.shape[-1]
    inner = h2.shape[-1]
    half_full = full // 2
    half_inner = inner // 2
    cur_half = lax.dynamic_slice_in_dim(cur.reshape(cells, full), half_index * half_full, half_full, 1)
    block_half = lax.dynamic_slice_in_dim(
        grad_block.reshape(cells, full), half_index * half_full, half_full, 1
    )
    two_half = lax.dynamic_slice_in_dim(
        grad_two.reshape(cells, inner), half_index * half_inner, half_inner, 1
    )
    reduce_term = jnp.dot(cur_half.T, grad_one.reshape(cells, inner), preferred_element_type=jnp.float32)
    spatial_term = jnp.dot(taps.T, two_half, preferred_element_type=jnp.float32)
    expand_term = jnp.dot(h2.reshape(cells, inner).T, block_half, preferred_element_type=jnp.float32)
    small_half = lax.dynamic_slice_in_dim(small, half_index * half_inner, half_inner, 1)
    small_rows = jnp.pad(small_half, ((0, 8 - small_half.shape[0]), (0, 0)))
    spatial_small = jnp.concatenate([spatial_term, small_rows], axis=0)
    return tuple(
        piece.astype(jnp.bfloat16)[None] for piece in (reduce_term, spatial_small, expand_term)
    )


def weight_pair(ops, cells, height, breadth, chan_index):
    cur, h1e, h2, reduced, spatial_out, grad_block, masked_two, grad_two, masked_one, grad_one = ops
    taps = grid_taps(h1e, height, breadth, False)
    small = jnp.stack(
        [
            jnp.sum(masked_one * reduced, axis=(0, 1, 2)),
            jnp.sum(masked_two * spatial_out, axis=(0, 1, 2)),
            jnp.sum(masked_one, axis=(0, 1, 2)),
            jnp.sum(masked_two, axis=(0, 1, 2)),
        ]
    )
    theirs = weight_halves(ops, taps, small, cells, 1 - chan_index)
    mine = weight_halves(ops, taps, small, cells, chan_index)
    return theirs + mine


def halving_all_reduce(value, axis):
    count = lax.axis_size(axis)
    assert count & (count - 1) == 0
    place = lax.axis_index(axis)
    steps = count.bit_length() - 1
    current = value
    for step in range(steps):
        bit = 1 << step
        upper = (place // bit) % 2
        half = current.shape[0] // 2
        keep = lax.dynamic_slice_in_dim(current, upper * half, half, 0)
        send = lax.dynamic_slice_in_dim(current, (1 - upper) * half, half, 0)
        got = lax.ppermute(send, axis, [(i, i ^ bit) for i in range(count)])
        current = (keep.astype(jnp.float32) + got.astype(jnp.float32)).astype(value.dtype)
    for step in reversed(range(steps)):
        bit = 1 << step
        upper = (place // bit) % 2
        got = lax.ppermute(current, axis, [(i, i ^ bit) for i in range(count)])
        current = jnp.where(
            upper == 0,
            jnp.concatenate([current, got], axis=0),
            jnp.concatenate([got, current], axis=0),
        )
    return current


def local(
    features,
    tissue,
    row_label,
    prototypes,
    reduce_weight,
    spatial_weight,
    expand_weight,
    norm_gain,
    norm_bias,
):
    regions, height, breadth, full_width = features.shape
    chain = lax.axis_size("sections")
    position = lax.axis_index("sections")
    chan_index = lax.axis_index("chan")
    reduce_all = gather_blocks(reduce_weight[0], 0, chain, position, chan_index)
    spatial_all = gather_blocks(spatial_weight[0], 3, chain, position, chan_index)
    expand_all = gather_blocks(expand_weight[0], 1, chain, position, chan_index)
    gain_all = gather_blocks(norm_gain[0], None, chain, position, chan_index)
    bias_all = gather_blocks(norm_bias[0], None, chain, position, chan_index)
    inner_width = reduce_all[0].shape[1]
    tissue_mask = tissue.astype(jnp.float32)[:, :, :, None]
    cells = regions * height * breadth
    inner_shape = (regions, height, breadth, inner_width)
    outer_shape = (regions, height, breadth, full_width)

    current = features
    saved = []
    for b in range(chain):
        gain_pair, bias_pair = gain_all[b], bias_all[b]
        reduced = jnp.dot(
            current.reshape(cells, full_width), reduce_all[b], preferred_element_type=jnp.float32
        ).reshape(inner_shape)
        pre_reduce = gain_pair[0] * reduced + bias_pair[0]
        hidden_one = jnp.maximum(pre_reduce, 0.0).astype(jnp.bfloat16)
        hidden_ext = halo_rows(hidden_one)
        spatial_out = jnp.dot(
            grid_taps(hidden_ext, height, breadth, False),
            spatial_all[b].reshape(9 * inner_width, inner_width),
            preferred_element_type=jnp.float32,
        ).reshape(inner_shape)
        pre_spatial = gain_pair[1] * spatial_out + bias_pair[1]
        hidden_two = jnp.maximum(pre_spatial, 0.0).astype(jnp.bfloat16)
        expanded = jnp.dot(
            hidden_two.reshape(cells, inner_width), expand_all[b], preferred_element_type=jnp.float32
        ).reshape(outer_shape)
        block_out = (
            tissue_mask * jnp.maximum(current.astype(jnp.float32) + expanded, 0.0)
        ).astype(jnp.bfloat16)
        saved.append((current, hidden_ext, reduced, pre_reduce, spatial_out, pre_spatial, hidden_two, block_out))
        current = block_out

    classes = prototypes.shape[0]
    chosen = (row_label[:, :, None] == jnp.arange(classes, dtype=jnp.int32)).astype(jnp.float32)
    target_rows = jnp.einsum("mrk,kc->mrc", chosen, prototypes.astype(jnp.float32))
    total_cells = regions * height * lax.axis_size("tiles") * lax.axis_size("chan") * breadth
    upstream = (
        tissue_mask * (current.astype(jnp.float32) - target_rows[:, :, None, :]) / total_cells
    ).astype(jnp.bfloat16)

    block_ops = [None] * chain
    for b in reversed(range(chain)):
        block_in, hidden_ext, reduced, pre_reduce, spatial_out, pre_spatial, hidden_two, block_out = saved[b]
        needed = b >= position
        gain_pair = gain_all[b]

        def first_back(upstream=upstream, block_out=block_out, pre_spatial=pre_spatial, b=b, gain_pair=gain_pair):
            grad_block = jnp.where(block_out > 0, upstream, jnp.zeros_like(upstream))
            back_two = jnp.dot(
                grad_block.reshape(cells, full_width), expand_all[b].T, preferred_element_type=jnp.float32
            ).reshape(inner_shape)
            masked_two = jnp.where(pre_spatial > 0, back_two, jnp.float32(0.0))
            grad_two = (masked_two * gain_pair[1]).astype(jnp.bfloat16)
            return grad_block, masked_two, grad_two

        def first_skip():
            return (
                jnp.zeros(outer_shape, jnp.bfloat16),
                jnp.zeros(inner_shape, jnp.float32),
                jnp.zeros(inner_shape, jnp.bfloat16),
            )

        grad_block, masked_two, grad_two = lax.cond(needed, first_back, first_skip)
        grad_ext = halo_rows(grad_two)

        def second_back(grad_ext=grad_ext, pre_reduce=pre_reduce, b=b, gain_pair=gain_pair):
            back_one = jnp.dot(
                grid_taps(grad_ext, height, breadth, True),
                jnp.transpose(spatial_all[b], (0, 1, 3, 2)).reshape(9 * inner_width, inner_width),
                preferred_element_type=jnp.float32,
            ).reshape(inner_shape)
            masked_one = jnp.where(pre_reduce > 0, back_one, jnp.float32(0.0))
            grad_one = (masked_one * gain_pair[0]).astype(jnp.bfloat16)
            return masked_one, grad_one

        def second_skip():
            return (jnp.zeros(inner_shape, jnp.float32), jnp.zeros(inner_shape, jnp.bfloat16))

        masked_one, grad_one = lax.cond(needed, second_back, second_skip)
        block_ops[b] = (
            block_in, hidden_ext, hidden_two, reduced, spatial_out,
            grad_block, masked_two, grad_two, masked_one, grad_one,
        )
        if b > 0:

            def pass_back(grad_block=grad_block, grad_one=grad_one, b=b):
                return (
                    grad_block.astype(jnp.float32)
                    + jnp.dot(
                        grad_one.reshape(cells, inner_width),
                        reduce_all[b].T,
                        preferred_element_type=jnp.float32,
                    ).reshape(outer_shape)
                ).astype(jnp.bfloat16)

            upstream = lax.cond(
                b > position, pass_back, lambda: jnp.zeros(outer_shape, jnp.bfloat16)
            )

    pieces = lax.switch(
        position,
        [
            functools.partial(
                lambda k: weight_pair(block_ops[k], cells, height, breadth, chan_index), k
            )
            for k in range(chain)
        ],
    )
    theirs, mine = pieces[:3], pieces[3:]
    def pair_sum(own_piece, other_piece):
        arrived = lax.ppermute(other_piece, "chan", [(0, 1), (1, 0)])
        return (own_piece.astype(jnp.float32) + arrived.astype(jnp.float32)).astype(jnp.bfloat16)

    spatial_pair = pair_sum(mine[1], theirs[1])
    spatial_pair, later = lax.optimization_barrier(
        (spatial_pair, (mine[0], theirs[0], mine[2], theirs[2]))
    )
    spatial_total = lax.psum(spatial_pair, "tiles")
    reduce_pair = pair_sum(later[0], later[1])
    expand_pair = pair_sum(later[2], later[3])
    totals = (
        halving_all_reduce(reduce_pair[0], "tiles")[None],
        spatial_total,
        halving_all_reduce(expand_pair[0], "tiles")[None],
    )
    half_inner = inner_width // 2
    grad_reduce = totals[0]
    grad_spatial = totals[1][:, : 9 * inner_width].reshape(1, 3, 3, inner_width, half_inner)
    grad_expand = totals[2]
    small = totals[1][:, 9 * inner_width : 9 * inner_width + 4].astype(jnp.float32)
    return (grad_reduce, grad_spatial, grad_expand, small[:, 0:2], small[:, 2:4])


def solution(mesh):
    placed = (
        P("groups", ("tiles", "chan"), None, None),
        P("groups", ("tiles", "chan"), None),
        P("groups", ("tiles", "chan")),
        P(),
        P("sections", "chan", None),
        P("sections", None, None, None, "chan"),
        P("sections", None, "chan"),
        P("sections", None, None),
        P("sections", None, None),
    )
    return jax.shard_map(
        local,
        mesh=mesh,
        in_specs=placed,
        out_specs=(
            P(("groups", "sections"), "chan", None),
            P(("groups", "sections"), None, None, None, "chan"),
            P(("groups", "sections"), None, "chan"),
            P(("groups", "sections"), None, "chan"),
            P(("groups", "sections"), None, "chan"),
        ),
        check_vma=False,
    )
```

```python
import functools

import jax
import jax.numpy as jnp
from jax import lax
from jax.sharding import PartitionSpec as P

ROW_AXES = ("tiles", "chan")


def halo_rows(block):
    count = lax.axis_size(ROW_AXES)
    forward = [(i, i + 1) for i in range(count - 1)]
    backward = [(target, source) for source, target in forward]
    low = lax.ppermute(block[:, -1:], ROW_AXES, forward)
    high = lax.ppermute(block[:, :1], ROW_AXES, backward)
    return jnp.concatenate([low, block, high], axis=1)


def grid_taps(extended, height, breadth, mirrored):
    padded = jnp.pad(extended, ((0, 0), (0, 0), (1, 1), (0, 0)))
    tap_list = []
    for shift_row in range(3):
        for shift_col in range(3):
            if mirrored:
                start_row = 2 - shift_row
                start_col = 2 - shift_col
            else:
                start_row = shift_row
                start_col = shift_col
            tap_list.append(
                padded[:, start_row : start_row + height, start_col : start_col + breadth]
            )
    stacked = jnp.concatenate(tap_list, axis=3)
    return stacked.reshape(extended.shape[0] * height * breadth, stacked.shape[3])


def gather_blocks(half, chan_axis, chain, position, chan_index):
    received = [
        lax.ppermute(half, "sections", [(i, (i + k) % chain) for i in range(chain)])
        for k in range(1, chain)
    ]
    stacked = jnp.stack([half] + received)
    if chan_axis is not None:
        other = lax.ppermute(stacked, "chan", [(0, 1), (1, 0)])
        stacked = jnp.where(
            chan_index == 0,
            jnp.concatenate([stacked, other], axis=chan_axis + 1),
            jnp.concatenate([other, stacked], axis=chan_axis + 1),
        )
    return [
        lax.dynamic_index_in_dim(stacked, (position - b + chain) % chain, 0, keepdims=False)
        for b in range(chain)
    ]


def spatial_halves(ops, height, breadth, chan_index):
    cur, h1e, h2, reduced, spatial_out, grad_block, masked_two, grad_two, masked_one, grad_one = ops
    inner = h2.shape[-1]
    half_inner = inner // 2
    cells = grad_two.shape[0] * grad_two.shape[1] * grad_two.shape[2]
    taps = grid_taps(h1e, height, breadth, False)
    small = jnp.stack(
        [
            jnp.sum(masked_one * reduced, axis=(0, 1, 2)),
            jnp.sum(masked_two * spatial_out, axis=(0, 1, 2)),
            jnp.sum(masked_one, axis=(0, 1, 2)),
            jnp.sum(masked_two, axis=(0, 1, 2)),
        ]
    )
    pieces = []
    for half_index in (1 - chan_index, chan_index):
        two_half = lax.dynamic_slice_in_dim(
            grad_two.reshape(cells, inner), half_index * half_inner, half_inner, 1
        )
        spatial_term = jnp.dot(taps.T, two_half, preferred_element_type=jnp.float32)
        small_half = lax.dynamic_slice_in_dim(small, half_index * half_inner, half_inner, 1)
        small_rows = jnp.pad(small_half, ((0, 8 - small_half.shape[0]), (0, 0)))
        pieces.append(jnp.concatenate([spatial_term, small_rows], axis=0).astype(jnp.bfloat16)[None])
    return tuple(pieces)


def dense_halves(ops, chan_index):
    cur, h1e, h2, reduced, spatial_out, grad_block, masked_two, grad_two, masked_one, grad_one = ops
    full = cur.shape[-1]
    inner = h2.shape[-1]
    half_full = full // 2
    cells = cur.shape[0] * cur.shape[1] * cur.shape[2]
    pieces = []
    for half_index in (1 - chan_index, chan_index):
        cur_half = lax.dynamic_slice_in_dim(
            cur.reshape(cells, full), half_index * half_full, half_full, 1
        )
        block_half = lax.dynamic_slice_in_dim(
            grad_block.reshape(cells, full), half_index * half_full, half_full, 1
        )
        reduce_term = jnp.dot(
            cur_half.T, grad_one.reshape(cells, inner), preferred_element_type=jnp.float32
        )
        expand_term = jnp.dot(
            h2.reshape(cells, inner).T, block_half, preferred_element_type=jnp.float32
        )
        pieces.append(reduce_term.astype(jnp.bfloat16)[None])
        pieces.append(expand_term.astype(jnp.bfloat16)[None])
    return tuple(pieces)


def halving_all_reduce(value, axis):
    count = lax.axis_size(axis)
    assert count & (count - 1) == 0
    place = lax.axis_index(axis)
    steps = count.bit_length() - 1
    current = value
    for step in range(steps):
        bit = 1 << step
        upper = (place // bit) % 2
        half = current.shape[0] // 2
        keep = lax.dynamic_slice_in_dim(current, upper * half, half, 0)
        send = lax.dynamic_slice_in_dim(current, (1 - upper) * half, half, 0)
        got = lax.ppermute(send, axis, [(i, i ^ bit) for i in range(count)])
        current = (keep.astype(jnp.float32) + got.astype(jnp.float32)).astype(value.dtype)
    for step in reversed(range(steps)):
        bit = 1 << step
        upper = (place // bit) % 2
        got = lax.ppermute(current, axis, [(i, i ^ bit) for i in range(count)])
        current = jnp.where(
            upper == 0,
            jnp.concatenate([current, got], axis=0),
            jnp.concatenate([got, current], axis=0),
        )
    return current


def local(
    features,
    tissue,
    row_label,
    prototypes,
    reduce_weight,
    spatial_weight,
    expand_weight,
    norm_gain,
    norm_bias,
):
    regions, height, breadth, full_width = features.shape
    chain = lax.axis_size("sections")
    position = lax.axis_index("sections")
    chan_index = lax.axis_index("chan")
    reduce_all = gather_blocks(reduce_weight[0], 0, chain, position, chan_index)
    spatial_all = gather_blocks(spatial_weight[0], 3, chain, position, chan_index)
    expand_all = gather_blocks(expand_weight[0], 1, chain, position, chan_index)
    gain_all = gather_blocks(norm_gain[0], None, chain, position, chan_index)
    bias_all = gather_blocks(norm_bias[0], None, chain, position, chan_index)
    inner_width = reduce_all[0].shape[1]
    tissue_mask = tissue.astype(jnp.float32)[:, :, :, None]
    cells = regions * height * breadth
    inner_shape = (regions, height, breadth, inner_width)
    outer_shape = (regions, height, breadth, full_width)

    current = features
    saved = []
    for b in range(chain):
        gain_pair, bias_pair = gain_all[b], bias_all[b]
        reduced = jnp.dot(
            current.reshape(cells, full_width), reduce_all[b], preferred_element_type=jnp.float32
        ).reshape(inner_shape)
        pre_reduce = gain_pair[0] * reduced + bias_pair[0]
        hidden_one = jnp.maximum(pre_reduce, 0.0).astype(jnp.bfloat16)
        hidden_ext = halo_rows(hidden_one)
        spatial_out = jnp.dot(
            grid_taps(hidden_ext, height, breadth, False),
            spatial_all[b].reshape(9 * inner_width, inner_width),
            preferred_element_type=jnp.float32,
        ).reshape(inner_shape)
        pre_spatial = gain_pair[1] * spatial_out + bias_pair[1]
        hidden_two = jnp.maximum(pre_spatial, 0.0).astype(jnp.bfloat16)
        expanded = jnp.dot(
            hidden_two.reshape(cells, inner_width), expand_all[b], preferred_element_type=jnp.float32
        ).reshape(outer_shape)
        block_out = (
            tissue_mask * jnp.maximum(current.astype(jnp.float32) + expanded, 0.0)
        ).astype(jnp.bfloat16)
        saved.append((current, hidden_ext, reduced, pre_reduce, spatial_out, pre_spatial, hidden_two, block_out))
        current = block_out

    classes = prototypes.shape[0]
    chosen = (row_label[:, :, None] == jnp.arange(classes, dtype=jnp.int32)).astype(jnp.float32)
    target_rows = jnp.einsum("mrk,kc->mrc", chosen, prototypes.astype(jnp.float32))
    total_cells = regions * height * lax.axis_size("tiles") * lax.axis_size("chan") * breadth
    upstream = (
        tissue_mask * (current.astype(jnp.float32) - target_rows[:, :, None, :]) / total_cells
    ).astype(jnp.bfloat16)

    block_ops = [None] * chain
    for b in reversed(range(chain)):
        block_in, hidden_ext, reduced, pre_reduce, spatial_out, pre_spatial, hidden_two, block_out = saved[b]
        needed = b >= position
        gain_pair = gain_all[b]

        def first_back(upstream=upstream, block_out=block_out, pre_spatial=pre_spatial, b=b, gain_pair=gain_pair):
            grad_block = jnp.where(block_out > 0, upstream, jnp.zeros_like(upstream))
            back_two = jnp.dot(
                grad_block.reshape(cells, full_width), expand_all[b].T, preferred_element_type=jnp.float32
            ).reshape(inner_shape)
            masked_two = jnp.where(pre_spatial > 0, back_two, jnp.float32(0.0))
            grad_two = (masked_two * gain_pair[1]).astype(jnp.bfloat16)
            return grad_block, masked_two, grad_two

        def first_skip():
            return (
                jnp.zeros(outer_shape, jnp.bfloat16),
                jnp.zeros(inner_shape, jnp.float32),
                jnp.zeros(inner_shape, jnp.bfloat16),
            )

        grad_block, masked_two, grad_two = lax.cond(needed, first_back, first_skip)
        grad_ext = halo_rows(grad_two)

        def second_back(grad_ext=grad_ext, pre_reduce=pre_reduce, b=b, gain_pair=gain_pair):
            back_one = jnp.dot(
                grid_taps(grad_ext, height, breadth, True),
                jnp.transpose(spatial_all[b], (0, 1, 3, 2)).reshape(9 * inner_width, inner_width),
                preferred_element_type=jnp.float32,
            ).reshape(inner_shape)
            masked_one = jnp.where(pre_reduce > 0, back_one, jnp.float32(0.0))
            grad_one = (masked_one * gain_pair[0]).astype(jnp.bfloat16)
            return masked_one, grad_one

        def second_skip():
            return (jnp.zeros(inner_shape, jnp.float32), jnp.zeros(inner_shape, jnp.bfloat16))

        masked_one, grad_one = lax.cond(needed, second_back, second_skip)
        block_ops[b] = (
            block_in, hidden_ext, hidden_two, reduced, spatial_out,
            grad_block, masked_two, grad_two, masked_one, grad_one,
        )
        if b > 0:

            def pass_back(grad_block=grad_block, grad_one=grad_one, b=b):
                return (
                    grad_block.astype(jnp.float32)
                    + jnp.dot(
                        grad_one.reshape(cells, inner_width),
                        reduce_all[b].T,
                        preferred_element_type=jnp.float32,
                    ).reshape(outer_shape)
                ).astype(jnp.bfloat16)

            upstream = lax.cond(
                b > position, pass_back, lambda: jnp.zeros(outer_shape, jnp.bfloat16)
            )

    def pair_sum(own_piece, other_piece):
        arrived = lax.ppermute(other_piece, "chan", [(0, 1), (1, 0)])
        return (own_piece.astype(jnp.float32) + arrived.astype(jnp.float32)).astype(jnp.bfloat16)

    spatial_theirs, spatial_mine = lax.switch(
        position,
        [
            functools.partial(lambda k: spatial_halves(block_ops[k], height, breadth, chan_index), k)
            for k in range(chain)
        ],
    )
    spatial_pair = pair_sum(spatial_mine, spatial_theirs)
    spatial_pair, later_ops = lax.optimization_barrier((spatial_pair, block_ops))
    spatial_total = lax.psum(spatial_pair, "tiles")
    reduce_theirs, expand_theirs, reduce_mine, expand_mine = lax.switch(
        position,
        [
            functools.partial(lambda k: dense_halves(later_ops[k], chan_index), k)
            for k in range(chain)
        ],
    )
    reduce_pair = pair_sum(reduce_mine, reduce_theirs)
    expand_pair = pair_sum(expand_mine, expand_theirs)
    totals = (
        halving_all_reduce(reduce_pair[0], "tiles")[None],
        spatial_total,
        halving_all_reduce(expand_pair[0], "tiles")[None],
    )
    half_inner = inner_width // 2
    grad_reduce = totals[0]
    grad_spatial = totals[1][:, : 9 * inner_width].reshape(1, 3, 3, inner_width, half_inner)
    grad_expand = totals[2]
    small = totals[1][:, 9 * inner_width : 9 * inner_width + 4].astype(jnp.float32)
    return (grad_reduce, grad_spatial, grad_expand, small[:, 0:2], small[:, 2:4])


def solution(mesh):
    placed = (
        P("groups", ("tiles", "chan"), None, None),
        P("groups", ("tiles", "chan"), None),
        P("groups", ("tiles", "chan")),
        P(),
        P("sections", "chan", None),
        P("sections", None, None, None, "chan"),
        P("sections", None, "chan"),
        P("sections", None, None),
        P("sections", None, None),
    )
    return jax.shard_map(
        local,
        mesh=mesh,
        in_specs=placed,
        out_specs=(
            P(("groups", "sections"), "chan", None),
            P(("groups", "sections"), None, None, None, "chan"),
            P(("groups", "sections"), None, "chan"),
            P(("groups", "sections"), None, "chan"),
            P(("groups", "sections"), None, "chan"),
        ),
        check_vma=False,
    )
```

```python
import functools

import jax
import jax.numpy as jnp
from jax import lax
from jax.sharding import PartitionSpec as P

ROW_AXES = ("tiles", "chan")


def halo_rows(block):
    count = lax.axis_size(ROW_AXES)
    forward = [(i, i + 1) for i in range(count - 1)]
    backward = [(target, source) for source, target in forward]
    low = lax.ppermute(block[:, -1:], ROW_AXES, forward)
    high = lax.ppermute(block[:, :1], ROW_AXES, backward)
    return jnp.concatenate([low, block, high], axis=1)


def grid_taps(extended, height, breadth, mirrored):
    padded = jnp.pad(extended, ((0, 0), (0, 0), (1, 1), (0, 0)))
    tap_list = []
    for shift_row in range(3):
        for shift_col in range(3):
            if mirrored:
                start_row = 2 - shift_row
                start_col = 2 - shift_col
            else:
                start_row = shift_row
                start_col = shift_col
            tap_list.append(
                padded[:, start_row : start_row + height, start_col : start_col + breadth]
            )
    stacked = jnp.concatenate(tap_list, axis=3)
    return stacked.reshape(extended.shape[0] * height * breadth, stacked.shape[3])


def gather_blocks(half, chan_axis, chain, position, chan_index):
    received = [
        lax.ppermute(half, "sections", [(i, (i + k) % chain) for i in range(chain)])
        for k in range(1, chain)
    ]
    stacked = jnp.stack([half] + received)
    if chan_axis is not None:
        other = lax.ppermute(stacked, "chan", [(0, 1), (1, 0)])
        stacked = jnp.where(
            chan_index == 0,
            jnp.concatenate([stacked, other], axis=chan_axis + 1),
            jnp.concatenate([other, stacked], axis=chan_axis + 1),
        )
    indexed = [
        lax.dynamic_index_in_dim(stacked, (position - b + chain) % chain, 0, keepdims=False)
        for b in range(chain)
    ]
    selected = []
    for b in range(chain):
        slot = (position - b + chain) % chain
        chosen = stacked[chain - 1]
        for k in reversed(range(chain - 1)):
            chosen = jnp.where(slot == k, stacked[k], chosen)
        selected.append(chosen)
    return selected, indexed


def spatial_halves(ops, height, breadth, chan_index):
    cur, h1e, h2, reduced, spatial_out, grad_block, masked_two, grad_two, masked_one, grad_one = ops
    inner = h2.shape[-1]
    half_inner = inner // 2
    cells = grad_two.shape[0] * grad_two.shape[1] * grad_two.shape[2]
    taps = grid_taps(h1e, height, breadth, False)
    small = jnp.stack(
        [
            jnp.sum(masked_one * reduced, axis=(0, 1, 2)),
            jnp.sum(masked_two * spatial_out, axis=(0, 1, 2)),
            jnp.sum(masked_one, axis=(0, 1, 2)),
            jnp.sum(masked_two, axis=(0, 1, 2)),
        ]
    )
    pieces = []
    for half_index in (1 - chan_index, chan_index):
        two_half = lax.dynamic_slice_in_dim(
            grad_two.reshape(cells, inner), half_index * half_inner, half_inner, 1
        )
        spatial_term = jnp.dot(taps.T, two_half, preferred_element_type=jnp.float32)
        small_half = lax.dynamic_slice_in_dim(small, half_index * half_inner, half_inner, 1)
        small_rows = jnp.pad(small_half, ((0, 8 - small_half.shape[0]), (0, 0)))
        pieces.append(jnp.concatenate([spatial_term, small_rows], axis=0).astype(jnp.bfloat16)[None])
    return tuple(pieces)


def dense_halves(ops, chan_index):
    cur, h1e, h2, reduced, spatial_out, grad_block, masked_two, grad_two, masked_one, grad_one = ops
    full = cur.shape[-1]
    inner = h2.shape[-1]
    half_full = full // 2
    cells = cur.shape[0] * cur.shape[1] * cur.shape[2]
    pieces = []
    for half_index in (1 - chan_index, chan_index):
        cur_half = lax.dynamic_slice_in_dim(
            cur.reshape(cells, full), half_index * half_full, half_full, 1
        )
        block_half = lax.dynamic_slice_in_dim(
            grad_block.reshape(cells, full), half_index * half_full, half_full, 1
        )
        reduce_term = jnp.dot(
            cur_half.T, grad_one.reshape(cells, inner), preferred_element_type=jnp.float32
        )
        expand_term = jnp.dot(
            h2.reshape(cells, inner).T, block_half, preferred_element_type=jnp.float32
        )
        pieces.append(reduce_term.astype(jnp.bfloat16)[None])
        pieces.append(expand_term.astype(jnp.bfloat16)[None])
    return tuple(pieces)


def halving_all_reduce(value, axis):
    count = lax.axis_size(axis)
    assert count & (count - 1) == 0
    place = lax.axis_index(axis)
    steps = count.bit_length() - 1
    current = value
    for step in range(steps):
        bit = 1 << step
        upper = (place // bit) % 2
        half = current.shape[0] // 2
        keep = lax.dynamic_slice_in_dim(current, upper * half, half, 0)
        send = lax.dynamic_slice_in_dim(current, (1 - upper) * half, half, 0)
        got = lax.ppermute(send, axis, [(i, i ^ bit) for i in range(count)])
        current = (keep.astype(jnp.float32) + got.astype(jnp.float32)).astype(value.dtype)
    for step in reversed(range(steps)):
        bit = 1 << step
        upper = (place // bit) % 2
        got = lax.ppermute(current, axis, [(i, i ^ bit) for i in range(count)])
        current = jnp.where(
            upper == 0,
            jnp.concatenate([current, got], axis=0),
            jnp.concatenate([got, current], axis=0),
        )
    return current


def local(
    features,
    tissue,
    row_label,
    prototypes,
    reduce_weight,
    spatial_weight,
    expand_weight,
    norm_gain,
    norm_bias,
):
    regions, height, breadth, full_width = features.shape
    chain = lax.axis_size("sections")
    position = lax.axis_index("sections")
    chan_index = lax.axis_index("chan")
    reduce_all = gather_blocks(reduce_weight[0], 0, chain, position, chan_index)[0]
    spatial_all, spatial_indexed = gather_blocks(spatial_weight[0], 3, chain, position, chan_index)
    expand_all = gather_blocks(expand_weight[0], 1, chain, position, chan_index)[0]
    gain_all = gather_blocks(norm_gain[0], None, chain, position, chan_index)[1]
    bias_all = gather_blocks(norm_bias[0], None, chain, position, chan_index)[1]
    inner_width = reduce_all[0].shape[1]
    tissue_mask = tissue.astype(jnp.float32)[:, :, :, None]
    cells = regions * height * breadth
    inner_shape = (regions, height, breadth, inner_width)
    outer_shape = (regions, height, breadth, full_width)

    current = features
    saved = []
    for b in range(chain):
        gain_pair, bias_pair = gain_all[b], bias_all[b]
        reduced = jnp.dot(
            current.reshape(cells, full_width), reduce_all[b], preferred_element_type=jnp.float32
        ).reshape(inner_shape)
        pre_reduce = gain_pair[0] * reduced + bias_pair[0]
        hidden_one = jnp.maximum(pre_reduce, 0.0).astype(jnp.bfloat16)
        hidden_ext = halo_rows(hidden_one)
        spatial_out = jnp.dot(
            grid_taps(hidden_ext, height, breadth, False),
            spatial_all[b].reshape(9 * inner_width, inner_width),
            preferred_element_type=jnp.float32,
        ).reshape(inner_shape)
        pre_spatial = gain_pair[1] * spatial_out + bias_pair[1]
        hidden_two = jnp.maximum(pre_spatial, 0.0).astype(jnp.bfloat16)
        expanded = jnp.dot(
            hidden_two.reshape(cells, inner_width), expand_all[b], preferred_element_type=jnp.float32
        ).reshape(outer_shape)
        block_out = (
            tissue_mask * jnp.maximum(current.astype(jnp.float32) + expanded, 0.0)
        ).astype(jnp.bfloat16)
        saved.append((current, hidden_ext, reduced, pre_reduce, spatial_out, pre_spatial, hidden_two, block_out))
        current = block_out

    classes = prototypes.shape[0]
    chosen = (row_label[:, :, None] == jnp.arange(classes, dtype=jnp.int32)).astype(jnp.float32)
    target_rows = jnp.einsum("mrk,kc->mrc", chosen, prototypes.astype(jnp.float32))
    total_cells = regions * height * lax.axis_size("tiles") * lax.axis_size("chan") * breadth
    upstream = (
        tissue_mask * (current.astype(jnp.float32) - target_rows[:, :, None, :]) / total_cells
    ).astype(jnp.bfloat16)

    block_ops = [None] * chain
    for b in reversed(range(chain)):
        block_in, hidden_ext, reduced, pre_reduce, spatial_out, pre_spatial, hidden_two, block_out = saved[b]
        needed = b >= position
        gain_pair = gain_all[b]

        def first_back(upstream=upstream, block_out=block_out, pre_spatial=pre_spatial, b=b, gain_pair=gain_pair):
            grad_block = jnp.where(block_out > 0, upstream, jnp.zeros_like(upstream))
            back_two = jnp.dot(
                grad_block.reshape(cells, full_width), expand_all[b].T, preferred_element_type=jnp.float32
            ).reshape(inner_shape)
            masked_two = jnp.where(pre_spatial > 0, back_two, jnp.float32(0.0))
            grad_two = (masked_two * gain_pair[1]).astype(jnp.bfloat16)
            return grad_block, masked_two, grad_two

        def first_skip():
            return (
                jnp.zeros(outer_shape, jnp.bfloat16),
                jnp.zeros(inner_shape, jnp.float32),
                jnp.zeros(inner_shape, jnp.bfloat16),
            )

        grad_block, masked_two, grad_two = lax.cond(needed, first_back, first_skip)
        grad_ext = halo_rows(grad_two)

        def second_back(grad_ext=grad_ext, pre_reduce=pre_reduce, b=b, gain_pair=gain_pair):
            back_one = jnp.dot(
                grid_taps(grad_ext, height, breadth, True),
                jnp.transpose(spatial_indexed[b], (0, 1, 3, 2)).reshape(9 * inner_width, inner_width),
                preferred_element_type=jnp.float32,
            ).reshape(inner_shape)
            masked_one = jnp.where(pre_reduce > 0, back_one, jnp.float32(0.0))
            grad_one = (masked_one * gain_pair[0]).astype(jnp.bfloat16)
            return masked_one, grad_one

        def second_skip():
            return (jnp.zeros(inner_shape, jnp.float32), jnp.zeros(inner_shape, jnp.bfloat16))

        masked_one, grad_one = lax.cond(needed, second_back, second_skip)
        block_ops[b] = (
            block_in, hidden_ext, hidden_two, reduced, spatial_out,
            grad_block, masked_two, grad_two, masked_one, grad_one,
        )
        if b > 0:

            def pass_back(grad_block=grad_block, grad_one=grad_one, b=b):
                return (
                    grad_block.astype(jnp.float32)
                    + jnp.dot(
                        grad_one.reshape(cells, inner_width),
                        reduce_all[b].T,
                        preferred_element_type=jnp.float32,
                    ).reshape(outer_shape)
                ).astype(jnp.bfloat16)

            upstream = lax.cond(
                b > position, pass_back, lambda: jnp.zeros(outer_shape, jnp.bfloat16)
            )

    def pair_sum(own_piece, other_piece):
        arrived = lax.ppermute(other_piece, "chan", [(0, 1), (1, 0)])
        return (own_piece.astype(jnp.float32) + arrived.astype(jnp.float32)).astype(jnp.bfloat16)

    spatial_theirs, spatial_mine = lax.switch(
        position,
        [
            functools.partial(lambda k: spatial_halves(block_ops[k], height, breadth, chan_index), k)
            for k in range(chain)
        ],
    )
    spatial_pair = pair_sum(spatial_mine, spatial_theirs)
    spatial_pair, later_ops = lax.optimization_barrier((spatial_pair, block_ops))
    spatial_total = lax.psum(spatial_pair, "tiles")
    reduce_theirs, expand_theirs, reduce_mine, expand_mine = lax.switch(
        position,
        [
            functools.partial(lambda k: dense_halves(later_ops[k], chan_index), k)
            for k in range(chain)
        ],
    )
    reduce_pair = pair_sum(reduce_mine, reduce_theirs)
    expand_pair = pair_sum(expand_mine, expand_theirs)
    totals = (
        halving_all_reduce(reduce_pair[0], "tiles")[None],
        spatial_total,
        halving_all_reduce(expand_pair[0], "tiles")[None],
    )
    half_inner = inner_width // 2
    grad_reduce = totals[0]
    grad_spatial = totals[1][:, : 9 * inner_width].reshape(1, 3, 3, inner_width, half_inner)
    grad_expand = totals[2]
    small = totals[1][:, 9 * inner_width : 9 * inner_width + 4].astype(jnp.float32)
    return (grad_reduce, grad_spatial, grad_expand, small[:, 0:2], small[:, 2:4])


def solution(mesh):
    placed = (
        P("groups", ("tiles", "chan"), None, None),
        P("groups", ("tiles", "chan"), None),
        P("groups", ("tiles", "chan")),
        P(),
        P("sections", "chan", None),
        P("sections", None, None, None, "chan"),
        P("sections", None, "chan"),
        P("sections", None, None),
        P("sections", None, None),
    )
    return jax.shard_map(
        local,
        mesh=mesh,
        in_specs=placed,
        out_specs=(
            P(("groups", "sections"), "chan", None),
            P(("groups", "sections"), None, None, None, "chan"),
            P(("groups", "sections"), None, "chan"),
            P(("groups", "sections"), None, "chan"),
            P(("groups", "sections"), None, "chan"),
        ),
        check_vma=False,
    )
```

```python
import functools

import jax
import jax.numpy as jnp
from jax import lax
from jax.sharding import PartitionSpec as P

ROW_AXES = ("tiles", "chan")


def halo_rows(block):
    count = lax.axis_size(ROW_AXES)
    forward = [(i, i + 1) for i in range(count - 1)]
    backward = [(target, source) for source, target in forward]
    low = lax.ppermute(block[:, -1:], ROW_AXES, forward)
    high = lax.ppermute(block[:, :1], ROW_AXES, backward)
    return jnp.concatenate([low, block, high], axis=1)


def grid_taps(extended, height, breadth, mirrored):
    padded = jnp.pad(extended, ((0, 0), (0, 0), (1, 1), (0, 0)))
    tap_list = []
    for shift_row in range(3):
        for shift_col in range(3):
            if mirrored:
                start_row = 2 - shift_row
                start_col = 2 - shift_col
            else:
                start_row = shift_row
                start_col = shift_col
            tap_list.append(
                padded[:, start_row : start_row + height, start_col : start_col + breadth]
            )
    stacked = jnp.concatenate(tap_list, axis=3)
    return stacked.reshape(extended.shape[0] * height * breadth, stacked.shape[3])


def gather_blocks(half, chan_axis, chain, position, chan_index):
    received = [
        lax.ppermute(half, "sections", [(i, (i + k) % chain) for i in range(chain)])
        for k in range(1, chain)
    ]
    stacked = jnp.stack([half] + received)
    if chan_axis is not None:
        other = lax.ppermute(stacked, "chan", [(0, 1), (1, 0)])
        stacked = jnp.where(
            chan_index == 0,
            jnp.concatenate([stacked, other], axis=chan_axis + 1),
            jnp.concatenate([other, stacked], axis=chan_axis + 1),
        )
    return [
        lax.dynamic_index_in_dim(stacked, (position - b + chain) % chain, 0, keepdims=False)
        for b in range(chain)
    ]


def spatial_halves(ops, height, breadth, chan_index):
    cur, h1e, h2, reduced, spatial_out, grad_block, masked_two, grad_two, masked_one, grad_one = ops
    inner = h2.shape[-1]
    half_inner = inner // 2
    cells = grad_two.shape[0] * grad_two.shape[1] * grad_two.shape[2]
    taps = grid_taps(h1e, height, breadth, False)
    small = jnp.stack(
        [
            jnp.sum(masked_one * reduced, axis=(0, 1, 2)),
            jnp.sum(masked_two * spatial_out, axis=(0, 1, 2)),
            jnp.sum(masked_one, axis=(0, 1, 2)),
            jnp.sum(masked_two, axis=(0, 1, 2)),
        ]
    )
    pieces = []
    for half_index in (1 - chan_index, chan_index):
        two_half = lax.dynamic_slice_in_dim(
            grad_two.reshape(cells, inner), half_index * half_inner, half_inner, 1
        )
        spatial_term = jnp.dot(taps.T, two_half, preferred_element_type=jnp.float32)
        small_half = lax.dynamic_slice_in_dim(small, half_index * half_inner, half_inner, 1)
        small_rows = jnp.pad(small_half, ((0, 8 - small_half.shape[0]), (0, 0)))
        pieces.append(jnp.concatenate([spatial_term, small_rows], axis=0).astype(jnp.bfloat16)[None])
    return tuple(pieces)


def dense_halves(ops, chan_index):
    cur, h1e, h2, reduced, spatial_out, grad_block, masked_two, grad_two, masked_one, grad_one = ops
    full = cur.shape[-1]
    inner = h2.shape[-1]
    half_full = full // 2
    cells = cur.shape[0] * cur.shape[1] * cur.shape[2]
    pieces = []
    for half_index in (1 - chan_index, chan_index):
        cur_half = lax.dynamic_slice_in_dim(
            cur.reshape(cells, full), half_index * half_full, half_full, 1
        )
        block_half = lax.dynamic_slice_in_dim(
            grad_block.reshape(cells, full), half_index * half_full, half_full, 1
        )
        reduce_term = jnp.dot(
            cur_half.T, grad_one.reshape(cells, inner), preferred_element_type=jnp.float32
        )
        expand_term = jnp.dot(
            h2.reshape(cells, inner).T, block_half, preferred_element_type=jnp.float32
        )
        pieces.append(reduce_term.astype(jnp.bfloat16)[None])
        pieces.append(expand_term.astype(jnp.bfloat16)[None])
    return tuple(pieces)


def halving_all_reduce(value, axis):
    count = lax.axis_size(axis)
    assert count & (count - 1) == 0
    place = lax.axis_index(axis)
    steps = count.bit_length() - 1
    rows = value.shape[0]
    spare = (-rows) % count
    current = jnp.pad(value, ((0, spare),) + ((0, 0),) * (value.ndim - 1))
    for step in range(steps):
        bit = 1 << step
        upper = (place // bit) % 2
        half = current.shape[0] // 2
        keep = lax.dynamic_slice_in_dim(current, upper * half, half, 0)
        send = lax.dynamic_slice_in_dim(current, (1 - upper) * half, half, 0)
        got = lax.ppermute(send, axis, [(i, i ^ bit) for i in range(count)])
        current = (keep.astype(jnp.float32) + got.astype(jnp.float32)).astype(value.dtype)
    for step in reversed(range(steps)):
        bit = 1 << step
        upper = (place // bit) % 2
        got = lax.ppermute(current, axis, [(i, i ^ bit) for i in range(count)])
        current = jnp.where(
            upper == 0,
            jnp.concatenate([current, got], axis=0),
            jnp.concatenate([got, current], axis=0),
        )
    return current[:rows]


def local(
    features,
    tissue,
    row_label,
    prototypes,
    reduce_weight,
    spatial_weight,
    expand_weight,
    norm_gain,
    norm_bias,
):
    regions, height, breadth, full_width = features.shape
    chain = lax.axis_size("sections")
    position = lax.axis_index("sections")
    chan_index = lax.axis_index("chan")
    reduce_all = gather_blocks(reduce_weight[0], 0, chain, position, chan_index)
    spatial_all = gather_blocks(spatial_weight[0], 3, chain, position, chan_index)
    expand_all = gather_blocks(expand_weight[0], 1, chain, position, chan_index)
    gain_all = gather_blocks(norm_gain[0], None, chain, position, chan_index)
    bias_all = gather_blocks(norm_bias[0], None, chain, position, chan_index)
    inner_width = reduce_all[0].shape[1]
    tissue_mask = tissue.astype(jnp.float32)[:, :, :, None]
    cells = regions * height * breadth
    inner_shape = (regions, height, breadth, inner_width)
    outer_shape = (regions, height, breadth, full_width)

    current = features
    saved = []
    for b in range(chain):
        gain_pair, bias_pair = gain_all[b], bias_all[b]
        reduced = jnp.dot(
            current.reshape(cells, full_width), reduce_all[b], preferred_element_type=jnp.float32
        ).reshape(inner_shape)
        pre_reduce = gain_pair[0] * reduced + bias_pair[0]
        hidden_one = jnp.maximum(pre_reduce, 0.0).astype(jnp.bfloat16)
        hidden_ext = halo_rows(hidden_one)
        spatial_out = jnp.dot(
            grid_taps(hidden_ext, height, breadth, False),
            spatial_all[b].reshape(9 * inner_width, inner_width),
            preferred_element_type=jnp.float32,
        ).reshape(inner_shape)
        pre_spatial = gain_pair[1] * spatial_out + bias_pair[1]
        hidden_two = jnp.maximum(pre_spatial, 0.0).astype(jnp.bfloat16)
        expanded = jnp.dot(
            hidden_two.reshape(cells, inner_width), expand_all[b], preferred_element_type=jnp.float32
        ).reshape(outer_shape)
        block_out = (
            tissue_mask * jnp.maximum(current.astype(jnp.float32) + expanded, 0.0)
        ).astype(jnp.bfloat16)
        saved.append((current, hidden_ext, reduced, pre_reduce, spatial_out, pre_spatial, hidden_two, block_out))
        current = block_out

    classes = prototypes.shape[0]
    chosen = (row_label[:, :, None] == jnp.arange(classes, dtype=jnp.int32)).astype(jnp.float32)
    target_rows = jnp.einsum("mrk,kc->mrc", chosen, prototypes.astype(jnp.float32))
    total_cells = regions * height * lax.axis_size("tiles") * lax.axis_size("chan") * breadth
    upstream = (
        tissue_mask * (current.astype(jnp.float32) - target_rows[:, :, None, :]) / total_cells
    ).astype(jnp.bfloat16)

    block_ops = [None] * chain
    for b in reversed(range(chain)):
        block_in, hidden_ext, reduced, pre_reduce, spatial_out, pre_spatial, hidden_two, block_out = saved[b]
        needed = b >= position
        gain_pair = gain_all[b]

        def first_back(upstream=upstream, block_out=block_out, pre_spatial=pre_spatial, b=b, gain_pair=gain_pair):
            grad_block = jnp.where(block_out > 0, upstream, jnp.zeros_like(upstream))
            back_two = jnp.dot(
                grad_block.reshape(cells, full_width), expand_all[b].T, preferred_element_type=jnp.float32
            ).reshape(inner_shape)
            masked_two = jnp.where(pre_spatial > 0, back_two, jnp.float32(0.0))
            grad_two = (masked_two * gain_pair[1]).astype(jnp.bfloat16)
            return grad_block, masked_two, grad_two

        def first_skip():
            return (
                jnp.zeros(outer_shape, jnp.bfloat16),
                jnp.zeros(inner_shape, jnp.float32),
                jnp.zeros(inner_shape, jnp.bfloat16),
            )

        grad_block, masked_two, grad_two = lax.cond(needed, first_back, first_skip)
        grad_ext = halo_rows(grad_two)

        def second_back(grad_ext=grad_ext, pre_reduce=pre_reduce, b=b, gain_pair=gain_pair):
            back_one = jnp.dot(
                grid_taps(grad_ext, height, breadth, True),
                jnp.transpose(spatial_all[b], (0, 1, 3, 2)).reshape(9 * inner_width, inner_width),
                preferred_element_type=jnp.float32,
            ).reshape(inner_shape)
            masked_one = jnp.where(pre_reduce > 0, back_one, jnp.float32(0.0))
            grad_one = (masked_one * gain_pair[0]).astype(jnp.bfloat16)
            return masked_one, grad_one

        def second_skip():
            return (jnp.zeros(inner_shape, jnp.float32), jnp.zeros(inner_shape, jnp.bfloat16))

        masked_one, grad_one = lax.cond(needed, second_back, second_skip)
        block_ops[b] = (
            block_in, hidden_ext, hidden_two, reduced, spatial_out,
            grad_block, masked_two, grad_two, masked_one, grad_one,
        )
        if b > 0:

            def pass_back(grad_block=grad_block, grad_one=grad_one, b=b):
                return (
                    grad_block.astype(jnp.float32)
                    + jnp.dot(
                        grad_one.reshape(cells, inner_width),
                        reduce_all[b].T,
                        preferred_element_type=jnp.float32,
                    ).reshape(outer_shape)
                ).astype(jnp.bfloat16)

            upstream = lax.cond(
                b > position, pass_back, lambda: jnp.zeros(outer_shape, jnp.bfloat16)
            )

    def pair_sum(own_piece, other_piece):
        arrived = lax.ppermute(other_piece, "chan", [(0, 1), (1, 0)])
        return (own_piece.astype(jnp.float32) + arrived.astype(jnp.float32)).astype(jnp.bfloat16)

    spatial_theirs, spatial_mine = lax.switch(
        position,
        [
            functools.partial(lambda k: spatial_halves(block_ops[k], height, breadth, chan_index), k)
            for k in range(chain)
        ],
    )
    spatial_pair = pair_sum(spatial_mine, spatial_theirs)
    spatial_pair, later_ops = lax.optimization_barrier((spatial_pair, block_ops))
    spatial_total = halving_all_reduce(spatial_pair[0], "tiles")[None]
    reduce_theirs, expand_theirs, reduce_mine, expand_mine = lax.switch(
        position,
        [
            functools.partial(lambda k: dense_halves(later_ops[k], chan_index), k)
            for k in range(chain)
        ],
    )
    reduce_pair = pair_sum(reduce_mine, reduce_theirs)
    expand_pair = pair_sum(expand_mine, expand_theirs)
    totals = (
        halving_all_reduce(reduce_pair[0], "tiles")[None],
        spatial_total,
        halving_all_reduce(expand_pair[0], "tiles")[None],
    )
    half_inner = inner_width // 2
    grad_reduce = totals[0]
    grad_spatial = totals[1][:, : 9 * inner_width].reshape(1, 3, 3, inner_width, half_inner)
    grad_expand = totals[2]
    small = totals[1][:, 9 * inner_width : 9 * inner_width + 4].astype(jnp.float32)
    return (grad_reduce, grad_spatial, grad_expand, small[:, 0:2], small[:, 2:4])


def solution(mesh):
    placed = (
        P("groups", ("tiles", "chan"), None, None),
        P("groups", ("tiles", "chan"), None),
        P("groups", ("tiles", "chan")),
        P(),
        P("sections", "chan", None),
        P("sections", None, None, None, "chan"),
        P("sections", None, "chan"),
        P("sections", None, None),
        P("sections", None, None),
    )
    return jax.shard_map(
        local,
        mesh=mesh,
        in_specs=placed,
        out_specs=(
            P(("groups", "sections"), "chan", None),
            P(("groups", "sections"), None, None, None, "chan"),
            P(("groups", "sections"), None, "chan"),
            P(("groups", "sections"), None, "chan"),
            P(("groups", "sections"), None, "chan"),
        ),
        check_vma=False,
    )
```

```python
import functools

import jax
import jax.numpy as jnp
from jax import lax
from jax.sharding import PartitionSpec as P

ROW_AXES = ("tiles", "chan")


def halo_rows(block):
    count = lax.axis_size(ROW_AXES)
    forward = [(i, i + 1) for i in range(count - 1)]
    backward = [(target, source) for source, target in forward]
    low = lax.ppermute(block[:, -1:], ROW_AXES, forward)
    high = lax.ppermute(block[:, :1], ROW_AXES, backward)
    return jnp.concatenate([low, block, high], axis=1)


def grid_taps(extended, height, breadth, mirrored):
    padded = jnp.pad(extended, ((0, 0), (0, 0), (1, 1), (0, 0)))
    tap_list = []
    for shift_row in range(3):
        for shift_col in range(3):
            if mirrored:
                start_row = 2 - shift_row
                start_col = 2 - shift_col
            else:
                start_row = shift_row
                start_col = shift_col
            tap_list.append(
                padded[:, start_row : start_row + height, start_col : start_col + breadth]
            )
    stacked = jnp.concatenate(tap_list, axis=3)
    return stacked.reshape(extended.shape[0] * height * breadth, stacked.shape[3])


def gather_blocks(half, chan_axis, chain, position, chan_index):
    received = [
        lax.ppermute(half, "sections", [(i, (i + k) % chain) for i in range(chain)])
        for k in range(1, chain)
    ]
    parts = [half] + received
    if chan_axis is not None:
        joined = []
        for part in parts:
            other = lax.ppermute(part, "chan", [(0, 1), (1, 0)])
            joined.append(
                jnp.where(
                    chan_index == 0,
                    jnp.concatenate([part, other], axis=chan_axis),
                    jnp.concatenate([other, part], axis=chan_axis),
                )
            )
        parts = joined
    stacked = jnp.stack(parts)
    return [
        lax.dynamic_index_in_dim(stacked, (position - b + chain) % chain, 0, keepdims=False)
        for b in range(chain)
    ]


def spatial_halves(ops, height, breadth, chan_index):
    cur, h1e, h2, reduced, spatial_out, grad_block, masked_two, grad_two, masked_one, grad_one = ops
    inner = h2.shape[-1]
    half_inner = inner // 2
    cells = grad_two.shape[0] * grad_two.shape[1] * grad_two.shape[2]
    taps = grid_taps(h1e, height, breadth, False)
    small = jnp.stack(
        [
            jnp.sum(masked_one * reduced, axis=(0, 1, 2)),
            jnp.sum(masked_two * spatial_out, axis=(0, 1, 2)),
            jnp.sum(masked_one, axis=(0, 1, 2)),
            jnp.sum(masked_two, axis=(0, 1, 2)),
        ]
    )
    pieces = []
    for half_index in (1 - chan_index, chan_index):
        two_half = lax.dynamic_slice_in_dim(
            grad_two.reshape(cells, inner), half_index * half_inner, half_inner, 1
        )
        spatial_term = jnp.dot(taps.T, two_half, preferred_element_type=jnp.float32)
        small_half = lax.dynamic_slice_in_dim(small, half_index * half_inner, half_inner, 1)
        small_rows = jnp.pad(small_half, ((0, 8 - small_half.shape[0]), (0, 0)))
        pieces.append(jnp.concatenate([spatial_term, small_rows], axis=0).astype(jnp.bfloat16)[None])
    return tuple(pieces)


def dense_halves(ops, chan_index):
    cur, h1e, h2, reduced, spatial_out, grad_block, masked_two, grad_two, masked_one, grad_one = ops
    full = cur.shape[-1]
    inner = h2.shape[-1]
    half_full = full // 2
    cells = cur.shape[0] * cur.shape[1] * cur.shape[2]
    pieces = []
    for half_index in (1 - chan_index, chan_index):
        cur_half = lax.dynamic_slice_in_dim(
            cur.reshape(cells, full), half_index * half_full, half_full, 1
        )
        block_half = lax.dynamic_slice_in_dim(
            grad_block.reshape(cells, full), half_index * half_full, half_full, 1
        )
        reduce_term = jnp.dot(
            cur_half.T, grad_one.reshape(cells, inner), preferred_element_type=jnp.float32
        )
        expand_term = jnp.dot(
            h2.reshape(cells, inner).T, block_half, preferred_element_type=jnp.float32
        )
        pieces.append(reduce_term.astype(jnp.bfloat16)[None])
        pieces.append(expand_term.astype(jnp.bfloat16)[None])
    return tuple(pieces)


def halving_all_reduce(value, axis):
    count = lax.axis_size(axis)
    assert count & (count - 1) == 0
    place = lax.axis_index(axis)
    steps = count.bit_length() - 1
    rows = value.shape[0]
    spare = (-rows) % count
    current = jnp.pad(value, ((0, spare),) + ((0, 0),) * (value.ndim - 1))
    for step in range(steps):
        bit = 1 << step
        upper = (place // bit) % 2
        half = current.shape[0] // 2
        keep = lax.dynamic_slice_in_dim(current, upper * half, half, 0)
        send = lax.dynamic_slice_in_dim(current, (1 - upper) * half, half, 0)
        got = lax.ppermute(send, axis, [(i, i ^ bit) for i in range(count)])
        current = (keep.astype(jnp.float32) + got.astype(jnp.float32)).astype(value.dtype)
    for step in reversed(range(steps)):
        bit = 1 << step
        upper = (place // bit) % 2
        got = lax.ppermute(current, axis, [(i, i ^ bit) for i in range(count)])
        current = jnp.where(
            upper == 0,
            jnp.concatenate([current, got], axis=0),
            jnp.concatenate([got, current], axis=0),
        )
    return current[:rows]


def local(
    features,
    tissue,
    row_label,
    prototypes,
    reduce_weight,
    spatial_weight,
    expand_weight,
    norm_gain,
    norm_bias,
):
    regions, height, breadth, full_width = features.shape
    chain = lax.axis_size("sections")
    position = lax.axis_index("sections")
    chan_index = lax.axis_index("chan")
    reduce_all = gather_blocks(reduce_weight[0], 0, chain, position, chan_index)
    spatial_all = gather_blocks(spatial_weight[0], 3, chain, position, chan_index)
    expand_all = gather_blocks(expand_weight[0], 1, chain, position, chan_index)
    gain_all = gather_blocks(norm_gain[0], None, chain, position, chan_index)
    bias_all = gather_blocks(norm_bias[0], None, chain, position, chan_index)
    inner_width = reduce_all[0].shape[1]
    tissue_mask = tissue.astype(jnp.float32)[:, :, :, None]
    cells = regions * height * breadth
    inner_shape = (regions, height, breadth, inner_width)
    outer_shape = (regions, height, breadth, full_width)

    current = features
    saved = []
    for b in range(chain):
        gain_pair, bias_pair = gain_all[b], bias_all[b]
        reduced = jnp.dot(
            current.reshape(cells, full_width), reduce_all[b], preferred_element_type=jnp.float32
        ).reshape(inner_shape)
        pre_reduce = gain_pair[0] * reduced + bias_pair[0]
        hidden_one = jnp.maximum(pre_reduce, 0.0).astype(jnp.bfloat16)
        hidden_ext = halo_rows(hidden_one)
        spatial_out = jnp.dot(
            grid_taps(hidden_ext, height, breadth, False),
            spatial_all[b].reshape(9 * inner_width, inner_width),
            preferred_element_type=jnp.float32,
        ).reshape(inner_shape)
        pre_spatial = gain_pair[1] * spatial_out + bias_pair[1]
        hidden_two = jnp.maximum(pre_spatial, 0.0).astype(jnp.bfloat16)
        expanded = jnp.dot(
            hidden_two.reshape(cells, inner_width), expand_all[b], preferred_element_type=jnp.float32
        ).reshape(outer_shape)
        block_out = (
            tissue_mask * jnp.maximum(current.astype(jnp.float32) + expanded, 0.0)
        ).astype(jnp.bfloat16)
        saved.append((current, hidden_ext, reduced, pre_reduce, spatial_out, pre_spatial, hidden_two, block_out))
        current = block_out

    classes = prototypes.shape[0]
    chosen = (row_label[:, :, None] == jnp.arange(classes, dtype=jnp.int32)).astype(jnp.float32)
    target_rows = jnp.einsum("mrk,kc->mrc", chosen, prototypes.astype(jnp.float32))
    total_cells = regions * height * lax.axis_size("tiles") * lax.axis_size("chan") * breadth
    upstream = (
        tissue_mask * (current.astype(jnp.float32) - target_rows[:, :, None, :]) / total_cells
    ).astype(jnp.bfloat16)

    block_ops = [None] * chain
    for b in reversed(range(chain)):
        block_in, hidden_ext, reduced, pre_reduce, spatial_out, pre_spatial, hidden_two, block_out = saved[b]
        needed = b >= position
        gain_pair = gain_all[b]

        def first_back(upstream=upstream, block_out=block_out, pre_spatial=pre_spatial, b=b, gain_pair=gain_pair):
            grad_block = jnp.where(block_out > 0, upstream, jnp.zeros_like(upstream))
            back_two = jnp.dot(
                grad_block.reshape(cells, full_width), expand_all[b].T, preferred_element_type=jnp.float32
            ).reshape(inner_shape)
            masked_two = jnp.where(pre_spatial > 0, back_two, jnp.float32(0.0))
            grad_two = (masked_two * gain_pair[1]).astype(jnp.bfloat16)
            return grad_block, masked_two, grad_two

        def first_skip():
            return (
                jnp.zeros(outer_shape, jnp.bfloat16),
                jnp.zeros(inner_shape, jnp.float32),
                jnp.zeros(inner_shape, jnp.bfloat16),
            )

        grad_block, masked_two, grad_two = lax.cond(needed, first_back, first_skip)
        grad_ext = halo_rows(grad_two)

        def second_back(grad_ext=grad_ext, pre_reduce=pre_reduce, b=b, gain_pair=gain_pair):
            back_one = jnp.dot(
                grid_taps(grad_ext, height, breadth, True),
                jnp.transpose(spatial_all[b], (0, 1, 3, 2)).reshape(9 * inner_width, inner_width),
                preferred_element_type=jnp.float32,
            ).reshape(inner_shape)
            masked_one = jnp.where(pre_reduce > 0, back_one, jnp.float32(0.0))
            grad_one = (masked_one * gain_pair[0]).astype(jnp.bfloat16)
            return masked_one, grad_one

        def second_skip():
            return (jnp.zeros(inner_shape, jnp.float32), jnp.zeros(inner_shape, jnp.bfloat16))

        masked_one, grad_one = lax.cond(needed, second_back, second_skip)
        block_ops[b] = (
            block_in, hidden_ext, hidden_two, reduced, spatial_out,
            grad_block, masked_two, grad_two, masked_one, grad_one,
        )
        if b > 0:

            def pass_back(grad_block=grad_block, grad_one=grad_one, b=b):
                return (
                    grad_block.astype(jnp.float32)
                    + jnp.dot(
                        grad_one.reshape(cells, inner_width),
                        reduce_all[b].T,
                        preferred_element_type=jnp.float32,
                    ).reshape(outer_shape)
                ).astype(jnp.bfloat16)

            upstream = lax.cond(
                b > position, pass_back, lambda: jnp.zeros(outer_shape, jnp.bfloat16)
            )

    def pair_sum(own_piece, other_piece):
        arrived = lax.ppermute(other_piece, "chan", [(0, 1), (1, 0)])
        return (own_piece.astype(jnp.float32) + arrived.astype(jnp.float32)).astype(jnp.bfloat16)

    spatial_theirs, spatial_mine = lax.switch(
        position,
        [
            functools.partial(lambda k: spatial_halves(block_ops[k], height, breadth, chan_index), k)
            for k in range(chain)
        ],
    )
    spatial_pair = pair_sum(spatial_mine, spatial_theirs)
    spatial_pair, later_ops = lax.optimization_barrier((spatial_pair, block_ops))
    spatial_total = halving_all_reduce(spatial_pair[0], "tiles")[None]
    reduce_theirs, expand_theirs, reduce_mine, expand_mine = lax.switch(
        position,
        [
            functools.partial(lambda k: dense_halves(later_ops[k], chan_index), k)
            for k in range(chain)
        ],
    )
    reduce_pair = pair_sum(reduce_mine, reduce_theirs)
    expand_pair = pair_sum(expand_mine, expand_theirs)
    totals = (
        halving_all_reduce(reduce_pair[0], "tiles")[None],
        spatial_total,
        halving_all_reduce(expand_pair[0], "tiles")[None],
    )
    half_inner = inner_width // 2
    grad_reduce = totals[0]
    grad_spatial = totals[1][:, : 9 * inner_width].reshape(1, 3, 3, inner_width, half_inner)
    grad_expand = totals[2]
    small = totals[1][:, 9 * inner_width : 9 * inner_width + 4].astype(jnp.float32)
    return (grad_reduce, grad_spatial, grad_expand, small[:, 0:2], small[:, 2:4])


def solution(mesh):
    placed = (
        P("groups", ("tiles", "chan"), None, None),
        P("groups", ("tiles", "chan"), None),
        P("groups", ("tiles", "chan")),
        P(),
        P("sections", "chan", None),
        P("sections", None, None, None, "chan"),
        P("sections", None, "chan"),
        P("sections", None, None),
        P("sections", None, None),
    )
    return jax.shard_map(
        local,
        mesh=mesh,
        in_specs=placed,
        out_specs=(
            P(("groups", "sections"), "chan", None),
            P(("groups", "sections"), None, None, None, "chan"),
            P(("groups", "sections"), None, "chan"),
            P(("groups", "sections"), None, "chan"),
            P(("groups", "sections"), None, "chan"),
        ),
        check_vma=False,
    )
```

```python
import functools

import jax
import jax.numpy as jnp
from jax import lax
from jax.sharding import PartitionSpec as P

ROW_AXES = ("tiles", "chan")


def halo_rows(block):
    count = lax.axis_size(ROW_AXES)
    forward = [(i, i + 1) for i in range(count - 1)]
    backward = [(target, source) for source, target in forward]
    low = lax.ppermute(block[:, -1:], ROW_AXES, forward)
    high = lax.ppermute(block[:, :1], ROW_AXES, backward)
    return jnp.concatenate([low, block, high], axis=1)


def grid_taps(extended, height, breadth, mirrored):
    padded = jnp.pad(extended, ((0, 0), (0, 0), (1, 1), (0, 0)))
    tap_list = []
    for shift_row in range(3):
        for shift_col in range(3):
            if mirrored:
                start_row = 2 - shift_row
                start_col = 2 - shift_col
            else:
                start_row = shift_row
                start_col = shift_col
            tap_list.append(
                padded[:, start_row : start_row + height, start_col : start_col + breadth]
            )
    stacked = jnp.concatenate(tap_list, axis=3)
    return stacked.reshape(extended.shape[0] * height * breadth, stacked.shape[3])


def gather_blocks(half, chan_axis, chain, position, chan_index):
    received = [
        lax.ppermute(half, "sections", [(i, (i + k) % chain) for i in range(chain)])
        for k in range(1, chain)
    ]
    parts = [half] + received
    if chan_axis is not None:
        joined = []
        for part in parts:
            other = lax.ppermute(part, "chan", [(0, 1), (1, 0)])
            joined.append(
                jnp.where(
                    chan_index == 0,
                    jnp.concatenate([part, other], axis=chan_axis),
                    jnp.concatenate([other, part], axis=chan_axis),
                )
            )
        parts = joined
    stacked = jnp.stack(parts)
    return [
        lax.dynamic_index_in_dim(stacked, (position - b + chain) % chain, 0, keepdims=False)
        for b in range(chain)
    ]


def spatial_halves(ops, height, breadth, chan_index):
    cur, h1e, h2, reduced, spatial_out, grad_block, masked_two, grad_two, masked_one, grad_one = ops
    inner = h2.shape[-1]
    half_inner = inner // 2
    cells = grad_two.shape[0] * grad_two.shape[1] * grad_two.shape[2]
    taps = grid_taps(h1e, height, breadth, False)
    small = jnp.stack(
        [
            jnp.sum(masked_one * reduced, axis=(0, 1, 2)),
            jnp.sum(masked_two * spatial_out, axis=(0, 1, 2)),
            jnp.sum(masked_one, axis=(0, 1, 2)),
            jnp.sum(masked_two, axis=(0, 1, 2)),
        ]
    )
    pieces = []
    for half_index in (1 - chan_index, chan_index):
        two_half = lax.dynamic_slice_in_dim(
            grad_two.reshape(cells, inner), half_index * half_inner, half_inner, 1
        )
        spatial_term = jnp.dot(taps.T, two_half, preferred_element_type=jnp.float32)
        small_half = lax.dynamic_slice_in_dim(small, half_index * half_inner, half_inner, 1)
        small_rows = jnp.pad(small_half, ((0, 8 - small_half.shape[0]), (0, 0)))
        pieces.append(jnp.concatenate([spatial_term, small_rows], axis=0).astype(jnp.bfloat16)[None])
    return tuple(pieces)


def dense_halves(ops, chan_index):
    cur, h1e, h2, reduced, spatial_out, grad_block, masked_two, grad_two, masked_one, grad_one = ops
    full = cur.shape[-1]
    inner = h2.shape[-1]
    half_full = full // 2
    cells = cur.shape[0] * cur.shape[1] * cur.shape[2]
    pieces = []
    for half_index in (1 - chan_index, chan_index):
        cur_half = lax.dynamic_slice_in_dim(
            cur.reshape(cells, full), half_index * half_full, half_full, 1
        )
        block_half = lax.dynamic_slice_in_dim(
            grad_block.reshape(cells, full), half_index * half_full, half_full, 1
        )
        reduce_term = jnp.dot(
            cur_half.T, grad_one.reshape(cells, inner), preferred_element_type=jnp.float32
        )
        expand_term = jnp.dot(
            h2.reshape(cells, inner).T, block_half, preferred_element_type=jnp.float32
        )
        pieces.append(reduce_term.astype(jnp.bfloat16)[None])
        pieces.append(expand_term.astype(jnp.bfloat16)[None])
    return tuple(pieces)


def halving_all_reduce(value, axis):
    count = lax.axis_size(axis)
    assert count & (count - 1) == 0
    place = lax.axis_index(axis)
    steps = count.bit_length() - 1
    rows = value.shape[0]
    spare = (-rows) % count
    current = jnp.pad(value, ((0, spare),) + ((0, 0),) * (value.ndim - 1))
    for step in range(steps):
        bit = 1 << step
        upper = (place // bit) % 2
        half = current.shape[0] // 2
        keep = lax.dynamic_slice_in_dim(current, upper * half, half, 0)
        send = lax.dynamic_slice_in_dim(current, (1 - upper) * half, half, 0)
        got = lax.ppermute(send, axis, [(i, i ^ bit) for i in range(count)])
        current = (keep.astype(jnp.float32) + got.astype(jnp.float32)).astype(value.dtype)
    for step in reversed(range(steps)):
        bit = 1 << step
        upper = (place // bit) % 2
        got = lax.ppermute(current, axis, [(i, i ^ bit) for i in range(count)])
        size = current.shape[0]
        merged = jnp.zeros((2 * size,) + current.shape[1:], current.dtype)
        merged = lax.dynamic_update_slice_in_dim(merged, current, upper * size, 0)
        current = lax.dynamic_update_slice_in_dim(merged, got, (1 - upper) * size, 0)
    return current[:rows]


def local(
    features,
    tissue,
    row_label,
    prototypes,
    reduce_weight,
    spatial_weight,
    expand_weight,
    norm_gain,
    norm_bias,
):
    regions, height, breadth, full_width = features.shape
    chain = lax.axis_size("sections")
    position = lax.axis_index("sections")
    chan_index = lax.axis_index("chan")
    reduce_all = gather_blocks(reduce_weight[0], 0, chain, position, chan_index)
    spatial_all = gather_blocks(spatial_weight[0], 3, chain, position, chan_index)
    expand_all = gather_blocks(expand_weight[0], 1, chain, position, chan_index)
    gain_all = gather_blocks(norm_gain[0], None, chain, position, chan_index)
    bias_all = gather_blocks(norm_bias[0], None, chain, position, chan_index)
    inner_width = reduce_all[0].shape[1]
    tissue_mask = tissue.astype(jnp.float32)[:, :, :, None]
    cells = regions * height * breadth
    inner_shape = (regions, height, breadth, inner_width)
    outer_shape = (regions, height, breadth, full_width)

    current = features
    saved = []
    for b in range(chain):
        gain_pair, bias_pair = gain_all[b], bias_all[b]
        reduced = jnp.dot(
            current.reshape(cells, full_width), reduce_all[b], preferred_element_type=jnp.float32
        ).reshape(inner_shape)
        pre_reduce = gain_pair[0] * reduced + bias_pair[0]
        hidden_one = jnp.maximum(pre_reduce, 0.0).astype(jnp.bfloat16)
        hidden_ext = halo_rows(hidden_one)
        spatial_out = jnp.dot(
            grid_taps(hidden_ext, height, breadth, False),
            spatial_all[b].reshape(9 * inner_width, inner_width),
            preferred_element_type=jnp.float32,
        ).reshape(inner_shape)
        pre_spatial = gain_pair[1] * spatial_out + bias_pair[1]
        hidden_two = jnp.maximum(pre_spatial, 0.0).astype(jnp.bfloat16)
        expanded = jnp.dot(
            hidden_two.reshape(cells, inner_width), expand_all[b], preferred_element_type=jnp.float32
        ).reshape(outer_shape)
        block_out = (
            tissue_mask * jnp.maximum(current.astype(jnp.float32) + expanded, 0.0)
        ).astype(jnp.bfloat16)
        saved.append((current, hidden_ext, reduced, pre_reduce, spatial_out, pre_spatial, hidden_two, block_out))
        current = block_out

    classes = prototypes.shape[0]
    chosen = (row_label[:, :, None] == jnp.arange(classes, dtype=jnp.int32)).astype(jnp.float32)
    target_rows = jnp.einsum("mrk,kc->mrc", chosen, prototypes.astype(jnp.float32))
    total_cells = regions * height * lax.axis_size("tiles") * lax.axis_size("chan") * breadth
    upstream = (
        tissue_mask * (current.astype(jnp.float32) - target_rows[:, :, None, :]) / total_cells
    ).astype(jnp.bfloat16)

    block_ops = [None] * chain
    for b in reversed(range(chain)):
        block_in, hidden_ext, reduced, pre_reduce, spatial_out, pre_spatial, hidden_two, block_out = saved[b]
        needed = b >= position
        gain_pair = gain_all[b]

        def first_back(upstream=upstream, block_out=block_out, pre_spatial=pre_spatial, b=b, gain_pair=gain_pair):
            grad_block = jnp.where(block_out > 0, upstream, jnp.zeros_like(upstream))
            back_two = jnp.dot(
                grad_block.reshape(cells, full_width), expand_all[b].T, preferred_element_type=jnp.float32
            ).reshape(inner_shape)
            masked_two = jnp.where(pre_spatial > 0, back_two, jnp.float32(0.0))
            grad_two = (masked_two * gain_pair[1]).astype(jnp.bfloat16)
            return grad_block, masked_two, grad_two

        def first_skip():
            return (
                jnp.zeros(outer_shape, jnp.bfloat16),
                jnp.zeros(inner_shape, jnp.float32),
                jnp.zeros(inner_shape, jnp.bfloat16),
            )

        grad_block, masked_two, grad_two = lax.cond(needed, first_back, first_skip)
        grad_ext = halo_rows(grad_two)

        def second_back(grad_ext=grad_ext, pre_reduce=pre_reduce, b=b, gain_pair=gain_pair):
            back_one = jnp.dot(
                grid_taps(grad_ext, height, breadth, True),
                jnp.transpose(spatial_all[b], (0, 1, 3, 2)).reshape(9 * inner_width, inner_width),
                preferred_element_type=jnp.float32,
            ).reshape(inner_shape)
            masked_one = jnp.where(pre_reduce > 0, back_one, jnp.float32(0.0))
            grad_one = (masked_one * gain_pair[0]).astype(jnp.bfloat16)
            return masked_one, grad_one

        def second_skip():
            return (jnp.zeros(inner_shape, jnp.float32), jnp.zeros(inner_shape, jnp.bfloat16))

        masked_one, grad_one = lax.cond(needed, second_back, second_skip)
        block_ops[b] = (
            block_in, hidden_ext, hidden_two, reduced, spatial_out,
            grad_block, masked_two, grad_two, masked_one, grad_one,
        )
        if b > 0:

            def pass_back(grad_block=grad_block, grad_one=grad_one, b=b):
                return (
                    grad_block.astype(jnp.float32)
                    + jnp.dot(
                        grad_one.reshape(cells, inner_width),
                        reduce_all[b].T,
                        preferred_element_type=jnp.float32,
                    ).reshape(outer_shape)
                ).astype(jnp.bfloat16)

            upstream = lax.cond(
                b > position, pass_back, lambda: jnp.zeros(outer_shape, jnp.bfloat16)
            )

    def pair_sum(own_piece, other_piece):
        arrived = lax.ppermute(other_piece, "chan", [(0, 1), (1, 0)])
        return (own_piece.astype(jnp.float32) + arrived.astype(jnp.float32)).astype(jnp.bfloat16)

    spatial_theirs, spatial_mine = lax.switch(
        position,
        [
            functools.partial(lambda k: spatial_halves(block_ops[k], height, breadth, chan_index), k)
            for k in range(chain)
        ],
    )
    spatial_pair = pair_sum(spatial_mine, spatial_theirs)
    spatial_pair, later_ops = lax.optimization_barrier((spatial_pair, block_ops))
    spatial_total = halving_all_reduce(spatial_pair[0], "tiles")[None]
    reduce_theirs, expand_theirs, reduce_mine, expand_mine = lax.switch(
        position,
        [
            functools.partial(lambda k: dense_halves(later_ops[k], chan_index), k)
            for k in range(chain)
        ],
    )
    reduce_pair = pair_sum(reduce_mine, reduce_theirs)
    expand_pair = pair_sum(expand_mine, expand_theirs)
    totals = (
        halving_all_reduce(reduce_pair[0], "tiles")[None],
        spatial_total,
        halving_all_reduce(expand_pair[0], "tiles")[None],
    )
    half_inner = inner_width // 2
    grad_reduce = totals[0]
    grad_spatial = totals[1][:, : 9 * inner_width].reshape(1, 3, 3, inner_width, half_inner)
    grad_expand = totals[2]
    small = totals[1][:, 9 * inner_width : 9 * inner_width + 4].astype(jnp.float32)
    return (grad_reduce, grad_spatial, grad_expand, small[:, 0:2], small[:, 2:4])


def solution(mesh):
    placed = (
        P("groups", ("tiles", "chan"), None, None),
        P("groups", ("tiles", "chan"), None),
        P("groups", ("tiles", "chan")),
        P(),
        P("sections", "chan", None),
        P("sections", None, None, None, "chan"),
        P("sections", None, "chan"),
        P("sections", None, None),
        P("sections", None, None),
    )
    return jax.shard_map(
        local,
        mesh=mesh,
        in_specs=placed,
        out_specs=(
            P(("groups", "sections"), "chan", None),
            P(("groups", "sections"), None, None, None, "chan"),
            P(("groups", "sections"), None, "chan"),
            P(("groups", "sections"), None, "chan"),
            P(("groups", "sections"), None, "chan"),
        ),
        check_vma=False,
    )
```

```python
import functools

import jax
import jax.numpy as jnp
from jax import lax
from jax.sharding import PartitionSpec as P

ROW_AXES = ("tiles", "chan")


def halo_rows(block):
    count = lax.axis_size(ROW_AXES)
    forward = [(i, i + 1) for i in range(count - 1)]
    backward = [(target, source) for source, target in forward]
    low = lax.ppermute(block[:, -1:], ROW_AXES, forward)
    high = lax.ppermute(block[:, :1], ROW_AXES, backward)
    return jnp.concatenate([low, block, high], axis=1)


def grid_taps(extended, height, breadth, mirrored):
    padded = jnp.pad(extended, ((0, 0), (0, 0), (1, 1), (0, 0)))
    tap_list = []
    for shift_row in range(3):
        for shift_col in range(3):
            if mirrored:
                start_row = 2 - shift_row
                start_col = 2 - shift_col
            else:
                start_row = shift_row
                start_col = shift_col
            tap_list.append(
                padded[:, start_row : start_row + height, start_col : start_col + breadth]
            )
    stacked = jnp.concatenate(tap_list, axis=3)
    return stacked.reshape(extended.shape[0] * height * breadth, stacked.shape[3])


def gather_blocks(half, chan_axis, chain, position, chan_index):
    received = [
        lax.ppermute(half, "sections", [(i, (i + k) % chain) for i in range(chain)])
        for k in range(1, chain)
    ]
    parts = [half] + received
    if chan_axis is not None:
        joined = []
        for part in parts:
            other = lax.ppermute(part, "chan", [(0, 1), (1, 0)])
            size = part.shape[chan_axis]
            shape = part.shape[:chan_axis] + (2 * size,) + part.shape[chan_axis + 1 :]
            merged = jnp.zeros(shape, part.dtype)
            merged = lax.dynamic_update_slice_in_dim(merged, part, chan_index * size, chan_axis)
            joined.append(
                lax.dynamic_update_slice_in_dim(merged, other, (1 - chan_index) * size, chan_axis)
            )
        parts = joined
    stacked = jnp.stack(parts)
    return [
        lax.dynamic_index_in_dim(stacked, (position - b + chain) % chain, 0, keepdims=False)
        for b in range(chain)
    ]


def spatial_halves(ops, height, breadth, chan_index):
    cur, h1e, h2, reduced, spatial_out, grad_block, masked_two, grad_two, masked_one, grad_one = ops
    inner = h2.shape[-1]
    half_inner = inner // 2
    cells = grad_two.shape[0] * grad_two.shape[1] * grad_two.shape[2]
    taps = grid_taps(h1e, height, breadth, False)
    small = jnp.stack(
        [
            jnp.sum(masked_one * reduced, axis=(0, 1, 2)),
            jnp.sum(masked_two * spatial_out, axis=(0, 1, 2)),
            jnp.sum(masked_one, axis=(0, 1, 2)),
            jnp.sum(masked_two, axis=(0, 1, 2)),
        ]
    )
    pieces = []
    for half_index in (1 - chan_index, chan_index):
        two_half = lax.dynamic_slice_in_dim(
            grad_two.reshape(cells, inner), half_index * half_inner, half_inner, 1
        )
        spatial_term = jnp.dot(taps.T, two_half, preferred_element_type=jnp.float32)
        small_half = lax.dynamic_slice_in_dim(small, half_index * half_inner, half_inner, 1)
        small_rows = jnp.pad(small_half, ((0, 8 - small_half.shape[0]), (0, 0)))
        pieces.append(jnp.concatenate([spatial_term, small_rows], axis=0).astype(jnp.bfloat16)[None])
    return tuple(pieces)


def dense_halves(ops, chan_index):
    cur, h1e, h2, reduced, spatial_out, grad_block, masked_two, grad_two, masked_one, grad_one = ops
    full = cur.shape[-1]
    inner = h2.shape[-1]
    half_full = full // 2
    cells = cur.shape[0] * cur.shape[1] * cur.shape[2]
    pieces = []
    for half_index in (1 - chan_index, chan_index):
        cur_half = lax.dynamic_slice_in_dim(
            cur.reshape(cells, full), half_index * half_full, half_full, 1
        )
        block_half = lax.dynamic_slice_in_dim(
            grad_block.reshape(cells, full), half_index * half_full, half_full, 1
        )
        reduce_term = jnp.dot(
            cur_half.T, grad_one.reshape(cells, inner), preferred_element_type=jnp.float32
        )
        expand_term = jnp.dot(
            h2.reshape(cells, inner).T, block_half, preferred_element_type=jnp.float32
        )
        pieces.append(reduce_term.astype(jnp.bfloat16)[None])
        pieces.append(expand_term.astype(jnp.bfloat16)[None])
    return tuple(pieces)


def halving_all_reduce(value, axis):
    count = lax.axis_size(axis)
    assert count & (count - 1) == 0
    place = lax.axis_index(axis)
    steps = count.bit_length() - 1
    rows = value.shape[0]
    spare = (-rows) % count
    current = jnp.pad(value, ((0, spare),) + ((0, 0),) * (value.ndim - 1))
    for step in range(steps):
        bit = 1 << step
        upper = (place // bit) % 2
        half = current.shape[0] // 2
        keep = lax.dynamic_slice_in_dim(current, upper * half, half, 0)
        send = lax.dynamic_slice_in_dim(current, (1 - upper) * half, half, 0)
        got = lax.ppermute(send, axis, [(i, i ^ bit) for i in range(count)])
        current = (keep.astype(jnp.float32) + got.astype(jnp.float32)).astype(value.dtype)
    for step in reversed(range(steps)):
        bit = 1 << step
        upper = (place // bit) % 2
        got = lax.ppermute(current, axis, [(i, i ^ bit) for i in range(count)])
        size = current.shape[0]
        merged = jnp.zeros((2 * size,) + current.shape[1:], current.dtype)
        merged = lax.dynamic_update_slice_in_dim(merged, current, upper * size, 0)
        current = lax.dynamic_update_slice_in_dim(merged, got, (1 - upper) * size, 0)
    return current[:rows]


def local(
    features,
    tissue,
    row_label,
    prototypes,
    reduce_weight,
    spatial_weight,
    expand_weight,
    norm_gain,
    norm_bias,
):
    regions, height, breadth, full_width = features.shape
    chain = lax.axis_size("sections")
    position = lax.axis_index("sections")
    chan_index = lax.axis_index("chan")
    reduce_all = gather_blocks(reduce_weight[0], 0, chain, position, chan_index)
    spatial_all = gather_blocks(spatial_weight[0], 3, chain, position, chan_index)
    expand_all = gather_blocks(expand_weight[0], 1, chain, position, chan_index)
    gain_all = gather_blocks(norm_gain[0], None, chain, position, chan_index)
    bias_all = gather_blocks(norm_bias[0], None, chain, position, chan_index)
    inner_width = reduce_all[0].shape[1]
    tissue_mask = tissue.astype(jnp.float32)[:, :, :, None]
    cells = regions * height * breadth
    inner_shape = (regions, height, breadth, inner_width)
    outer_shape = (regions, height, breadth, full_width)

    current = features
    saved = []
    for b in range(chain):
        gain_pair, bias_pair = gain_all[b], bias_all[b]
        reduced = jnp.dot(
            current.reshape(cells, full_width), reduce_all[b], preferred_element_type=jnp.float32
        ).reshape(inner_shape)
        pre_reduce = gain_pair[0] * reduced + bias_pair[0]
        hidden_one = jnp.maximum(pre_reduce, 0.0).astype(jnp.bfloat16)
        hidden_ext = halo_rows(hidden_one)
        spatial_out = jnp.dot(
            grid_taps(hidden_ext, height, breadth, False),
            spatial_all[b].reshape(9 * inner_width, inner_width),
            preferred_element_type=jnp.float32,
        ).reshape(inner_shape)
        pre_spatial = gain_pair[1] * spatial_out + bias_pair[1]
        hidden_two = jnp.maximum(pre_spatial, 0.0).astype(jnp.bfloat16)
        expanded = jnp.dot(
            hidden_two.reshape(cells, inner_width), expand_all[b], preferred_element_type=jnp.float32
        ).reshape(outer_shape)
        block_out = (
            tissue_mask * jnp.maximum(current.astype(jnp.float32) + expanded, 0.0)
        ).astype(jnp.bfloat16)
        saved.append((current, hidden_ext, reduced, pre_reduce, spatial_out, pre_spatial, hidden_two, block_out))
        current = block_out

    classes = prototypes.shape[0]
    chosen = (row_label[:, :, None] == jnp.arange(classes, dtype=jnp.int32)).astype(jnp.float32)
    target_rows = jnp.einsum("mrk,kc->mrc", chosen, prototypes.astype(jnp.float32))
    total_cells = regions * height * lax.axis_size("tiles") * lax.axis_size("chan") * breadth
    upstream = (
        tissue_mask * (current.astype(jnp.float32) - target_rows[:, :, None, :]) / total_cells
    ).astype(jnp.bfloat16)

    block_ops = [None] * chain
    for b in reversed(range(chain)):
        block_in, hidden_ext, reduced, pre_reduce, spatial_out, pre_spatial, hidden_two, block_out = saved[b]
        needed = b >= position
        gain_pair = gain_all[b]

        def first_back(upstream=upstream, block_out=block_out, pre_spatial=pre_spatial, b=b, gain_pair=gain_pair):
            grad_block = jnp.where(block_out > 0, upstream, jnp.zeros_like(upstream))
            back_two = jnp.dot(
                grad_block.reshape(cells, full_width), expand_all[b].T, preferred_element_type=jnp.float32
            ).reshape(inner_shape)
            masked_two = jnp.where(pre_spatial > 0, back_two, jnp.float32(0.0))
            grad_two = (masked_two * gain_pair[1]).astype(jnp.bfloat16)
            return grad_block, masked_two, grad_two

        def first_skip():
            return (
                jnp.zeros(outer_shape, jnp.bfloat16),
                jnp.zeros(inner_shape, jnp.float32),
                jnp.zeros(inner_shape, jnp.bfloat16),
            )

        grad_block, masked_two, grad_two = lax.cond(needed, first_back, first_skip)
        grad_ext = halo_rows(grad_two)

        def second_back(grad_ext=grad_ext, pre_reduce=pre_reduce, b=b, gain_pair=gain_pair):
            back_one = jnp.dot(
                grid_taps(grad_ext, height, breadth, True),
                jnp.transpose(spatial_all[b], (0, 1, 3, 2)).reshape(9 * inner_width, inner_width),
                preferred_element_type=jnp.float32,
            ).reshape(inner_shape)
            masked_one = jnp.where(pre_reduce > 0, back_one, jnp.float32(0.0))
            grad_one = (masked_one * gain_pair[0]).astype(jnp.bfloat16)
            return masked_one, grad_one

        def second_skip():
            return (jnp.zeros(inner_shape, jnp.float32), jnp.zeros(inner_shape, jnp.bfloat16))

        masked_one, grad_one = lax.cond(needed, second_back, second_skip)
        block_ops[b] = (
            block_in, hidden_ext, hidden_two, reduced, spatial_out,
            grad_block, masked_two, grad_two, masked_one, grad_one,
        )
        if b > 0:

            def pass_back(grad_block=grad_block, grad_one=grad_one, b=b):
                return (
                    grad_block.astype(jnp.float32)
                    + jnp.dot(
                        grad_one.reshape(cells, inner_width),
                        reduce_all[b].T,
                        preferred_element_type=jnp.float32,
                    ).reshape(outer_shape)
                ).astype(jnp.bfloat16)

            upstream = lax.cond(
                b > position, pass_back, lambda: jnp.zeros(outer_shape, jnp.bfloat16)
            )

    def pair_sum(own_piece, other_piece):
        arrived = lax.ppermute(other_piece, "chan", [(0, 1), (1, 0)])
        return (own_piece.astype(jnp.float32) + arrived.astype(jnp.float32)).astype(jnp.bfloat16)

    spatial_theirs, spatial_mine = lax.switch(
        position,
        [
            functools.partial(lambda k: spatial_halves(block_ops[k], height, breadth, chan_index), k)
            for k in range(chain)
        ],
    )
    spatial_pair = pair_sum(spatial_mine, spatial_theirs)
    spatial_pair, later_ops = lax.optimization_barrier((spatial_pair, block_ops))
    spatial_total = halving_all_reduce(spatial_pair[0], "tiles")[None]
    reduce_theirs, expand_theirs, reduce_mine, expand_mine = lax.switch(
        position,
        [
            functools.partial(lambda k: dense_halves(later_ops[k], chan_index), k)
            for k in range(chain)
        ],
    )
    reduce_pair = pair_sum(reduce_mine, reduce_theirs)
    expand_pair = pair_sum(expand_mine, expand_theirs)
    totals = (
        halving_all_reduce(reduce_pair[0], "tiles")[None],
        spatial_total,
        halving_all_reduce(expand_pair[0], "tiles")[None],
    )
    half_inner = inner_width // 2
    grad_reduce = totals[0]
    grad_spatial = totals[1][:, : 9 * inner_width].reshape(1, 3, 3, inner_width, half_inner)
    grad_expand = totals[2]
    small = totals[1][:, 9 * inner_width : 9 * inner_width + 4].astype(jnp.float32)
    return (grad_reduce, grad_spatial, grad_expand, small[:, 0:2], small[:, 2:4])


def solution(mesh):
    placed = (
        P("groups", ("tiles", "chan"), None, None),
        P("groups", ("tiles", "chan"), None),
        P("groups", ("tiles", "chan")),
        P(),
        P("sections", "chan", None),
        P("sections", None, None, None, "chan"),
        P("sections", None, "chan"),
        P("sections", None, None),
        P("sections", None, None),
    )
    return jax.shard_map(
        local,
        mesh=mesh,
        in_specs=placed,
        out_specs=(
            P(("groups", "sections"), "chan", None),
            P(("groups", "sections"), None, None, None, "chan"),
            P(("groups", "sections"), None, "chan"),
            P(("groups", "sections"), None, "chan"),
            P(("groups", "sections"), None, "chan"),
        ),
        check_vma=False,
    )
```
